32 devices in a mesh: dp: 4 (over z), seq: 8 (over y, x, core).
Axes of the slice: x: 2, y: 2, z: 4, core: 2. Of those that a mesh axis runs over, the one named last changes fastest.
Arguments:
- features: bfloat16 [4, 1024, 6144], P('dp', 'seq'), may hold values from -6 to 6
- short_filter: float32 [3, 6144], replicated, may hold values from -3 to 3
- response: bfloat16 [1024, 2048], P('seq'), may hold values from -0.1875 to 0.1875
- skip_gain: float32 [2048], replicated, may hold values from -3 to 3
- cotangent: bfloat16 [4, 1024, 2048], P('dp', 'seq'), may hold values from -6 to 6
Outputs:
- gated: bfloat16 [4, 1024, 2048], P('dp', 'seq')
- grad_feats: bfloat16 [4, 1024, 6144], P('dp', 'seq')
- grad_short: float32 [3, 6144], replicated
- grad_skip: float32 [2048], replicated
- grad_response: float32 [1024, 2048], P('seq', 'dp')
The draws below stay inside these ranges and needn't reach their ends.
All inputs are finite; a program needn't handle non-finite values.
Results may differ from the reference program's by a relative error of at most 0.0075.
Values may be sent and summed in bfloat16 or wider, within the bound.
No kernel may reach another device: no remote copies, remote signals or barrier semaphores. Data moves between devices by JAX's collectives and lax.ppermute only.
A program may use at most 128 MiB of HBM per device.

```python
import jax
import jax.numpy as jnp
from jax import lax

C = 2048
TOKENS = 1024
SEQS = 4


def block_scale(rng, dims, pieces, low, high):
    def one(position, shards_of):
        steps = jax.random.uniform(jax.random.fold_in(jax.random.fold_in(rng, 6), position), (shards_of,), jnp.float32, low / len(pieces), high / len(pieces))
        return jnp.repeat(jnp.exp(steps), dims[position] // shards_of).reshape((-1,) + (1,) * (len(dims) - position - 1))

    level = one(*pieces[0])
    for cut in pieces[1:]:
        level = level * one(*cut)
    return level


def centred(key, extent, spread, bound, pieces=(), kind=jnp.bfloat16):
    result = jax.random.normal(key, extent, jnp.float32) * spread
    if len(pieces) > 0:
        result = block_scale(key, extent, pieces, -0.22, 0.18) * result
    return jnp.clip(result, min=-bound, max=bound).astype(kind)


def setup_inputs(seed: int = 0) -> dict:
    key_of = jax.random.split(jax.random.key(seed), 6)
    return {
        "features": centred(key_of[0], (SEQS, TOKENS, 3 * C), 1.0, 6.0, ((0, 4), (1, 8))),
        "short_filter": centred(key_of[1], (3, 3 * C), 0.6, 3.0, (), jnp.float32),
        "response": centred(key_of[2], (TOKENS, C), TOKENS ** -0.5, 0.1875, ((0, 8),)),
        "skip_gain": centred(key_of[3], (C,), 0.5, 3.0, (), jnp.float32),
        "cotangent": centred(key_of[4], (SEQS, TOKENS, C), 1.0, 6.0, ((0, 4), (1, 8))),
    }


def reference(features, short_filter, response, skip_gain, cotangent):
    length = features.shape[1]
    chan_width = features.shape[2] // 3
    fft_length = 2 * length
    taps = short_filter.reshape(3, 3, chan_width)
    resp_spec = jnp.fft.rfft(response.astype(jnp.float32), n=fft_length, axis=0)

    def one_sequence(carry, inputs):
        feats, grad_out = inputs
        rows = feats.reshape(length, 3, chan_width)
        extended = jnp.concatenate([jnp.zeros((2, 3, chan_width), feats.dtype), rows], axis=0)
        mixed = taps[0] * extended[2:] + taps[1] * extended[1:-1] + taps[2] * extended[:-2]
        query_feat = mixed[:, 0]
        key_feat = mixed[:, 1]
        value_feat = mixed[:, 2]
        product = (key_feat * value_feat).astype(jnp.bfloat16)
        prod_spec = jnp.fft.rfft(product.astype(jnp.float32), n=fft_length, axis=0)
        conv_out = jnp.fft.irfft(prod_spec * resp_spec, n=fft_length, axis=0)[:length]
        carried = conv_out + skip_gain * product
        gated = (query_feat * carried).astype(jnp.bfloat16)
        grad_carried = (grad_out * query_feat).astype(jnp.bfloat16)
        grad_query = grad_out * carried
        grad_spec = jnp.fft.rfft(grad_carried.astype(jnp.float32), n=fft_length, axis=0)
        back_conv = jnp.fft.irfft(grad_spec * jnp.conj(resp_spec), n=fft_length, axis=0)[:length]
        grad_product = back_conv + skip_gain * grad_carried
        grad_mixed = jnp.stack([grad_query, grad_product * value_feat, grad_product * key_feat], axis=1)
        tail = jnp.concatenate([grad_mixed, jnp.zeros((2, 3, chan_width), jnp.float32)], axis=0)
        grad_feats = taps[0] * tail[:length] + taps[1] * tail[1:length + 1] + taps[2] * tail[2:]
        grad_taps = jnp.stack([jnp.sum(grad_mixed * extended[2 - tap_index:2 - tap_index + length], axis=0) for tap_index in range(3)])
        grad_skip = jnp.sum(grad_carried.astype(jnp.float32) * product.astype(jnp.float32), axis=0)
        resp_grad = grad_spec * jnp.conj(prod_spec)
        carry = (carry[0] + grad_taps, carry[1] + grad_skip, carry[2] + resp_grad)
        return carry, (gated, grad_feats.astype(jnp.bfloat16).reshape(length, 3 * chan_width))

    start = (jnp.zeros((3, 3, chan_width), jnp.float32), jnp.zeros((chan_width,), jnp.float32), jnp.zeros_like(resp_spec))
    totals, outputs = lax.scan(one_sequence, start, (features, cotangent))
    grad_response = jnp.fft.irfft(totals[2], n=fft_length, axis=0)[:length]
    return (outputs[0], outputs[1], totals[0].reshape(3, 3 * chan_width), totals[1], grad_response)
```

```python
import math

import jax
import jax.numpy as jnp
from jax import lax
from jax.sharding import PartitionSpec as P

precise = lax.Precision.HIGHEST


def dft_table(count):
    series = jnp.arange(count, dtype=jnp.int32)
    angle = (series[:, None] * series[None, :] % count).astype(jnp.float32) * (
        2.0 * math.pi / count
    )
    return (jnp.cos(angle), jnp.sin(angle))


def across_blocks(signal, offsets, blocks, fft_length):
    double = jnp.arange(2 * blocks, dtype=jnp.int32)
    single = jnp.arange(blocks, dtype=jnp.int32)
    angle = (double[:, None] * single[None, :] % (2 * blocks)).astype(jnp.float32) * (
        math.pi / blocks
    )
    table = jnp.stack([jnp.cos(angle), -jnp.sin(angle)])
    first = jnp.einsum("oap,bpjk->obajk", table, signal, precision=precise)
    twist = (double[:, None] * offsets[None, :] % fft_length).astype(jnp.float32) * (
        -2.0 * math.pi / fft_length
    )
    cosine = jnp.cos(twist)[None, :, :, None]
    sine = jnp.sin(twist)[None, :, :, None]
    return (first[0] * cosine - first[1] * sine, first[0] * sine + first[1] * cosine)


def within_blocks(part_real, part_imag):
    table_cos, table_sin = dft_table(part_real.shape[2])
    table = jnp.stack([jnp.stack([table_cos, table_sin]), jnp.stack([-table_sin, table_cos])])
    spectra = jnp.einsum(
        "oibj,ixajk->oxabk", table, jnp.stack([part_real, part_imag]), precision=precise
    )
    return (spectra[0], spectra[1])


def back_within(spec_real, spec_imag, firsts, fft_length):
    count = spec_real.shape[2]
    table_cos, table_sin = dft_table(count)
    table = jnp.stack([jnp.stack([table_cos, -table_sin]), jnp.stack([table_sin, table_cos])])
    backs = jnp.einsum(
        "oibj,ixabk->oxajk", table, jnp.stack([spec_real, spec_imag]), precision=precise
    )
    series = jnp.arange(count, dtype=jnp.int32)
    twist = (firsts[:, None] * series[None, :] % fft_length).astype(jnp.float32) * (
        2.0 * math.pi / fft_length
    )
    cosine = jnp.cos(twist)[None, :, :, None]
    sine = jnp.sin(twist)[None, :, :, None]
    return (backs[0] * cosine - backs[1] * sine, backs[0] * sine + backs[1] * cosine)


def back_across(part_real, part_imag, blocks, fft_length):
    double = jnp.arange(2 * blocks, dtype=jnp.int32)
    single = jnp.arange(blocks, dtype=jnp.int32)
    angle = (single[:, None] * double[None, :] % (2 * blocks)).astype(jnp.float32) * (
        math.pi / blocks
    )
    table = jnp.stack([jnp.cos(angle), -jnp.sin(angle)])
    result = jnp.einsum(
        "ipa,ibajk->bpjk", table, jnp.stack([part_real, part_imag]), precision=precise
    )
    return result * (1.0 / fft_length)


def times_spectrum(left, right):
    return (left[0] * right[0] - left[1] * right[1], left[0] * right[1] + left[1] * right[0])


def times_conjugate(left, right):
    return (left[0] * right[0] + left[1] * right[1], left[1] * right[0] - left[0] * right[1])


def block_core(extended, cotangent, taps, skip_gain, response, to_spectrum, to_signal, after_rows):
    count = cotangent.shape[1]
    batch = cotangent.shape[0]
    mixed = taps[0] * extended[:, 2:] + taps[1] * extended[:, 1:-1] + taps[2] * extended[:, :-2]
    query_feat = mixed[:, :, 0]
    key_feat = mixed[:, :, 1]
    value_feat = mixed[:, :, 2]
    product = (key_feat * value_feat).astype(jnp.bfloat16)
    stacked = to_spectrum(jnp.concatenate([product, response[None]], axis=0))
    prod_spec = (stacked[0][:batch], stacked[1][:batch])
    resp_spec = (stacked[0][batch:], stacked[1][batch:])
    conv_out = to_signal(times_spectrum(prod_spec, resp_spec))
    carried = conv_out + skip_gain * product
    gated = (query_feat * carried).astype(jnp.bfloat16)
    grad_carried = (cotangent * query_feat).astype(jnp.bfloat16)
    grad_query = cotangent * carried
    grad_spec = to_spectrum(grad_carried)
    back_conv = times_conjugate(grad_spec, resp_spec)
    resp_grad = times_conjugate(grad_spec, prod_spec)
    joined_real = jnp.concatenate(
        [back_conv[0], jnp.sum(resp_grad[0], axis=0, keepdims=True)], axis=0
    )
    joined_imag = jnp.concatenate(
        [back_conv[1], jnp.sum(resp_grad[1], axis=0, keepdims=True)], axis=0
    )
    both = to_signal((joined_real, joined_imag))
    grad_product = both[:batch] + skip_gain * grad_carried
    grad_mixed = jnp.stack([grad_query, grad_product * value_feat, grad_product * key_feat], axis=2)
    tail = jnp.concatenate([grad_mixed, after_rows(grad_mixed[:, :2])], axis=1)
    grad_feats = (
        taps[0] * tail[:, :count] + taps[1] * tail[:, 1 : count + 1] + taps[2] * tail[:, 2:]
    ).astype(jnp.bfloat16)
    grad_taps = jnp.stack(
        [
            jnp.sum(grad_mixed * extended[:, 2 - tap_index : 2 - tap_index + count], axis=(0, 1))
            for tap_index in range(3)
        ]
    )
    grad_skip = jnp.sum(grad_carried.astype(jnp.float32) * product.astype(jnp.float32), axis=(0, 1))
    return (gated, grad_feats, grad_taps, grad_skip, both[batch])


def local(features, short_filter, response, skip_gain, cotangent):
    seq_parts = lax.axis_size("seq")
    seq_index = lax.axis_index("seq")
    batch = features.shape[0]
    tok_rows = features.shape[1]
    chan_width = features.shape[2] // 3
    length = seq_parts * tok_rows
    taps = short_filter.reshape(3, 3, chan_width)
    narrow = chan_width // seq_parts
    offset = seq_index * narrow
    moved_feats, moved_cot, moved_resp = (
        lax.all_to_all(
            features.reshape(batch, 1, tok_rows, 3, chan_width),
            "seq",
            split_axis=4,
            concat_axis=1,
            tiled=True,
        ),
        lax.all_to_all(
            cotangent.reshape(batch, 1, tok_rows, 1, chan_width),
            "seq",
            split_axis=4,
            concat_axis=1,
            tiled=True,
        ),
        lax.all_to_all(
            response.reshape(1, 1, tok_rows, 1, chan_width),
            "seq",
            split_axis=4,
            concat_axis=1,
            tiled=True,
        ),
    )
    local_feats = moved_feats.reshape(batch, length, 3, narrow)
    local_cot = moved_cot.reshape(batch, length, narrow)
    local_resp = moved_resp.reshape(length, narrow)
    extended = jnp.concatenate(
        [jnp.zeros((batch, 2, 3, narrow), features.dtype), local_feats], axis=1
    )
    fft_length = 2 * length

    def local_spectrum(signal):
        blocks = signal.reshape(signal.shape[0], seq_parts, tok_rows, narrow).astype(jnp.float32)
        part_real, part_imag = across_blocks(
            blocks, jnp.arange(tok_rows, dtype=jnp.int32), seq_parts, fft_length
        )
        return within_blocks(part_real, part_imag)

    def local_signal(spectrum):
        part_real, part_imag = back_within(
            spectrum[0], spectrum[1], jnp.arange(2 * seq_parts, dtype=jnp.int32), fft_length
        )
        values = back_across(part_real, part_imag, seq_parts, fft_length)
        return values.reshape(values.shape[0], length, narrow)

    def no_rows(rows_part):
        return jnp.zeros_like(rows_part)

    gated, grad_feats, grad_taps, grad_skip, filter_part = block_core(
        extended,
        local_cot,
        lax.dynamic_slice_in_dim(taps, offset, narrow, 2),
        lax.dynamic_slice_in_dim(skip_gain, offset, narrow, 0),
        local_resp,
        local_spectrum,
        local_signal,
        no_rows,
    )
    gated, grad_feats = (
        lax.all_to_all(
            gated.reshape(batch, seq_parts, tok_rows, 1, narrow),
            "seq",
            split_axis=1,
            concat_axis=4,
            tiled=True,
        ),
        lax.all_to_all(
            grad_feats.reshape(batch, seq_parts, tok_rows, 3, narrow),
            "seq",
            split_axis=1,
            concat_axis=4,
            tiled=True,
        ),
    )
    dp_parts = lax.axis_size("dp")
    extra = 16
    small = jnp.concatenate(
        [grad_taps.reshape(9, narrow), grad_skip[None], jnp.zeros((extra - 10, narrow), jnp.float32)],
        axis=0,
    )
    chunks = jnp.concatenate(
        [
            filter_part.reshape(seq_parts, tok_rows, narrow),
            jnp.broadcast_to(small[None], (seq_parts, extra, narrow)),
        ],
        axis=1,
    )
    moved = lax.all_to_all(
        chunks.reshape(1, seq_parts, tok_rows + extra, 1, narrow),
        "seq",
        split_axis=1,
        concat_axis=4,
        tiled=True,
    ).reshape(tok_rows + extra, chan_width)
    block = chan_width // dp_parts
    small_all = moved[tok_rows : tok_rows + 10]
    small_rows = small_all.reshape(10, dp_parts, block).transpose(1, 0, 2).reshape(dp_parts * 10, block)
    joined = jnp.concatenate([moved[:tok_rows], jnp.tile(small_rows, (1, dp_parts))], axis=0)
    reduced = lax.psum_scatter(joined, "dp", scatter_dimension=1, tiled=True)
    filter_total = reduced[:tok_rows]
    small_total = (
        reduced[tok_rows:].reshape(dp_parts, 10, block).transpose(1, 0, 2).reshape(10, chan_width)
    )
    gated = gated.reshape(batch, tok_rows, chan_width)
    grad_feats = grad_feats.reshape(batch, tok_rows, 3 * chan_width)
    totals = (small_total[:9].reshape(3, 3 * chan_width), small_total[9])
    return (gated, grad_feats, totals[0], totals[1], filter_total)


def solution(mesh):
    placed = (P("dp", "seq", None), P(), P("seq", None), P(), P("dp", "seq", None))
    return jax.shard_map(
        local,
        mesh=mesh,
        in_specs=placed,
        out_specs=(P("dp", "seq", None), P("dp", "seq", None), P(), P(), P("seq", "dp")),
        check_vma=False,
    )
```

```python
import math

import jax
import jax.numpy as jnp
from jax import lax
from jax.sharding import PartitionSpec as P

precise = lax.Precision.HIGHEST


def dft_table(count):
    series = jnp.arange(count, dtype=jnp.int32)
    angle = (series[:, None] * series[None, :] % count).astype(jnp.float32) * (
        2.0 * math.pi / count
    )
    return (jnp.cos(angle), jnp.sin(angle))


def across_blocks(signal, offsets, blocks, fft_length):
    double = jnp.arange(2 * blocks, dtype=jnp.int32)
    single = jnp.arange(blocks, dtype=jnp.int32)
    angle = (double[:, None] * single[None, :] % (2 * blocks)).astype(jnp.float32) * (
        math.pi / blocks
    )
    table = jnp.stack([jnp.cos(angle), -jnp.sin(angle)])
    first = jnp.einsum("oap,bpjk->obajk", table, signal, precision=precise)
    twist = (double[:, None] * offsets[None, :] % fft_length).astype(jnp.float32) * (
        -2.0 * math.pi / fft_length
    )
    cosine = jnp.cos(twist)[None, :, :, None]
    sine = jnp.sin(twist)[None, :, :, None]
    return (first[0] * cosine - first[1] * sine, first[0] * sine + first[1] * cosine)


def within_blocks(part_real, part_imag):
    table_cos, table_sin = dft_table(part_real.shape[2])
    table = jnp.stack([jnp.stack([table_cos, table_sin]), jnp.stack([-table_sin, table_cos])])
    spectra = jnp.einsum(
        "oibj,ixajk->oxabk", table, jnp.stack([part_real, part_imag]), precision=precise
    )
    return (spectra[0], spectra[1])


def back_within(spec_real, spec_imag, firsts, fft_length):
    count = spec_real.shape[2]
    table_cos, table_sin = dft_table(count)
    table = jnp.stack([jnp.stack([table_cos, -table_sin]), jnp.stack([table_sin, table_cos])])
    backs = jnp.einsum(
        "oibj,ixabk->oxajk", table, jnp.stack([spec_real, spec_imag]), precision=precise
    )
    series = jnp.arange(count, dtype=jnp.int32)
    twist = (firsts[:, None] * series[None, :] % fft_length).astype(jnp.float32) * (
        2.0 * math.pi / fft_length
    )
    cosine = jnp.cos(twist)[None, :, :, None]
    sine = jnp.sin(twist)[None, :, :, None]
    return (backs[0] * cosine - backs[1] * sine, backs[0] * sine + backs[1] * cosine)


def back_across(part_real, part_imag, blocks, fft_length):
    double = jnp.arange(2 * blocks, dtype=jnp.int32)
    single = jnp.arange(blocks, dtype=jnp.int32)
    angle = (single[:, None] * double[None, :] % (2 * blocks)).astype(jnp.float32) * (
        math.pi / blocks
    )
    table = jnp.stack([jnp.cos(angle), -jnp.sin(angle)])
    result = jnp.einsum(
        "ipa,ibajk->bpjk", table, jnp.stack([part_real, part_imag]), precision=precise
    )
    return result * (1.0 / fft_length)


def times_spectrum(left, right):
    return (left[0] * right[0] - left[1] * right[1], left[0] * right[1] + left[1] * right[0])


def times_conjugate(left, right):
    return (left[0] * right[0] + left[1] * right[1], left[1] * right[0] - left[0] * right[1])


def block_core(extended, cotangent, taps, skip_gain, response, to_spectrum, to_signal, after_rows):
    count = cotangent.shape[1]
    batch = cotangent.shape[0]
    mixed = taps[0] * extended[:, 2:] + taps[1] * extended[:, 1:-1] + taps[2] * extended[:, :-2]
    query_feat = mixed[:, :, 0]
    key_feat = mixed[:, :, 1]
    value_feat = mixed[:, :, 2]
    product = (key_feat * value_feat).astype(jnp.bfloat16)
    stacked = to_spectrum(jnp.concatenate([product, response[None]], axis=0))
    prod_spec = (stacked[0][:batch], stacked[1][:batch])
    resp_spec = (stacked[0][batch:], stacked[1][batch:])
    conv_out = to_signal(times_spectrum(prod_spec, resp_spec))
    carried = conv_out + skip_gain * product
    gated = (query_feat * carried).astype(jnp.bfloat16)
    grad_carried = (cotangent * query_feat).astype(jnp.bfloat16)
    grad_query = cotangent * carried
    grad_spec = to_spectrum(grad_carried)
    back_conv = times_conjugate(grad_spec, resp_spec)
    resp_grad = times_conjugate(grad_spec, prod_spec)
    joined_real = jnp.concatenate(
        [back_conv[0], jnp.sum(resp_grad[0], axis=0, keepdims=True)], axis=0
    )
    joined_imag = jnp.concatenate(
        [back_conv[1], jnp.sum(resp_grad[1], axis=0, keepdims=True)], axis=0
    )
    both = to_signal((joined_real, joined_imag))
    grad_product = both[:batch] + skip_gain * grad_carried
    grad_mixed = jnp.stack([grad_query, grad_product * value_feat, grad_product * key_feat], axis=2)
    tail = jnp.concatenate([grad_mixed, after_rows(grad_mixed[:, :2])], axis=1)
    grad_feats = (
        taps[0] * tail[:, :count] + taps[1] * tail[:, 1 : count + 1] + taps[2] * tail[:, 2:]
    ).astype(jnp.bfloat16)
    grad_taps = jnp.stack(
        [
            jnp.sum(grad_mixed * extended[:, 2 - tap_index : 2 - tap_index + count], axis=(0, 1))
            for tap_index in range(3)
        ]
    )
    grad_skip = jnp.sum(grad_carried.astype(jnp.float32) * product.astype(jnp.float32), axis=(0, 1))
    return (gated, grad_feats, grad_taps, grad_skip, both[batch])


def local(features, short_filter, response, skip_gain, cotangent):
    seq_parts = lax.axis_size("seq")
    seq_index = lax.axis_index("seq")
    batch = features.shape[0]
    tok_rows = features.shape[1]
    chan_width = features.shape[2] // 3
    length = seq_parts * tok_rows
    taps = short_filter.reshape(3, 3, chan_width)
    narrow = chan_width // seq_parts
    offset = seq_index * narrow
    joined_in = jnp.concatenate(
        [
            features.reshape(tok_rows, 3 * chan_width),
            cotangent.reshape(tok_rows, chan_width),
            response,
        ],
        axis=1,
    )
    arranged = joined_in.reshape(tok_rows, 5, seq_parts, narrow).transpose(2, 0, 1, 3)
    moved_in = lax.all_to_all(arranged, "seq", 0, 0, tiled=True).reshape(length, 5, narrow)
    moved_feats = moved_in[:, :3]
    moved_cot = moved_in[:, 3]
    moved_resp = moved_in[:, 4]
    local_feats = moved_feats.reshape(batch, length, 3, narrow)
    local_cot = moved_cot.reshape(batch, length, narrow)
    local_resp = moved_resp
    extended = jnp.concatenate(
        [jnp.zeros((batch, 2, 3, narrow), features.dtype), local_feats], axis=1
    )
    fft_length = 2 * length

    def local_spectrum(signal):
        blocks = signal.reshape(signal.shape[0], seq_parts, tok_rows, narrow).astype(jnp.float32)
        part_real, part_imag = across_blocks(
            blocks, jnp.arange(tok_rows, dtype=jnp.int32), seq_parts, fft_length
        )
        return within_blocks(part_real, part_imag)

    def local_signal(spectrum):
        part_real, part_imag = back_within(
            spectrum[0], spectrum[1], jnp.arange(2 * seq_parts, dtype=jnp.int32), fft_length
        )
        values = back_across(part_real, part_imag, seq_parts, fft_length)
        return values.reshape(values.shape[0], length, narrow)

    def no_rows(rows_part):
        return jnp.zeros_like(rows_part)

    gated, grad_feats, grad_taps, grad_skip, filter_part = block_core(
        extended,
        local_cot,
        lax.dynamic_slice_in_dim(taps, offset, narrow, 2),
        lax.dynamic_slice_in_dim(skip_gain, offset, narrow, 0),
        local_resp,
        local_spectrum,
        local_signal,
        no_rows,
    )
    gated = lax.all_to_all(
        gated.reshape(seq_parts, tok_rows, narrow), "seq", 0, 0, tiled=True
    ).transpose(1, 0, 2)
    grad_feats = lax.all_to_all(
        grad_feats.reshape(seq_parts, tok_rows, 3, narrow), "seq", 0, 0, tiled=True
    ).transpose(1, 2, 0, 3)
    dp_parts = lax.axis_size("dp")
    extra = 16
    small = jnp.concatenate(
        [grad_taps.reshape(9, narrow), grad_skip[None], jnp.zeros((extra - 10, narrow), jnp.float32)],
        axis=0,
    )
    chunks = jnp.concatenate(
        [
            filter_part.reshape(seq_parts, tok_rows, narrow),
            jnp.broadcast_to(small[None], (seq_parts, extra, narrow)),
        ],
        axis=1,
    )
    moved = (
        lax.all_to_all(chunks, "seq", 0, 0, tiled=True)
        .transpose(1, 0, 2)
        .reshape(tok_rows + extra, chan_width)
    )
    block = chan_width // dp_parts
    small_all = moved[tok_rows : tok_rows + 10]
    small_rows = small_all.reshape(10, dp_parts, block).transpose(1, 0, 2).reshape(dp_parts * 10, block)
    joined = jnp.concatenate([moved[:tok_rows], jnp.tile(small_rows, (1, dp_parts))], axis=0)
    reduced = lax.psum_scatter(joined, "dp", scatter_dimension=1, tiled=True)
    filter_total = reduced[:tok_rows]
    small_total = (
        reduced[tok_rows:].reshape(dp_parts, 10, block).transpose(1, 0, 2).reshape(10, chan_width)
    )
    gated = gated.reshape(batch, tok_rows, chan_width)
    grad_feats = grad_feats.reshape(batch, tok_rows, 3 * chan_width)
    totals = (small_total[:9].reshape(3, 3 * chan_width), small_total[9])
    return (gated, grad_feats, totals[0], totals[1], filter_total)


def solution(mesh):
    placed = (P("dp", "seq", None), P(), P("seq", None), P(), P("dp", "seq", None))
    return jax.shard_map(
        local,
        mesh=mesh,
        in_specs=placed,
        out_specs=(P("dp", "seq", None), P("dp", "seq", None), P(), P(), P("seq", "dp")),
        check_vma=False,
    )
```

```python
import math

import jax
import jax.numpy as jnp
from jax import lax
from jax.sharding import PartitionSpec as P


precise = lax.Precision.HIGHEST


def dft_table(count):
    series = jnp.arange(count, dtype=jnp.int32)
    angle = (series[:, None] * series[None, :] % count).astype(jnp.float32) * (
        2.0 * math.pi / count
    )
    return (jnp.cos(angle), jnp.sin(angle))


def across_blocks(signal, offsets, blocks, fft_length):
    double = jnp.arange(2 * blocks, dtype=jnp.int32)
    single = jnp.arange(blocks, dtype=jnp.int32)
    angle = (double[:, None] * single[None, :] % (2 * blocks)).astype(jnp.float32) * (
        math.pi / blocks
    )
    table = jnp.stack([jnp.cos(angle), -jnp.sin(angle)])
    first = jnp.einsum("oap,bpjk->obajk", table, signal, precision=precise)
    twist = (double[:, None] * offsets[None, :] % fft_length).astype(jnp.float32) * (
        -2.0 * math.pi / fft_length
    )
    cosine = jnp.cos(twist)[None, :, :, None]
    sine = jnp.sin(twist)[None, :, :, None]
    return (first[0] * cosine - first[1] * sine, first[0] * sine + first[1] * cosine)


def within_blocks(part_real, part_imag):
    table_cos, table_sin = dft_table(part_real.shape[2])
    table = jnp.stack([jnp.stack([table_cos, table_sin]), jnp.stack([-table_sin, table_cos])])
    spectra = jnp.einsum(
        "oibj,ixajk->oxabk", table, jnp.stack([part_real, part_imag]), precision=precise
    )
    return (spectra[0], spectra[1])


def back_within(spec_real, spec_imag, firsts, fft_length):
    count = spec_real.shape[2]
    table_cos, table_sin = dft_table(count)
    table = jnp.stack([jnp.stack([table_cos, -table_sin]), jnp.stack([table_sin, table_cos])])
    backs = jnp.einsum(
        "oibj,ixabk->oxajk", table, jnp.stack([spec_real, spec_imag]), precision=precise
    )
    series = jnp.arange(count, dtype=jnp.int32)
    twist = (firsts[:, None] * series[None, :] % fft_length).astype(jnp.float32) * (
        2.0 * math.pi / fft_length
    )
    cosine = jnp.cos(twist)[None, :, :, None]
    sine = jnp.sin(twist)[None, :, :, None]
    return (backs[0] * cosine - backs[1] * sine, backs[0] * sine + backs[1] * cosine)


def back_across(part_real, part_imag, blocks, fft_length):
    double = jnp.arange(2 * blocks, dtype=jnp.int32)
    single = jnp.arange(blocks, dtype=jnp.int32)
    angle = (single[:, None] * double[None, :] % (2 * blocks)).astype(jnp.float32) * (
        math.pi / blocks
    )
    table = jnp.stack([jnp.cos(angle), -jnp.sin(angle)])
    result = jnp.einsum(
        "ipa,ibajk->bpjk", table, jnp.stack([part_real, part_imag]), precision=precise
    )
    return result * (1.0 / fft_length)


def times_spectrum(left, right):
    return (left[0] * right[0] - left[1] * right[1], left[0] * right[1] + left[1] * right[0])


def times_conjugate(left, right):
    return (left[0] * right[0] + left[1] * right[1], left[1] * right[0] - left[0] * right[1])


def blocked_core(extended, cotangent, taps, skip_gain, response, to_spectrum, to_signal, after_rows):
    count = cotangent.shape[1]
    batch = cotangent.shape[0]
    mixed = taps[0] * extended[:, 2:] + taps[1] * extended[:, 1:-1] + taps[2] * extended[:, :-2]
    query_feat = mixed[:, :, 0]
    key_feat = mixed[:, :, 1]
    value_feat = mixed[:, :, 2]
    product = (key_feat * value_feat).astype(jnp.bfloat16)
    stacked = to_spectrum(jnp.concatenate([product, response[None]], axis=0))
    prod_spec = (stacked[0][:batch], stacked[1][:batch])
    resp_spec = (stacked[0][batch:], stacked[1][batch:])
    conv_out = to_signal(times_spectrum(prod_spec, resp_spec))
    carried = conv_out + skip_gain * product
    gated = (query_feat * carried).astype(jnp.bfloat16)
    grad_carried = (cotangent * query_feat).astype(jnp.bfloat16)
    grad_query = cotangent * carried
    grad_spec = to_spectrum(grad_carried)
    back_conv = times_conjugate(grad_spec, resp_spec)
    resp_grad = times_conjugate(grad_spec, prod_spec)
    joined_real = jnp.concatenate(
        [back_conv[0], jnp.sum(resp_grad[0], axis=0, keepdims=True)], axis=0
    )
    joined_imag = jnp.concatenate(
        [back_conv[1], jnp.sum(resp_grad[1], axis=0, keepdims=True)], axis=0
    )
    both = to_signal((joined_real, joined_imag))
    grad_product = both[:batch] + skip_gain * grad_carried
    grad_mixed = jnp.stack([grad_query, grad_product * value_feat, grad_product * key_feat], axis=2)
    tail = jnp.concatenate([grad_mixed, after_rows(grad_mixed[:, :2])], axis=1)
    grad_feats = (
        taps[0] * tail[:, :count] + taps[1] * tail[:, 1 : count + 1] + taps[2] * tail[:, 2:]
    ).astype(jnp.bfloat16)
    grad_taps = jnp.stack(
        [
            jnp.sum(grad_mixed * extended[:, 2 - tap_index : 2 - tap_index + count], axis=(0, 1))
            for tap_index in range(3)
        ]
    )
    grad_skip = jnp.sum(grad_carried.astype(jnp.float32) * product.astype(jnp.float32), axis=(0, 1))
    return (gated, grad_feats, grad_taps, grad_skip, both[batch])


def dft_tables(length):
    fft_length = 2 * length
    bins = length + 1
    freq = lax.broadcasted_iota(jnp.int32, (bins, length), 0)
    time = lax.broadcasted_iota(jnp.int32, (bins, length), 1)
    angle = lax.optimization_barrier((freq * time) % fft_length).astype(jnp.float32) * (
        2.0 * math.pi / fft_length
    )
    table = jnp.concatenate([jnp.cos(angle), -jnp.sin(angle)], axis=0)
    high = table.astype(jnp.bfloat16)
    low = (table - high.astype(jnp.float32)).astype(jnp.bfloat16)
    return high, low


def bf16_dot(left, right, dims):
    return lax.dot_general(left, right, (dims, ((), ())), preferred_element_type=jnp.float32)


def to_spectrum(tables, signal):
    high, low = tables
    forward = ((1,), (0,))
    return bf16_dot(high, signal, forward) + bf16_dot(low, signal, forward)


def to_signal(tables, spectrum):
    high, low = tables
    bins = high.shape[0] // 2
    fft_length = 2 * (bins - 1)
    row = lax.broadcasted_iota(jnp.int32, (2 * bins, 1), 0)
    edge = (row == 0) | (row == bins - 1) | (row == bins) | (row == 2 * bins - 1)
    weight = jnp.where(edge, 1.0 / fft_length, 2.0 / fft_length)
    scaled = spectrum * weight
    spec_high = scaled.astype(jnp.bfloat16)
    spec_low = (scaled - spec_high.astype(jnp.float32)).astype(jnp.bfloat16)
    backward = ((0,), (0,))
    return (
        bf16_dot(high, spec_high, backward)
        + bf16_dot(high, spec_low, backward)
        + bf16_dot(low, spec_high, backward)
    )


def split(spectrum):
    bins = spectrum.shape[0] // 2
    return spectrum[:bins], spectrum[bins:]


def join(real, imag):
    return jnp.concatenate([real, imag], axis=0)


def block_core(feats, cot, resp, taps, skip_gain):
    length = feats.shape[0]
    narrow = feats.shape[2]
    tables = dft_tables(length)
    extended = jnp.concatenate([jnp.zeros((2, 3, narrow), feats.dtype), feats], axis=0)
    mixed = taps[0] * extended[2:] + taps[1] * extended[1:-1] + taps[2] * extended[:-2]
    query_feat = mixed[:, 0]
    key_feat = mixed[:, 1]
    value_feat = mixed[:, 2]
    product = (key_feat * value_feat).astype(jnp.bfloat16)
    first = to_spectrum(tables, jnp.concatenate([product, resp], axis=1))
    prod_re, prod_im = split(first[:, :narrow])
    resp_re, resp_im = split(first[:, narrow:])
    conv_out = to_signal(
        tables, join(prod_re * resp_re - prod_im * resp_im, prod_re * resp_im + prod_im * resp_re)
    )
    carried = conv_out + skip_gain * product
    gated = (query_feat * carried).astype(jnp.bfloat16)
    grad_carried = (cot * query_feat).astype(jnp.bfloat16)
    grad_query = cot * carried
    grad_re, grad_im = split(to_spectrum(tables, grad_carried))
    back_spec = join(grad_re * resp_re + grad_im * resp_im, grad_im * resp_re - grad_re * resp_im)
    filt_spec = join(grad_re * prod_re + grad_im * prod_im, grad_im * prod_re - grad_re * prod_im)
    both = to_signal(tables, jnp.concatenate([back_spec, filt_spec], axis=1))
    grad_product = both[:, :narrow] + skip_gain * grad_carried
    grad_mixed = jnp.stack([grad_query, grad_product * value_feat, grad_product * key_feat], axis=1)
    tail = jnp.concatenate([grad_mixed, jnp.zeros((2, 3, narrow), jnp.float32)], axis=0)
    grad_feats = (
        taps[0] * tail[:length] + taps[1] * tail[1 : length + 1] + taps[2] * tail[2:]
    ).astype(jnp.bfloat16)
    grad_taps = jnp.stack(
        [
            jnp.sum(grad_mixed * extended[2 - tap_index : 2 - tap_index + length], axis=0)
            for tap_index in range(3)
        ]
    )
    grad_skip = jnp.sum(grad_carried.astype(jnp.float32) * product.astype(jnp.float32), axis=0)
    return gated, grad_feats, grad_taps, grad_skip, both[:, narrow:]


def blocked_fallback(moved_in, taps, skip_gain, seq_parts, tok_rows, narrow):
    length = seq_parts * tok_rows
    fft_length = 2 * length
    local_feats = moved_in[None, :, :3]
    extended = jnp.concatenate(
        [jnp.zeros((1, 2, 3, narrow), local_feats.dtype), local_feats], axis=1
    )

    def local_spectrum(signal):
        blocks = signal.reshape(signal.shape[0], seq_parts, tok_rows, narrow).astype(jnp.float32)
        part_real, part_imag = across_blocks(
            blocks, jnp.arange(tok_rows, dtype=jnp.int32), seq_parts, fft_length
        )
        return within_blocks(part_real, part_imag)

    def local_signal(spectrum):
        part_real, part_imag = back_within(
            spectrum[0], spectrum[1], jnp.arange(2 * seq_parts, dtype=jnp.int32), fft_length
        )
        values = back_across(part_real, part_imag, seq_parts, fft_length)
        return values.reshape(values.shape[0], length, narrow)

    def no_rows(rows_part):
        return jnp.zeros_like(rows_part)

    return blocked_core(
        extended,
        moved_in[None, :, 3],
        taps,
        skip_gain,
        moved_in[:, 4],
        local_spectrum,
        local_signal,
        no_rows,
    )


def local(features, short_filter, response, skip_gain, cotangent):
    seq_parts = lax.axis_size("seq")
    dp_parts = lax.axis_size("dp")
    seq_index = lax.axis_index("seq")
    tok_rows = features.shape[1]
    chan_width = features.shape[2] // 3
    length = seq_parts * tok_rows
    narrow = chan_width // seq_parts
    offset = seq_index * narrow
    taps = short_filter.reshape(3, 3, chan_width)
    joined_in = jnp.concatenate(
        [
            features.reshape(tok_rows, 3 * chan_width),
            cotangent.reshape(tok_rows, chan_width),
            response,
        ],
        axis=1,
    )
    arranged = joined_in.reshape(tok_rows, 5, seq_parts, narrow).transpose(2, 0, 1, 3)
    moved_in = lax.all_to_all(arranged, "seq", 0, 0, tiled=True).reshape(length, 5, narrow)
    local_taps = lax.dynamic_slice_in_dim(taps, offset, narrow, 2)
    local_skip = lax.dynamic_slice_in_dim(skip_gain, offset, narrow, 0)
    if length <= 2048:
        gated, grad_feats, grad_taps, grad_skip, filter_part = block_core(
            moved_in[:, :3], moved_in[:, 3], moved_in[:, 4], local_taps, local_skip
        )
    else:
        gated, grad_feats, grad_taps, grad_skip, filter_part = blocked_fallback(
            moved_in, local_taps, local_skip, seq_parts, tok_rows, narrow
        )
        gated = gated.reshape(length, narrow)
        grad_feats = grad_feats.reshape(length, 3, narrow)
    gated = lax.all_to_all(
        gated.reshape(seq_parts, tok_rows, narrow), "seq", 0, 0, tiled=True
    ).transpose(1, 0, 2)
    grad_feats = lax.all_to_all(
        grad_feats.reshape(seq_parts, tok_rows, 3, narrow), "seq", 0, 0, tiled=True
    ).transpose(1, 2, 0, 3)
    extra = 16
    small = jnp.concatenate(
        [grad_taps.reshape(9, narrow), grad_skip[None], jnp.zeros((extra - 10, narrow), jnp.float32)],
        axis=0,
    )
    chunks = jnp.concatenate(
        [
            filter_part.reshape(seq_parts, tok_rows, narrow),
            jnp.broadcast_to(small[None], (seq_parts, extra, narrow)),
        ],
        axis=1,
    )
    moved = (
        lax.all_to_all(chunks, "seq", 0, 0, tiled=True)
        .transpose(1, 0, 2)
        .reshape(tok_rows + extra, chan_width)
    )
    block = chan_width // dp_parts
    small_all = moved[tok_rows : tok_rows + 10]
    small_rows = small_all.reshape(10, dp_parts, block).transpose(1, 0, 2).reshape(dp_parts * 10, block)
    joined = jnp.concatenate([moved[:tok_rows], jnp.tile(small_rows, (1, dp_parts))], axis=0)
    reduced = lax.psum_scatter(joined, "dp", scatter_dimension=1, tiled=True)
    filter_total = reduced[:tok_rows]
    small_total = (
        reduced[tok_rows:].reshape(dp_parts, 10, block).transpose(1, 0, 2).reshape(10, chan_width)
    )
    gated = gated.reshape(1, tok_rows, chan_width)
    grad_feats = grad_feats.reshape(1, tok_rows, 3 * chan_width)
    return (
        gated,
        grad_feats,
        small_total[:9].reshape(3, 3 * chan_width),
        small_total[9],
        filter_total,
    )


def solution(mesh):
    placed = (P("dp", "seq", None), P(), P("seq", None), P(), P("dp", "seq", None))
    return jax.shard_map(
        local,
        mesh=mesh,
        in_specs=placed,
        out_specs=(P("dp", "seq", None), P("dp", "seq", None), P(), P(), P("seq", "dp")),
        check_vma=False,
    )
```

```python
import math

import jax
import jax.numpy as jnp
from jax import lax
from jax.sharding import PartitionSpec as P


precise = lax.Precision.HIGHEST


def dft_table(count):
    series = jnp.arange(count, dtype=jnp.int32)
    angle = (series[:, None] * series[None, :] % count).astype(jnp.float32) * (
        2.0 * math.pi / count
    )
    return (jnp.cos(angle), jnp.sin(angle))


def across_blocks(signal, offsets, blocks, fft_length):
    double = jnp.arange(2 * blocks, dtype=jnp.int32)
    single = jnp.arange(blocks, dtype=jnp.int32)
    angle = (double[:, None] * single[None, :] % (2 * blocks)).astype(jnp.float32) * (
        math.pi / blocks
    )
    table = jnp.stack([jnp.cos(angle), -jnp.sin(angle)])
    first = jnp.einsum("oap,bpjk->obajk", table, signal, precision=precise)
    twist = (double[:, None] * offsets[None, :] % fft_length).astype(jnp.float32) * (
        -2.0 * math.pi / fft_length
    )
    cosine = jnp.cos(twist)[None, :, :, None]
    sine = jnp.sin(twist)[None, :, :, None]
    return (first[0] * cosine - first[1] * sine, first[0] * sine + first[1] * cosine)


def within_blocks(part_real, part_imag):
    table_cos, table_sin = dft_table(part_real.shape[2])
    table = jnp.stack([jnp.stack([table_cos, table_sin]), jnp.stack([-table_sin, table_cos])])
    spectra = jnp.einsum(
        "oibj,ixajk->oxabk", table, jnp.stack([part_real, part_imag]), precision=precise
    )
    return (spectra[0], spectra[1])


def back_within(spec_real, spec_imag, firsts, fft_length):
    count = spec_real.shape[2]
    table_cos, table_sin = dft_table(count)
    table = jnp.stack([jnp.stack([table_cos, -table_sin]), jnp.stack([table_sin, table_cos])])
    backs = jnp.einsum(
        "oibj,ixabk->oxajk", table, jnp.stack([spec_real, spec_imag]), precision=precise
    )
    series = jnp.arange(count, dtype=jnp.int32)
    twist = (firsts[:, None] * series[None, :] % fft_length).astype(jnp.float32) * (
        2.0 * math.pi / fft_length
    )
    cosine = jnp.cos(twist)[None, :, :, None]
    sine = jnp.sin(twist)[None, :, :, None]
    return (backs[0] * cosine - backs[1] * sine, backs[0] * sine + backs[1] * cosine)


def back_across(part_real, part_imag, blocks, fft_length):
    double = jnp.arange(2 * blocks, dtype=jnp.int32)
    single = jnp.arange(blocks, dtype=jnp.int32)
    angle = (single[:, None] * double[None, :] % (2 * blocks)).astype(jnp.float32) * (
        math.pi / blocks
    )
    table = jnp.stack([jnp.cos(angle), -jnp.sin(angle)])
    result = jnp.einsum(
        "ipa,ibajk->bpjk", table, jnp.stack([part_real, part_imag]), precision=precise
    )
    return result * (1.0 / fft_length)


def times_spectrum(left, right):
    return (left[0] * right[0] - left[1] * right[1], left[0] * right[1] + left[1] * right[0])


def times_conjugate(left, right):
    return (left[0] * right[0] + left[1] * right[1], left[1] * right[0] - left[0] * right[1])


def blocked_core(extended, cotangent, taps, skip_gain, response, to_spectrum, to_signal, after_rows):
    count = cotangent.shape[1]
    batch = cotangent.shape[0]
    mixed = taps[0] * extended[:, 2:] + taps[1] * extended[:, 1:-1] + taps[2] * extended[:, :-2]
    query_feat = mixed[:, :, 0]
    key_feat = mixed[:, :, 1]
    value_feat = mixed[:, :, 2]
    product = (key_feat * value_feat).astype(jnp.bfloat16)
    stacked = to_spectrum(jnp.concatenate([product, response[None]], axis=0))
    prod_spec = (stacked[0][:batch], stacked[1][:batch])
    resp_spec = (stacked[0][batch:], stacked[1][batch:])
    conv_out = to_signal(times_spectrum(prod_spec, resp_spec))
    carried = conv_out + skip_gain * product
    gated = (query_feat * carried).astype(jnp.bfloat16)
    grad_carried = (cotangent * query_feat).astype(jnp.bfloat16)
    grad_query = cotangent * carried
    grad_spec = to_spectrum(grad_carried)
    back_conv = times_conjugate(grad_spec, resp_spec)
    resp_grad = times_conjugate(grad_spec, prod_spec)
    joined_real = jnp.concatenate(
        [back_conv[0], jnp.sum(resp_grad[0], axis=0, keepdims=True)], axis=0
    )
    joined_imag = jnp.concatenate(
        [back_conv[1], jnp.sum(resp_grad[1], axis=0, keepdims=True)], axis=0
    )
    both = to_signal((joined_real, joined_imag))
    grad_product = both[:batch] + skip_gain * grad_carried
    grad_mixed = jnp.stack([grad_query, grad_product * value_feat, grad_product * key_feat], axis=2)
    tail = jnp.concatenate([grad_mixed, after_rows(grad_mixed[:, :2])], axis=1)
    grad_feats = (
        taps[0] * tail[:, :count] + taps[1] * tail[:, 1 : count + 1] + taps[2] * tail[:, 2:]
    ).astype(jnp.bfloat16)
    grad_taps = jnp.stack(
        [
            jnp.sum(grad_mixed * extended[:, 2 - tap_index : 2 - tap_index + count], axis=(0, 1))
            for tap_index in range(3)
        ]
    )
    grad_skip = jnp.sum(grad_carried.astype(jnp.float32) * product.astype(jnp.float32), axis=(0, 1))
    return (gated, grad_feats, grad_taps, grad_skip, both[batch])


def dft_tables(length):
    fft_length = 2 * length
    bins = length + 1
    freq = lax.broadcasted_iota(jnp.int32, (bins, length), 0)
    time = lax.broadcasted_iota(jnp.int32, (bins, length), 1)
    angle = lax.optimization_barrier((freq * time) % fft_length).astype(jnp.float32) * (
        2.0 * math.pi / fft_length
    )
    table = jnp.concatenate([jnp.cos(angle), -jnp.sin(angle)], axis=0)
    high = table.astype(jnp.bfloat16)
    low = (table - high.astype(jnp.float32)).astype(jnp.bfloat16)
    return high, low


def bf16_dot(left, right, dims):
    return lax.dot_general(left, right, (dims, ((), ())), preferred_element_type=jnp.float32)


def to_spectrum(tables, signal):
    high, low = tables
    forward = ((1,), (0,))
    return bf16_dot(high, signal, forward) + bf16_dot(low, signal, forward)


def to_signal(tables, spectrum):
    high, low = tables
    bins = high.shape[0] // 2
    fft_length = 2 * (bins - 1)
    row = lax.broadcasted_iota(jnp.int32, (2 * bins, 1), 0)
    edge = (row == 0) | (row == bins - 1) | (row == bins) | (row == 2 * bins - 1)
    weight = jnp.where(edge, 1.0 / fft_length, 2.0 / fft_length)
    scaled = spectrum * weight
    spec_high = scaled.astype(jnp.bfloat16)
    spec_low = (scaled - spec_high.astype(jnp.float32)).astype(jnp.bfloat16)
    backward = ((0,), (0,))
    return (
        bf16_dot(high, spec_high, backward)
        + bf16_dot(high, spec_low, backward)
        + bf16_dot(low, spec_high, backward)
    )


def split(spectrum):
    bins = spectrum.shape[0] // 2
    return spectrum[:bins], spectrum[bins:]


def join(real, imag):
    return jnp.concatenate([real, imag], axis=0)


def block_core(feats, cot, resp, taps, skip_gain, filter_exchange, filter_reduce):
    length = feats.shape[0]
    narrow = feats.shape[2]
    tables = dft_tables(length)
    extended = jnp.concatenate([jnp.zeros((2, 3, narrow), feats.dtype), feats], axis=0)
    mixed = taps[0] * extended[2:] + taps[1] * extended[1:-1] + taps[2] * extended[:-2]
    query_feat = mixed[:, 0]
    key_feat = mixed[:, 1]
    value_feat = mixed[:, 2]
    product = (key_feat * value_feat).astype(jnp.bfloat16)
    first = to_spectrum(tables, jnp.concatenate([product, resp], axis=1))
    prod_re, prod_im = split(first[:, :narrow])
    resp_re, resp_im = split(first[:, narrow:])
    conv_out = to_signal(
        tables, join(prod_re * resp_re - prod_im * resp_im, prod_re * resp_im + prod_im * resp_re)
    )
    carried = conv_out + skip_gain * product
    gated = (query_feat * carried).astype(jnp.bfloat16)
    grad_carried = (cot * query_feat).astype(jnp.bfloat16)
    grad_query = cot * carried
    grad_re, grad_im = split(to_spectrum(tables, grad_carried))
    back_spec = join(grad_re * resp_re + grad_im * resp_im, grad_im * resp_re - grad_re * resp_im)
    filt_spec = join(grad_re * prod_re + grad_im * prod_im, grad_im * prod_re - grad_re * prod_im)
    filter_part = to_signal(tables, filt_spec)
    filter_moved = filter_exchange(filter_part)
    back_spec, filter_moved = lax.optimization_barrier((back_spec, filter_moved))
    filter_total = filter_reduce(filter_moved)
    back_conv = to_signal(tables, back_spec)
    grad_product = back_conv + skip_gain * grad_carried
    grad_mixed = jnp.stack([grad_query, grad_product * value_feat, grad_product * key_feat], axis=1)
    tail = jnp.concatenate([grad_mixed, jnp.zeros((2, 3, narrow), jnp.float32)], axis=0)
    grad_feats = (
        taps[0] * tail[:length] + taps[1] * tail[1 : length + 1] + taps[2] * tail[2:]
    ).astype(jnp.bfloat16)
    grad_taps = jnp.stack(
        [
            jnp.sum(grad_mixed * extended[2 - tap_index : 2 - tap_index + length], axis=0)
            for tap_index in range(3)
        ]
    )
    grad_skip = jnp.sum(grad_carried.astype(jnp.float32) * product.astype(jnp.float32), axis=0)
    return gated, grad_feats, grad_taps, grad_skip, filter_total


def blocked_fallback(moved_in, taps, skip_gain, seq_parts, tok_rows, narrow):
    length = seq_parts * tok_rows
    fft_length = 2 * length
    local_feats = moved_in[None, :, :3]
    extended = jnp.concatenate(
        [jnp.zeros((1, 2, 3, narrow), local_feats.dtype), local_feats], axis=1
    )

    def local_spectrum(signal):
        blocks = signal.reshape(signal.shape[0], seq_parts, tok_rows, narrow).astype(jnp.float32)
        part_real, part_imag = across_blocks(
            blocks, jnp.arange(tok_rows, dtype=jnp.int32), seq_parts, fft_length
        )
        return within_blocks(part_real, part_imag)

    def local_signal(spectrum):
        part_real, part_imag = back_within(
            spectrum[0], spectrum[1], jnp.arange(2 * seq_parts, dtype=jnp.int32), fft_length
        )
        values = back_across(part_real, part_imag, seq_parts, fft_length)
        return values.reshape(values.shape[0], length, narrow)

    def no_rows(rows_part):
        return jnp.zeros_like(rows_part)

    return blocked_core(
        extended,
        moved_in[None, :, 3],
        taps,
        skip_gain,
        moved_in[:, 4],
        local_spectrum,
        local_signal,
        no_rows,
    )


def local(features, short_filter, response, skip_gain, cotangent):
    seq_parts = lax.axis_size("seq")
    dp_parts = lax.axis_size("dp")
    seq_index = lax.axis_index("seq")
    tok_rows = features.shape[1]
    chan_width = features.shape[2] // 3
    length = seq_parts * tok_rows
    narrow = chan_width // seq_parts
    offset = seq_index * narrow
    taps = short_filter.reshape(3, 3, chan_width)
    joined_in = jnp.concatenate(
        [
            features.reshape(tok_rows, 3 * chan_width),
            cotangent.reshape(tok_rows, chan_width),
            response,
        ],
        axis=1,
    )
    arranged = joined_in.reshape(tok_rows, 5, seq_parts, narrow).transpose(2, 0, 1, 3)
    moved_in = lax.all_to_all(arranged, "seq", 0, 0, tiled=True).reshape(length, 5, narrow)
    def filter_exchange(filter_part):
        return lax.all_to_all(
            filter_part.reshape(seq_parts, tok_rows, narrow), "seq", 0, 0, tiled=True
        )

    def filter_reduce(moved):
        moved = moved.transpose(1, 0, 2).reshape(tok_rows, chan_width)
        return lax.psum_scatter(moved, "dp", scatter_dimension=1, tiled=True)

    local_taps = lax.dynamic_slice_in_dim(taps, offset, narrow, 2)
    local_skip = lax.dynamic_slice_in_dim(skip_gain, offset, narrow, 0)
    if length <= 2048:
        gated, grad_feats, grad_taps, grad_skip, filter_total = block_core(
            moved_in[:, :3], moved_in[:, 3], moved_in[:, 4], local_taps, local_skip, filter_exchange, filter_reduce
        )
    else:
        gated, grad_feats, grad_taps, grad_skip, filter_part = blocked_fallback(
            moved_in, local_taps, local_skip, seq_parts, tok_rows, narrow
        )
        filter_total = filter_reduce(filter_exchange(filter_part))
        gated = gated.reshape(length, narrow)
        grad_feats = grad_feats.reshape(length, 3, narrow)
    gated = lax.all_to_all(
        gated.reshape(seq_parts, tok_rows, narrow), "seq", 0, 0, tiled=True
    ).transpose(1, 0, 2)
    grad_feats = lax.all_to_all(
        grad_feats.reshape(seq_parts, tok_rows, 3, narrow), "seq", 0, 0, tiled=True
    ).transpose(1, 2, 0, 3)
    extra = 16
    small = jnp.concatenate(
        [grad_taps.reshape(9, narrow), grad_skip[None], jnp.zeros((extra - 10, narrow), jnp.float32)],
        axis=0,
    )
    small_all = (
        lax.all_to_all(jnp.broadcast_to(small[None], (seq_parts, extra, narrow)), "seq", 0, 0, tiled=True)
        .transpose(1, 0, 2)
        .reshape(extra, chan_width)
    )
    small_all, filter_total = lax.optimization_barrier((small_all, filter_total))
    small_total = lax.psum(small_all, "dp")
    gated = gated.reshape(1, tok_rows, chan_width)
    grad_feats = grad_feats.reshape(1, tok_rows, 3 * chan_width)
    return (
        gated,
        grad_feats,
        small_total[:9].reshape(3, 3 * chan_width),
        small_total[9],
        filter_total,
    )


def solution(mesh):
    placed = (P("dp", "seq", None), P(), P("seq", None), P(), P("dp", "seq", None))
    return jax.shard_map(
        local,
        mesh=mesh,
        in_specs=placed,
        out_specs=(P("dp", "seq", None), P("dp", "seq", None), P(), P(), P("seq", "dp")),
        check_vma=False,
    )
```

```python
import math

import jax
import jax.numpy as jnp
from jax import lax
from jax.sharding import PartitionSpec as P


precise = lax.Precision.HIGHEST


def dft_table(count):
    series = jnp.arange(count, dtype=jnp.int32)
    angle = (series[:, None] * series[None, :] % count).astype(jnp.float32) * (
        2.0 * math.pi / count
    )
    return (jnp.cos(angle), jnp.sin(angle))


def across_blocks(signal, offsets, blocks, fft_length):
    double = jnp.arange(2 * blocks, dtype=jnp.int32)
    single = jnp.arange(blocks, dtype=jnp.int32)
    angle = (double[:, None] * single[None, :] % (2 * blocks)).astype(jnp.float32) * (
        math.pi / blocks
    )
    table = jnp.stack([jnp.cos(angle), -jnp.sin(angle)])
    first = jnp.einsum("oap,bpjk->obajk", table, signal, precision=precise)
    twist = (double[:, None] * offsets[None, :] % fft_length).astype(jnp.float32) * (
        -2.0 * math.pi / fft_length
    )
    cosine = jnp.cos(twist)[None, :, :, None]
    sine = jnp.sin(twist)[None, :, :, None]
    return (first[0] * cosine - first[1] * sine, first[0] * sine + first[1] * cosine)


def within_blocks(part_real, part_imag):
    table_cos, table_sin = dft_table(part_real.shape[2])
    table = jnp.stack([jnp.stack([table_cos, table_sin]), jnp.stack([-table_sin, table_cos])])
    spectra = jnp.einsum(
        "oibj,ixajk->oxabk", table, jnp.stack([part_real, part_imag]), precision=precise
    )
    return (spectra[0], spectra[1])


def back_within(spec_real, spec_imag, firsts, fft_length):
    count = spec_real.shape[2]
    table_cos, table_sin = dft_table(count)
    table = jnp.stack([jnp.stack([table_cos, -table_sin]), jnp.stack([table_sin, table_cos])])
    backs = jnp.einsum(
        "oibj,ixabk->oxajk", table, jnp.stack([spec_real, spec_imag]), precision=precise
    )
    series = jnp.arange(count, dtype=jnp.int32)
    twist = (firsts[:, None] * series[None, :] % fft_length).astype(jnp.float32) * (
        2.0 * math.pi / fft_length
    )
    cosine = jnp.cos(twist)[None, :, :, None]
    sine = jnp.sin(twist)[None, :, :, None]
    return (backs[0] * cosine - backs[1] * sine, backs[0] * sine + backs[1] * cosine)


def back_across(part_real, part_imag, blocks, fft_length):
    double = jnp.arange(2 * blocks, dtype=jnp.int32)
    single = jnp.arange(blocks, dtype=jnp.int32)
    angle = (single[:, None] * double[None, :] % (2 * blocks)).astype(jnp.float32) * (
        math.pi / blocks
    )
    table = jnp.stack([jnp.cos(angle), -jnp.sin(angle)])
    result = jnp.einsum(
        "ipa,ibajk->bpjk", table, jnp.stack([part_real, part_imag]), precision=precise
    )
    return result * (1.0 / fft_length)


def times_spectrum(left, right):
    return (left[0] * right[0] - left[1] * right[1], left[0] * right[1] + left[1] * right[0])


def times_conjugate(left, right):
    return (left[0] * right[0] + left[1] * right[1], left[1] * right[0] - left[0] * right[1])


def blocked_core(extended, cotangent, taps, skip_gain, response, to_spectrum, to_signal, after_rows):
    count = cotangent.shape[1]
    batch = cotangent.shape[0]
    mixed = taps[0] * extended[:, 2:] + taps[1] * extended[:, 1:-1] + taps[2] * extended[:, :-2]
    query_feat = mixed[:, :, 0]
    key_feat = mixed[:, :, 1]
    value_feat = mixed[:, :, 2]
    product = (key_feat * value_feat).astype(jnp.bfloat16)
    stacked = to_spectrum(jnp.concatenate([product, response[None]], axis=0))
    prod_spec = (stacked[0][:batch], stacked[1][:batch])
    resp_spec = (stacked[0][batch:], stacked[1][batch:])
    conv_out = to_signal(times_spectrum(prod_spec, resp_spec))
    carried = conv_out + skip_gain * product
    gated = (query_feat * carried).astype(jnp.bfloat16)
    grad_carried = (cotangent * query_feat).astype(jnp.bfloat16)
    grad_query = cotangent * carried
    grad_spec = to_spectrum(grad_carried)
    back_conv = times_conjugate(grad_spec, resp_spec)
    resp_grad = times_conjugate(grad_spec, prod_spec)
    joined_real = jnp.concatenate(
        [back_conv[0], jnp.sum(resp_grad[0], axis=0, keepdims=True)], axis=0
    )
    joined_imag = jnp.concatenate(
        [back_conv[1], jnp.sum(resp_grad[1], axis=0, keepdims=True)], axis=0
    )
    both = to_signal((joined_real, joined_imag))
    grad_product = both[:batch] + skip_gain * grad_carried
    grad_mixed = jnp.stack([grad_query, grad_product * value_feat, grad_product * key_feat], axis=2)
    tail = jnp.concatenate([grad_mixed, after_rows(grad_mixed[:, :2])], axis=1)
    grad_feats = (
        taps[0] * tail[:, :count] + taps[1] * tail[:, 1 : count + 1] + taps[2] * tail[:, 2:]
    ).astype(jnp.bfloat16)
    grad_taps = jnp.stack(
        [
            jnp.sum(grad_mixed * extended[:, 2 - tap_index : 2 - tap_index + count], axis=(0, 1))
            for tap_index in range(3)
        ]
    )
    grad_skip = jnp.sum(grad_carried.astype(jnp.float32) * product.astype(jnp.float32), axis=(0, 1))
    return (gated, grad_feats, grad_taps, grad_skip, both[batch])


def dft_tables(length):
    fft_length = 2 * length
    bins = length + 1
    freq = lax.broadcasted_iota(jnp.int32, (bins, length), 0)
    time = lax.broadcasted_iota(jnp.int32, (bins, length), 1)
    angle = lax.optimization_barrier((freq * time) % fft_length).astype(jnp.float32) * (
        2.0 * math.pi / fft_length
    )
    table = jnp.concatenate([jnp.cos(angle), -jnp.sin(angle)], axis=0)
    high = table.astype(jnp.bfloat16)
    low = (table - high.astype(jnp.float32)).astype(jnp.bfloat16)
    return high, low


def bf16_dot(left, right, dims):
    return lax.dot_general(left, right, (dims, ((), ())), preferred_element_type=jnp.float32)


def to_spectrum(tables, signal):
    high, low = tables
    forward = ((1,), (0,))
    return bf16_dot(high, signal, forward) + bf16_dot(low, signal, forward)


def to_signal(tables, spectrum):
    high, low = tables
    bins = high.shape[0] // 2
    fft_length = 2 * (bins - 1)
    row = lax.broadcasted_iota(jnp.int32, (2 * bins, 1), 0)
    edge = (row == 0) | (row == bins - 1) | (row == bins) | (row == 2 * bins - 1)
    weight = jnp.where(edge, 1.0 / fft_length, 2.0 / fft_length)
    scaled = spectrum * weight
    spec_high = scaled.astype(jnp.bfloat16)
    spec_low = (scaled - spec_high.astype(jnp.float32)).astype(jnp.bfloat16)
    backward = ((0,), (0,))
    return (
        bf16_dot(high, spec_high, backward)
        + bf16_dot(high, spec_low, backward)
        + bf16_dot(low, spec_high, backward)
    )


def split(spectrum):
    bins = spectrum.shape[0] // 2
    return spectrum[:bins], spectrum[bins:]


def join(real, imag):
    return jnp.concatenate([real, imag], axis=0)


def block_core(feats, cot, resp, taps, skip_gain, gated_exchange):
    length = feats.shape[0]
    narrow = feats.shape[2]
    tables = dft_tables(length)
    extended = jnp.concatenate([jnp.zeros((2, 3, narrow), feats.dtype), feats], axis=0)
    mixed = taps[0] * extended[2:] + taps[1] * extended[1:-1] + taps[2] * extended[:-2]
    query_feat = mixed[:, 0]
    key_feat = mixed[:, 1]
    value_feat = mixed[:, 2]
    product = (key_feat * value_feat).astype(jnp.bfloat16)
    first = to_spectrum(tables, jnp.concatenate([product, resp], axis=1))
    prod_re, prod_im = split(first[:, :narrow])
    resp_re, resp_im = split(first[:, narrow:])
    conv_out = to_signal(
        tables, join(prod_re * resp_re - prod_im * resp_im, prod_re * resp_im + prod_im * resp_re)
    )
    carried = conv_out + skip_gain * product
    gated = (query_feat * carried).astype(jnp.bfloat16)
    grad_carried = (cot * query_feat).astype(jnp.bfloat16)
    grad_query = cot * carried
    gated_moved = gated_exchange(gated)
    grad_re, grad_im = split(to_spectrum(tables, grad_carried))
    back_spec = join(grad_re * resp_re + grad_im * resp_im, grad_im * resp_re - grad_re * resp_im)
    filt_spec = join(grad_re * prod_re + grad_im * prod_im, grad_im * prod_re - grad_re * prod_im)
    back_spec, gated_moved = lax.optimization_barrier((back_spec, gated_moved))
    back_conv = to_signal(tables, back_spec)
    grad_product = back_conv + skip_gain * grad_carried
    grad_mixed = jnp.stack([grad_query, grad_product * value_feat, grad_product * key_feat], axis=1)
    tail = jnp.concatenate([grad_mixed, jnp.zeros((2, 3, narrow), jnp.float32)], axis=0)
    grad_feats = (
        taps[0] * tail[:length] + taps[1] * tail[1 : length + 1] + taps[2] * tail[2:]
    ).astype(jnp.bfloat16)
    grad_taps = jnp.stack(
        [
            jnp.sum(grad_mixed * extended[2 - tap_index : 2 - tap_index + length], axis=0)
            for tap_index in range(3)
        ]
    )
    grad_skip = jnp.sum(grad_carried.astype(jnp.float32) * product.astype(jnp.float32), axis=0)
    filter_part = to_signal(tables, filt_spec)
    return gated_moved, grad_feats, grad_taps, grad_skip, filter_part


def blocked_fallback(moved_in, taps, skip_gain, seq_parts, tok_rows, narrow):
    length = seq_parts * tok_rows
    fft_length = 2 * length
    local_feats = moved_in[None, :, :3]
    extended = jnp.concatenate(
        [jnp.zeros((1, 2, 3, narrow), local_feats.dtype), local_feats], axis=1
    )

    def local_spectrum(signal):
        blocks = signal.reshape(signal.shape[0], seq_parts, tok_rows, narrow).astype(jnp.float32)
        part_real, part_imag = across_blocks(
            blocks, jnp.arange(tok_rows, dtype=jnp.int32), seq_parts, fft_length
        )
        return within_blocks(part_real, part_imag)

    def local_signal(spectrum):
        part_real, part_imag = back_within(
            spectrum[0], spectrum[1], jnp.arange(2 * seq_parts, dtype=jnp.int32), fft_length
        )
        values = back_across(part_real, part_imag, seq_parts, fft_length)
        return values.reshape(values.shape[0], length, narrow)

    def no_rows(rows_part):
        return jnp.zeros_like(rows_part)

    return blocked_core(
        extended,
        moved_in[None, :, 3],
        taps,
        skip_gain,
        moved_in[:, 4],
        local_spectrum,
        local_signal,
        no_rows,
    )


def local(features, short_filter, response, skip_gain, cotangent):
    seq_parts = lax.axis_size("seq")
    dp_parts = lax.axis_size("dp")
    seq_index = lax.axis_index("seq")
    tok_rows = features.shape[1]
    chan_width = features.shape[2] // 3
    length = seq_parts * tok_rows
    narrow = chan_width // seq_parts
    offset = seq_index * narrow
    taps = short_filter.reshape(3, 3, chan_width)
    joined_in = jnp.concatenate(
        [
            features.reshape(tok_rows, 3 * chan_width),
            cotangent.reshape(tok_rows, chan_width),
            response,
        ],
        axis=1,
    )
    arranged = joined_in.reshape(tok_rows, 5, seq_parts, narrow).transpose(2, 0, 1, 3)
    moved_in = lax.all_to_all(arranged, "seq", 0, 0, tiled=True).reshape(length, 5, narrow)
    local_taps = lax.dynamic_slice_in_dim(taps, offset, narrow, 2)
    local_skip = lax.dynamic_slice_in_dim(skip_gain, offset, narrow, 0)
    def gated_exchange(gated):
        return lax.all_to_all(gated.reshape(seq_parts, tok_rows, narrow), "seq", 0, 0, tiled=True)

    if length <= 2048:
        gated, grad_feats, grad_taps, grad_skip, filter_part = block_core(
            moved_in[:, :3], moved_in[:, 3], moved_in[:, 4], local_taps, local_skip, gated_exchange
        )
    else:
        gated, grad_feats, grad_taps, grad_skip, filter_part = blocked_fallback(
            moved_in, local_taps, local_skip, seq_parts, tok_rows, narrow
        )
        gated = gated_exchange(gated.reshape(length, narrow))
        grad_feats = grad_feats.reshape(length, 3, narrow)
    gated = gated.transpose(1, 0, 2)
    extra = 16
    small = jnp.concatenate(
        [grad_taps.reshape(9, narrow), grad_skip[None], jnp.zeros((extra - 10, narrow), jnp.float32)],
        axis=0,
    )
    chunks = jnp.concatenate(
        [
            filter_part.reshape(seq_parts, tok_rows, narrow),
            jnp.broadcast_to(small[None], (seq_parts, extra, narrow)),
        ],
        axis=1,
    )
    moved = (
        lax.all_to_all(chunks, "seq", 0, 0, tiled=True)
        .transpose(1, 0, 2)
        .reshape(tok_rows + extra, chan_width)
    )
    grad_feats, moved = lax.optimization_barrier((grad_feats, moved))
    grad_feats = lax.all_to_all(
        grad_feats.reshape(seq_parts, tok_rows, 3, narrow), "seq", 0, 0, tiled=True
    ).transpose(1, 2, 0, 3)
    block = chan_width // dp_parts
    small_all = moved[tok_rows : tok_rows + 10]
    small_rows = small_all.reshape(10, dp_parts, block).transpose(1, 0, 2).reshape(dp_parts * 10, block)
    joined = jnp.concatenate([moved[:tok_rows], jnp.tile(small_rows, (1, dp_parts))], axis=0)
    reduced = lax.psum_scatter(joined, "dp", scatter_dimension=1, tiled=True)
    filter_total = reduced[:tok_rows]
    small_total = (
        reduced[tok_rows:].reshape(dp_parts, 10, block).transpose(1, 0, 2).reshape(10, chan_width)
    )
    gated = gated.reshape(1, tok_rows, chan_width)
    grad_feats = grad_feats.reshape(1, tok_rows, 3 * chan_width)
    return (
        gated,
        grad_feats,
        small_total[:9].reshape(3, 3 * chan_width),
        small_total[9],
        filter_total,
    )


def solution(mesh):
    placed = (P("dp", "seq", None), P(), P("seq", None), P(), P("dp", "seq", None))
    return jax.shard_map(
        local,
        mesh=mesh,
        in_specs=placed,
        out_specs=(P("dp", "seq", None), P("dp", "seq", None), P(), P(), P("seq", "dp")),
        check_vma=False,
    )
```

```python
import math

import jax
import jax.numpy as jnp
from jax import lax
from jax.sharding import PartitionSpec as P


precise = lax.Precision.HIGHEST


def dft_table(count):
    series = jnp.arange(count, dtype=jnp.int32)
    angle = (series[:, None] * series[None, :] % count).astype(jnp.float32) * (
        2.0 * math.pi / count
    )
    return (jnp.cos(angle), jnp.sin(angle))


def across_blocks(signal, offsets, blocks, fft_length):
    double = jnp.arange(2 * blocks, dtype=jnp.int32)
    single = jnp.arange(blocks, dtype=jnp.int32)
    angle = (double[:, None] * single[None, :] % (2 * blocks)).astype(jnp.float32) * (
        math.pi / blocks
    )
    table = jnp.stack([jnp.cos(angle), -jnp.sin(angle)])
    first = jnp.einsum("oap,bpjk->obajk", table, signal, precision=precise)
    twist = (double[:, None] * offsets[None, :] % fft_length).astype(jnp.float32) * (
        -2.0 * math.pi / fft_length
    )
    cosine = jnp.cos(twist)[None, :, :, None]
    sine = jnp.sin(twist)[None, :, :, None]
    return (first[0] * cosine - first[1] * sine, first[0] * sine + first[1] * cosine)


def within_blocks(part_real, part_imag):
    table_cos, table_sin = dft_table(part_real.shape[2])
    table = jnp.stack([jnp.stack([table_cos, table_sin]), jnp.stack([-table_sin, table_cos])])
    spectra = jnp.einsum(
        "oibj,ixajk->oxabk", table, jnp.stack([part_real, part_imag]), precision=precise
    )
    return (spectra[0], spectra[1])


def back_within(spec_real, spec_imag, firsts, fft_length):
    count = spec_real.shape[2]
    table_cos, table_sin = dft_table(count)
    table = jnp.stack([jnp.stack([table_cos, -table_sin]), jnp.stack([table_sin, table_cos])])
    backs = jnp.einsum(
        "oibj,ixabk->oxajk", table, jnp.stack([spec_real, spec_imag]), precision=precise
    )
    series = jnp.arange(count, dtype=jnp.int32)
    twist = (firsts[:, None] * series[None, :] % fft_length).astype(jnp.float32) * (
        2.0 * math.pi / fft_length
    )
    cosine = jnp.cos(twist)[None, :, :, None]
    sine = jnp.sin(twist)[None, :, :, None]
    return (backs[0] * cosine - backs[1] * sine, backs[0] * sine + backs[1] * cosine)


def back_across(part_real, part_imag, blocks, fft_length):
    double = jnp.arange(2 * blocks, dtype=jnp.int32)
    single = jnp.arange(blocks, dtype=jnp.int32)
    angle = (single[:, None] * double[None, :] % (2 * blocks)).astype(jnp.float32) * (
        math.pi / blocks
    )
    table = jnp.stack([jnp.cos(angle), -jnp.sin(angle)])
    result = jnp.einsum(
        "ipa,ibajk->bpjk", table, jnp.stack([part_real, part_imag]), precision=precise
    )
    return result * (1.0 / fft_length)


def times_spectrum(left, right):
    return (left[0] * right[0] - left[1] * right[1], left[0] * right[1] + left[1] * right[0])


def times_conjugate(left, right):
    return (left[0] * right[0] + left[1] * right[1], left[1] * right[0] - left[0] * right[1])


def blocked_core(extended, cotangent, taps, skip_gain, response, to_spectrum, to_signal, after_rows):
    count = cotangent.shape[1]
    batch = cotangent.shape[0]
    mixed = taps[0] * extended[:, 2:] + taps[1] * extended[:, 1:-1] + taps[2] * extended[:, :-2]
    query_feat = mixed[:, :, 0]
    key_feat = mixed[:, :, 1]
    value_feat = mixed[:, :, 2]
    product = (key_feat * value_feat).astype(jnp.bfloat16)
    stacked = to_spectrum(jnp.concatenate([product, response[None]], axis=0))
    prod_spec = (stacked[0][:batch], stacked[1][:batch])
    resp_spec = (stacked[0][batch:], stacked[1][batch:])
    conv_out = to_signal(times_spectrum(prod_spec, resp_spec))
    carried = conv_out + skip_gain * product
    gated = (query_feat * carried).astype(jnp.bfloat16)
    grad_carried = (cotangent * query_feat).astype(jnp.bfloat16)
    grad_query = cotangent * carried
    grad_spec = to_spectrum(grad_carried)
    back_conv = times_conjugate(grad_spec, resp_spec)
    resp_grad = times_conjugate(grad_spec, prod_spec)
    joined_real = jnp.concatenate(
        [back_conv[0], jnp.sum(resp_grad[0], axis=0, keepdims=True)], axis=0
    )
    joined_imag = jnp.concatenate(
        [back_conv[1], jnp.sum(resp_grad[1], axis=0, keepdims=True)], axis=0
    )
    both = to_signal((joined_real, joined_imag))
    grad_product = both[:batch] + skip_gain * grad_carried
    grad_mixed = jnp.stack([grad_query, grad_product * value_feat, grad_product * key_feat], axis=2)
    tail = jnp.concatenate([grad_mixed, after_rows(grad_mixed[:, :2])], axis=1)
    grad_feats = (
        taps[0] * tail[:, :count] + taps[1] * tail[:, 1 : count + 1] + taps[2] * tail[:, 2:]
    ).astype(jnp.bfloat16)
    grad_taps = jnp.stack(
        [
            jnp.sum(grad_mixed * extended[:, 2 - tap_index : 2 - tap_index + count], axis=(0, 1))
            for tap_index in range(3)
        ]
    )
    grad_skip = jnp.sum(grad_carried.astype(jnp.float32) * product.astype(jnp.float32), axis=(0, 1))
    return (gated, grad_feats, grad_taps, grad_skip, both[batch])


def dft_tables(length):
    fft_length = 2 * length
    bins = length + 1
    freq = lax.broadcasted_iota(jnp.int32, (bins, length), 0)
    time = lax.broadcasted_iota(jnp.int32, (bins, length), 1)
    angle = lax.optimization_barrier((freq * time) % fft_length).astype(jnp.float32) * (
        2.0 * math.pi / fft_length
    )
    table = jnp.concatenate([jnp.cos(angle), -jnp.sin(angle)], axis=0)
    high = table.astype(jnp.bfloat16)
    low = (table - high.astype(jnp.float32)).astype(jnp.bfloat16)
    return high, low


def bf16_dot(left, right, dims):
    return lax.dot_general(left, right, (dims, ((), ())), preferred_element_type=jnp.float32)


def to_spectrum(tables, signal):
    high, low = tables
    forward = ((1,), (0,))
    return bf16_dot(high, signal, forward) + bf16_dot(low, signal, forward)


def to_signal(tables, spectrum):
    high, low = tables
    bins = high.shape[0] // 2
    fft_length = 2 * (bins - 1)
    row = lax.broadcasted_iota(jnp.int32, (2 * bins, 1), 0)
    edge = (row == 0) | (row == bins - 1) | (row == bins) | (row == 2 * bins - 1)
    weight = jnp.where(edge, 1.0 / fft_length, 2.0 / fft_length)
    scaled = spectrum * weight
    spec_high = scaled.astype(jnp.bfloat16)
    spec_low = (scaled - spec_high.astype(jnp.float32)).astype(jnp.bfloat16)
    backward = ((0,), (0,))
    return (
        bf16_dot(high, spec_high, backward)
        + bf16_dot(high, spec_low, backward)
        + bf16_dot(low, spec_high, backward)
    )


def split(spectrum):
    bins = spectrum.shape[0] // 2
    return spectrum[:bins], spectrum[bins:]


def join(real, imag):
    return jnp.concatenate([real, imag], axis=0)


def block_core(feats, cot, resp, taps, skip_gain):
    length = feats.shape[0]
    narrow = feats.shape[2]
    tables = dft_tables(length)
    extended = jnp.concatenate([jnp.zeros((2, 3, narrow), feats.dtype), feats], axis=0)
    mixed = taps[0] * extended[2:] + taps[1] * extended[1:-1] + taps[2] * extended[:-2]
    query_feat = mixed[:, 0]
    key_feat = mixed[:, 1]
    value_feat = mixed[:, 2]
    product = (key_feat * value_feat).astype(jnp.bfloat16)
    first = to_spectrum(tables, jnp.concatenate([product, resp], axis=1))
    prod_re, prod_im = split(first[:, :narrow])
    resp_re, resp_im = split(first[:, narrow:])
    conv_out = to_signal(
        tables, join(prod_re * resp_re - prod_im * resp_im, prod_re * resp_im + prod_im * resp_re)
    )
    carried = conv_out + skip_gain * product
    gated = (query_feat * carried).astype(jnp.bfloat16)
    grad_carried = (cot * query_feat).astype(jnp.bfloat16)
    grad_query = cot * carried
    grad_re, grad_im = split(to_spectrum(tables, grad_carried))
    back_spec = join(grad_re * resp_re + grad_im * resp_im, grad_im * resp_re - grad_re * resp_im)
    filt_spec = join(grad_re * prod_re + grad_im * prod_im, grad_im * prod_re - grad_re * prod_im)
    both = to_signal(tables, jnp.concatenate([back_spec, filt_spec], axis=1))
    grad_product = both[:, :narrow] + skip_gain * grad_carried
    grad_mixed = jnp.stack([grad_query, grad_product * value_feat, grad_product * key_feat], axis=1)
    tail = jnp.concatenate([grad_mixed, jnp.zeros((2, 3, narrow), jnp.float32)], axis=0)
    grad_feats = (
        taps[0] * tail[:length] + taps[1] * tail[1 : length + 1] + taps[2] * tail[2:]
    ).astype(jnp.bfloat16)
    grad_taps = jnp.stack(
        [
            jnp.sum(grad_mixed * extended[2 - tap_index : 2 - tap_index + length], axis=0)
            for tap_index in range(3)
        ]
    )
    grad_skip = jnp.sum(grad_carried.astype(jnp.float32) * product.astype(jnp.float32), axis=0)
    return gated, grad_feats, grad_taps, grad_skip, both[:, narrow:]


def blocked_fallback(moved_in, taps, skip_gain, seq_parts, tok_rows, narrow):
    length = seq_parts * tok_rows
    fft_length = 2 * length
    local_feats = moved_in[None, :, :3]
    extended = jnp.concatenate(
        [jnp.zeros((1, 2, 3, narrow), local_feats.dtype), local_feats], axis=1
    )

    def local_spectrum(signal):
        blocks = signal.reshape(signal.shape[0], seq_parts, tok_rows, narrow).astype(jnp.float32)
        part_real, part_imag = across_blocks(
            blocks, jnp.arange(tok_rows, dtype=jnp.int32), seq_parts, fft_length
        )
        return within_blocks(part_real, part_imag)

    def local_signal(spectrum):
        part_real, part_imag = back_within(
            spectrum[0], spectrum[1], jnp.arange(2 * seq_parts, dtype=jnp.int32), fft_length
        )
        values = back_across(part_real, part_imag, seq_parts, fft_length)
        return values.reshape(values.shape[0], length, narrow)

    def no_rows(rows_part):
        return jnp.zeros_like(rows_part)

    return blocked_core(
        extended,
        moved_in[None, :, 3],
        taps,
        skip_gain,
        moved_in[:, 4],
        local_spectrum,
        local_signal,
        no_rows,
    )


def permuted_exchange(chunks, index, parts):
    received = [lax.dynamic_index_in_dim(chunks, index, 0, keepdims=False)]
    for shift in range(1, parts):
        outgoing = lax.dynamic_index_in_dim(chunks, (index + shift) % parts, 0, keepdims=False)
        pairs = [(source, (source + shift) % parts) for source in range(parts)]
        received.append(lax.ppermute(outgoing, "seq", pairs))
    relative = jnp.stack(received)
    order = (index - jnp.arange(parts, dtype=jnp.int32)) % parts
    return jnp.take(relative, order, axis=0)


def local(features, short_filter, response, skip_gain, cotangent):
    seq_parts = lax.axis_size("seq")
    dp_parts = lax.axis_size("dp")
    seq_index = lax.axis_index("seq")
    tok_rows = features.shape[1]
    chan_width = features.shape[2] // 3
    length = seq_parts * tok_rows
    narrow = chan_width // seq_parts
    offset = seq_index * narrow
    taps = short_filter.reshape(3, 3, chan_width)
    joined_in = jnp.concatenate(
        [
            features.reshape(tok_rows, 3 * chan_width),
            cotangent.reshape(tok_rows, chan_width),
            response,
        ],
        axis=1,
    )
    arranged = joined_in.reshape(tok_rows, 5, seq_parts, narrow).transpose(2, 0, 1, 3)
    moved_in = permuted_exchange(arranged, seq_index, seq_parts).reshape(length, 5, narrow)
    local_taps = lax.dynamic_slice_in_dim(taps, offset, narrow, 2)
    local_skip = lax.dynamic_slice_in_dim(skip_gain, offset, narrow, 0)
    if length <= 2048:
        gated, grad_feats, grad_taps, grad_skip, filter_part = block_core(
            moved_in[:, :3], moved_in[:, 3], moved_in[:, 4], local_taps, local_skip
        )
    else:
        gated, grad_feats, grad_taps, grad_skip, filter_part = blocked_fallback(
            moved_in, local_taps, local_skip, seq_parts, tok_rows, narrow
        )
        gated = gated.reshape(length, narrow)
        grad_feats = grad_feats.reshape(length, 3, narrow)
    gated = lax.all_to_all(
        gated.reshape(seq_parts, tok_rows, narrow), "seq", 0, 0, tiled=True
    ).transpose(1, 0, 2)
    grad_feats = lax.all_to_all(
        grad_feats.reshape(seq_parts, tok_rows, 3, narrow), "seq", 0, 0, tiled=True
    ).transpose(1, 2, 0, 3)
    extra = 16
    small = jnp.concatenate(
        [grad_taps.reshape(9, narrow), grad_skip[None], jnp.zeros((extra - 10, narrow), jnp.float32)],
        axis=0,
    )
    chunks = jnp.concatenate(
        [
            filter_part.reshape(seq_parts, tok_rows, narrow),
            jnp.broadcast_to(small[None], (seq_parts, extra, narrow)),
        ],
        axis=1,
    )
    moved = (
        lax.all_to_all(chunks, "seq", 0, 0, tiled=True)
        .transpose(1, 0, 2)
        .reshape(tok_rows + extra, chan_width)
    )
    block = chan_width // dp_parts
    small_all = moved[tok_rows : tok_rows + 10]
    small_rows = small_all.reshape(10, dp_parts, block).transpose(1, 0, 2).reshape(dp_parts * 10, block)
    joined = jnp.concatenate([moved[:tok_rows], jnp.tile(small_rows, (1, dp_parts))], axis=0)
    reduced = lax.psum_scatter(joined, "dp", scatter_dimension=1, tiled=True)
    filter_total = reduced[:tok_rows]
    small_total = (
        reduced[tok_rows:].reshape(dp_parts, 10, block).transpose(1, 0, 2).reshape(10, chan_width)
    )
    gated = gated.reshape(1, tok_rows, chan_width)
    grad_feats = grad_feats.reshape(1, tok_rows, 3 * chan_width)
    return (
        gated,
        grad_feats,
        small_total[:9].reshape(3, 3 * chan_width),
        small_total[9],
        filter_total,
    )


def solution(mesh):
    placed = (P("dp", "seq", None), P(), P("seq", None), P(), P("dp", "seq", None))
    return jax.shard_map(
        local,
        mesh=mesh,
        in_specs=placed,
        out_specs=(P("dp", "seq", None), P("dp", "seq", None), P(), P(), P("seq", "dp")),
        check_vma=False,
    )
```

```python
import math

import jax
import jax.numpy as jnp
from jax import lax
from jax.sharding import PartitionSpec as P


precise = lax.Precision.HIGHEST


def dft_table(count):
    series = jnp.arange(count, dtype=jnp.int32)
    angle = (series[:, None] * series[None, :] % count).astype(jnp.float32) * (
        2.0 * math.pi / count
    )
    return (jnp.cos(angle), jnp.sin(angle))


def across_blocks(signal, offsets, blocks, fft_length):
    double = jnp.arange(2 * blocks, dtype=jnp.int32)
    single = jnp.arange(blocks, dtype=jnp.int32)
    angle = (double[:, None] * single[None, :] % (2 * blocks)).astype(jnp.float32) * (
        math.pi / blocks
    )
    table = jnp.stack([jnp.cos(angle), -jnp.sin(angle)])
    first = jnp.einsum("oap,bpjk->obajk", table, signal, precision=precise)
    twist = (double[:, None] * offsets[None, :] % fft_length).astype(jnp.float32) * (
        -2.0 * math.pi / fft_length
    )
    cosine = jnp.cos(twist)[None, :, :, None]
    sine = jnp.sin(twist)[None, :, :, None]
    return (first[0] * cosine - first[1] * sine, first[0] * sine + first[1] * cosine)


def within_blocks(part_real, part_imag):
    table_cos, table_sin = dft_table(part_real.shape[2])
    table = jnp.stack([jnp.stack([table_cos, table_sin]), jnp.stack([-table_sin, table_cos])])
    spectra = jnp.einsum(
        "oibj,ixajk->oxabk", table, jnp.stack([part_real, part_imag]), precision=precise
    )
    return (spectra[0], spectra[1])


def back_within(spec_real, spec_imag, firsts, fft_length):
    count = spec_real.shape[2]
    table_cos, table_sin = dft_table(count)
    table = jnp.stack([jnp.stack([table_cos, -table_sin]), jnp.stack([table_sin, table_cos])])
    backs = jnp.einsum(
        "oibj,ixabk->oxajk", table, jnp.stack([spec_real, spec_imag]), precision=precise
    )
    series = jnp.arange(count, dtype=jnp.int32)
    twist = (firsts[:, None] * series[None, :] % fft_length).astype(jnp.float32) * (
        2.0 * math.pi / fft_length
    )
    cosine = jnp.cos(twist)[None, :, :, None]
    sine = jnp.sin(twist)[None, :, :, None]
    return (backs[0] * cosine - backs[1] * sine, backs[0] * sine + backs[1] * cosine)


def back_across(part_real, part_imag, blocks, fft_length):
    double = jnp.arange(2 * blocks, dtype=jnp.int32)
    single = jnp.arange(blocks, dtype=jnp.int32)
    angle = (single[:, None] * double[None, :] % (2 * blocks)).astype(jnp.float32) * (
        math.pi / blocks
    )
    table = jnp.stack([jnp.cos(angle), -jnp.sin(angle)])
    result = jnp.einsum(
        "ipa,ibajk->bpjk", table, jnp.stack([part_real, part_imag]), precision=precise
    )
    return result * (1.0 / fft_length)


def times_spectrum(left, right):
    return (left[0] * right[0] - left[1] * right[1], left[0] * right[1] + left[1] * right[0])


def times_conjugate(left, right):
    return (left[0] * right[0] + left[1] * right[1], left[1] * right[0] - left[0] * right[1])


def blocked_core(extended, cotangent, taps, skip_gain, response, to_spectrum, to_signal, after_rows):
    count = cotangent.shape[1]
    batch = cotangent.shape[0]
    mixed = taps[0] * extended[:, 2:] + taps[1] * extended[:, 1:-1] + taps[2] * extended[:, :-2]
    query_feat = mixed[:, :, 0]
    key_feat = mixed[:, :, 1]
    value_feat = mixed[:, :, 2]
    product = (key_feat * value_feat).astype(jnp.bfloat16)
    stacked = to_spectrum(jnp.concatenate([product, response[None]], axis=0))
    prod_spec = (stacked[0][:batch], stacked[1][:batch])
    resp_spec = (stacked[0][batch:], stacked[1][batch:])
    conv_out = to_signal(times_spectrum(prod_spec, resp_spec))
    carried = conv_out + skip_gain * product
    gated = (query_feat * carried).astype(jnp.bfloat16)
    grad_carried = (cotangent * query_feat).astype(jnp.bfloat16)
    grad_query = cotangent * carried
    grad_spec = to_spectrum(grad_carried)
    back_conv = times_conjugate(grad_spec, resp_spec)
    resp_grad = times_conjugate(grad_spec, prod_spec)
    joined_real = jnp.concatenate(
        [back_conv[0], jnp.sum(resp_grad[0], axis=0, keepdims=True)], axis=0
    )
    joined_imag = jnp.concatenate(
        [back_conv[1], jnp.sum(resp_grad[1], axis=0, keepdims=True)], axis=0
    )
    both = to_signal((joined_real, joined_imag))
    grad_product = both[:batch] + skip_gain * grad_carried
    grad_mixed = jnp.stack([grad_query, grad_product * value_feat, grad_product * key_feat], axis=2)
    tail = jnp.concatenate([grad_mixed, after_rows(grad_mixed[:, :2])], axis=1)
    grad_feats = (
        taps[0] * tail[:, :count] + taps[1] * tail[:, 1 : count + 1] + taps[2] * tail[:, 2:]
    ).astype(jnp.bfloat16)
    grad_taps = jnp.stack(
        [
            jnp.sum(grad_mixed * extended[:, 2 - tap_index : 2 - tap_index + count], axis=(0, 1))
            for tap_index in range(3)
        ]
    )
    grad_skip = jnp.sum(grad_carried.astype(jnp.float32) * product.astype(jnp.float32), axis=(0, 1))
    return (gated, grad_feats, grad_taps, grad_skip, both[batch])


def dft_tables(length):
    fft_length = 2 * length
    bins = length + 1
    freq = lax.broadcasted_iota(jnp.int32, (bins, length), 0)
    time = lax.broadcasted_iota(jnp.int32, (bins, length), 1)
    angle = lax.optimization_barrier((freq * time) % fft_length).astype(jnp.float32) * (
        2.0 * math.pi / fft_length
    )
    table = jnp.concatenate([jnp.cos(angle), -jnp.sin(angle)], axis=0)
    high = table.astype(jnp.bfloat16)
    low = (table - high.astype(jnp.float32)).astype(jnp.bfloat16)
    return high, low


def bf16_dot(left, right, dims):
    return lax.dot_general(left, right, (dims, ((), ())), preferred_element_type=jnp.float32)


def to_spectrum(tables, signal):
    high, low = tables
    forward = ((1,), (0,))
    return bf16_dot(high, signal, forward) + bf16_dot(low, signal, forward)


def to_signal(tables, spectrum):
    high, low = tables
    bins = high.shape[0] // 2
    fft_length = 2 * (bins - 1)
    row = lax.broadcasted_iota(jnp.int32, (2 * bins, 1), 0)
    edge = (row == 0) | (row == bins - 1) | (row == bins) | (row == 2 * bins - 1)
    weight = jnp.where(edge, 1.0 / fft_length, 2.0 / fft_length)
    scaled = spectrum * weight
    spec_high = scaled.astype(jnp.bfloat16)
    spec_low = (scaled - spec_high.astype(jnp.float32)).astype(jnp.bfloat16)
    backward = ((0,), (0,))
    return (
        bf16_dot(high, spec_high, backward)
        + bf16_dot(high, spec_low, backward)
        + bf16_dot(low, spec_high, backward)
    )


def split(spectrum):
    bins = spectrum.shape[0] // 2
    return spectrum[:bins], spectrum[bins:]


def join(real, imag):
    return jnp.concatenate([real, imag], axis=0)


def block_core(feats, cot, resp, taps, skip_gain):
    length = feats.shape[0]
    narrow = feats.shape[2]
    tables = dft_tables(length)
    extended = jnp.concatenate([jnp.zeros((2, 3, narrow), feats.dtype), feats], axis=0)
    mixed = taps[0] * extended[2:] + taps[1] * extended[1:-1] + taps[2] * extended[:-2]
    query_feat = mixed[:, 0]
    key_feat = mixed[:, 1]
    value_feat = mixed[:, 2]
    product = (key_feat * value_feat).astype(jnp.bfloat16)
    first = to_spectrum(tables, jnp.concatenate([product, resp], axis=1))
    prod_re, prod_im = split(first[:, :narrow])
    resp_re, resp_im = split(first[:, narrow:])
    conv_out = to_signal(
        tables, join(prod_re * resp_re - prod_im * resp_im, prod_re * resp_im + prod_im * resp_re)
    )
    carried = conv_out + skip_gain * product
    gated = (query_feat * carried).astype(jnp.bfloat16)
    grad_carried = (cot * query_feat).astype(jnp.bfloat16)
    grad_query = cot * carried
    grad_re, grad_im = split(to_spectrum(tables, grad_carried))
    back_spec = join(grad_re * resp_re + grad_im * resp_im, grad_im * resp_re - grad_re * resp_im)
    filt_spec = join(grad_re * prod_re + grad_im * prod_im, grad_im * prod_re - grad_re * prod_im)
    both = to_signal(tables, jnp.concatenate([back_spec, filt_spec], axis=1))
    grad_product = both[:, :narrow] + skip_gain * grad_carried
    grad_mixed = jnp.stack([grad_query, grad_product * value_feat, grad_product * key_feat], axis=1)
    tail = jnp.concatenate([grad_mixed, jnp.zeros((2, 3, narrow), jnp.float32)], axis=0)
    grad_feats = (
        taps[0] * tail[:length] + taps[1] * tail[1 : length + 1] + taps[2] * tail[2:]
    ).astype(jnp.bfloat16)
    grad_taps = jnp.stack(
        [
            jnp.sum(grad_mixed * extended[2 - tap_index : 2 - tap_index + length], axis=0)
            for tap_index in range(3)
        ]
    )
    grad_skip = jnp.sum(grad_carried.astype(jnp.float32) * product.astype(jnp.float32), axis=0)
    return gated, grad_feats, grad_taps, grad_skip, both[:, narrow:]


def blocked_fallback(moved_in, taps, skip_gain, seq_parts, tok_rows, narrow):
    length = seq_parts * tok_rows
    fft_length = 2 * length
    local_feats = moved_in[None, :, :3]
    extended = jnp.concatenate(
        [jnp.zeros((1, 2, 3, narrow), local_feats.dtype), local_feats], axis=1
    )

    def local_spectrum(signal):
        blocks = signal.reshape(signal.shape[0], seq_parts, tok_rows, narrow).astype(jnp.float32)
        part_real, part_imag = across_blocks(
            blocks, jnp.arange(tok_rows, dtype=jnp.int32), seq_parts, fft_length
        )
        return within_blocks(part_real, part_imag)

    def local_signal(spectrum):
        part_real, part_imag = back_within(
            spectrum[0], spectrum[1], jnp.arange(2 * seq_parts, dtype=jnp.int32), fft_length
        )
        values = back_across(part_real, part_imag, seq_parts, fft_length)
        return values.reshape(values.shape[0], length, narrow)

    def no_rows(rows_part):
        return jnp.zeros_like(rows_part)

    return blocked_core(
        extended,
        moved_in[None, :, 3],
        taps,
        skip_gain,
        moved_in[:, 4],
        local_spectrum,
        local_signal,
        no_rows,
    )


def local(features, short_filter, response, skip_gain, cotangent):
    seq_parts = lax.axis_size("seq")
    dp_parts = lax.axis_size("dp")
    seq_index = lax.axis_index("seq")
    tok_rows = features.shape[1]
    chan_width = features.shape[2] // 3
    length = seq_parts * tok_rows
    narrow = chan_width // seq_parts
    offset = seq_index * narrow
    taps = short_filter.reshape(3, 3, chan_width)
    joined_in = jnp.concatenate(
        [
            features.reshape(tok_rows, 3 * chan_width),
            cotangent.reshape(tok_rows, chan_width),
            response,
        ],
        axis=1,
    )
    arranged = joined_in.reshape(tok_rows, 5, seq_parts, narrow).transpose(2, 0, 1, 3)
    moved_in = lax.all_to_all(arranged, "seq", 0, 0, tiled=True).reshape(length, 5, narrow)
    local_taps = lax.dynamic_slice_in_dim(taps, offset, narrow, 2)
    local_skip = lax.dynamic_slice_in_dim(skip_gain, offset, narrow, 0)
    if length <= 2048:
        gated, grad_feats, grad_taps, grad_skip, filter_part = block_core(
            moved_in[:, :3], moved_in[:, 3], moved_in[:, 4], local_taps, local_skip
        )
    else:
        gated, grad_feats, grad_taps, grad_skip, filter_part = blocked_fallback(
            moved_in, local_taps, local_skip, seq_parts, tok_rows, narrow
        )
        gated = gated.reshape(length, narrow)
        grad_feats = grad_feats.reshape(length, 3, narrow)
    joined_out = jnp.concatenate(
        [gated.reshape(seq_parts, tok_rows, 1, narrow), grad_feats.reshape(seq_parts, tok_rows, 3, narrow)],
        axis=2,
    )
    moved_out = lax.all_to_all(joined_out, "seq", 0, 0, tiled=True).transpose(1, 2, 0, 3)
    gated = moved_out[:, 0]
    grad_feats = moved_out[:, 1:]
    extra = 16
    small = jnp.concatenate(
        [grad_taps.reshape(9, narrow), grad_skip[None], jnp.zeros((extra - 10, narrow), jnp.float32)],
        axis=0,
    )
    chunks = jnp.concatenate(
        [
            filter_part.reshape(seq_parts, tok_rows, narrow),
            jnp.broadcast_to(small[None], (seq_parts, extra, narrow)),
        ],
        axis=1,
    )
    moved = (
        lax.all_to_all(chunks, "seq", 0, 0, tiled=True)
        .transpose(1, 0, 2)
        .reshape(tok_rows + extra, chan_width)
    )
    block = chan_width // dp_parts
    small_all = moved[tok_rows : tok_rows + 10]
    small_rows = small_all.reshape(10, dp_parts, block).transpose(1, 0, 2).reshape(dp_parts * 10, block)
    joined = jnp.concatenate([moved[:tok_rows], jnp.tile(small_rows, (1, dp_parts))], axis=0)
    reduced = lax.psum_scatter(joined, "dp", scatter_dimension=1, tiled=True)
    filter_total = reduced[:tok_rows]
    small_total = (
        reduced[tok_rows:].reshape(dp_parts, 10, block).transpose(1, 0, 2).reshape(10, chan_width)
    )
    gated = gated.reshape(1, tok_rows, chan_width)
    grad_feats = grad_feats.reshape(1, tok_rows, 3 * chan_width)
    return (
        gated,
        grad_feats,
        small_total[:9].reshape(3, 3 * chan_width),
        small_total[9],
        filter_total,
    )


def solution(mesh):
    placed = (P("dp", "seq", None), P(), P("seq", None), P(), P("dp", "seq", None))
    return jax.shard_map(
        local,
        mesh=mesh,
        in_specs=placed,
        out_specs=(P("dp", "seq", None), P("dp", "seq", None), P(), P(), P("seq", "dp")),
        check_vma=False,
    )
```

```python
import math

import jax
import jax.numpy as jnp
from jax import lax
from jax.sharding import PartitionSpec as P


precise = lax.Precision.HIGHEST


def dft_table(count):
    series = jnp.arange(count, dtype=jnp.int32)
    angle = (series[:, None] * series[None, :] % count).astype(jnp.float32) * (
        2.0 * math.pi / count
    )
    return (jnp.cos(angle), jnp.sin(angle))


def across_blocks(signal, offsets, blocks, fft_length):
    double = jnp.arange(2 * blocks, dtype=jnp.int32)
    single = jnp.arange(blocks, dtype=jnp.int32)
    angle = (double[:, None] * single[None, :] % (2 * blocks)).astype(jnp.float32) * (
        math.pi / blocks
    )
    table = jnp.stack([jnp.cos(angle), -jnp.sin(angle)])
    first = jnp.einsum("oap,bpjk->obajk", table, signal, precision=precise)
    twist = (double[:, None] * offsets[None, :] % fft_length).astype(jnp.float32) * (
        -2.0 * math.pi / fft_length
    )
    cosine = jnp.cos(twist)[None, :, :, None]
    sine = jnp.sin(twist)[None, :, :, None]
    return (first[0] * cosine - first[1] * sine, first[0] * sine + first[1] * cosine)


def within_blocks(part_real, part_imag):
    table_cos, table_sin = dft_table(part_real.shape[2])
    table = jnp.stack([jnp.stack([table_cos, table_sin]), jnp.stack([-table_sin, table_cos])])
    spectra = jnp.einsum(
        "oibj,ixajk->oxabk", table, jnp.stack([part_real, part_imag]), precision=precise
    )
    return (spectra[0], spectra[1])


def back_within(spec_real, spec_imag, firsts, fft_length):
    count = spec_real.shape[2]
    table_cos, table_sin = dft_table(count)
    table = jnp.stack([jnp.stack([table_cos, -table_sin]), jnp.stack([table_sin, table_cos])])
    backs = jnp.einsum(
        "oibj,ixabk->oxajk", table, jnp.stack([spec_real, spec_imag]), precision=precise
    )
    series = jnp.arange(count, dtype=jnp.int32)
    twist = (firsts[:, None] * series[None, :] % fft_length).astype(jnp.float32) * (
        2.0 * math.pi / fft_length
    )
    cosine = jnp.cos(twist)[None, :, :, None]
    sine = jnp.sin(twist)[None, :, :, None]
    return (backs[0] * cosine - backs[1] * sine, backs[0] * sine + backs[1] * cosine)


def back_across(part_real, part_imag, blocks, fft_length):
    double = jnp.arange(2 * blocks, dtype=jnp.int32)
    single = jnp.arange(blocks, dtype=jnp.int32)
    angle = (single[:, None] * double[None, :] % (2 * blocks)).astype(jnp.float32) * (
        math.pi / blocks
    )
    table = jnp.stack([jnp.cos(angle), -jnp.sin(angle)])
    result = jnp.einsum(
        "ipa,ibajk->bpjk", table, jnp.stack([part_real, part_imag]), precision=precise
    )
    return result * (1.0 / fft_length)


def times_spectrum(left, right):
    return (left[0] * right[0] - left[1] * right[1], left[0] * right[1] + left[1] * right[0])


def times_conjugate(left, right):
    return (left[0] * right[0] + left[1] * right[1], left[1] * right[0] - left[0] * right[1])


def blocked_core(extended, cotangent, taps, skip_gain, response, to_spectrum, to_signal, after_rows):
    count = cotangent.shape[1]
    batch = cotangent.shape[0]
    mixed = taps[0] * extended[:, 2:] + taps[1] * extended[:, 1:-1] + taps[2] * extended[:, :-2]
    query_feat = mixed[:, :, 0]
    key_feat = mixed[:, :, 1]
    value_feat = mixed[:, :, 2]
    product = (key_feat * value_feat).astype(jnp.bfloat16)
    stacked = to_spectrum(jnp.concatenate([product, response[None]], axis=0))
    prod_spec = (stacked[0][:batch], stacked[1][:batch])
    resp_spec = (stacked[0][batch:], stacked[1][batch:])
    conv_out = to_signal(times_spectrum(prod_spec, resp_spec))
    carried = conv_out + skip_gain * product
    gated = (query_feat * carried).astype(jnp.bfloat16)
    grad_carried = (cotangent * query_feat).astype(jnp.bfloat16)
    grad_query = cotangent * carried
    grad_spec = to_spectrum(grad_carried)
    back_conv = times_conjugate(grad_spec, resp_spec)
    resp_grad = times_conjugate(grad_spec, prod_spec)
    joined_real = jnp.concatenate(
        [back_conv[0], jnp.sum(resp_grad[0], axis=0, keepdims=True)], axis=0
    )
    joined_imag = jnp.concatenate(
        [back_conv[1], jnp.sum(resp_grad[1], axis=0, keepdims=True)], axis=0
    )
    both = to_signal((joined_real, joined_imag))
    grad_product = both[:batch] + skip_gain * grad_carried
    grad_mixed = jnp.stack([grad_query, grad_product * value_feat, grad_product * key_feat], axis=2)
    tail = jnp.concatenate([grad_mixed, after_rows(grad_mixed[:, :2])], axis=1)
    grad_feats = (
        taps[0] * tail[:, :count] + taps[1] * tail[:, 1 : count + 1] + taps[2] * tail[:, 2:]
    ).astype(jnp.bfloat16)
    grad_taps = jnp.stack(
        [
            jnp.sum(grad_mixed * extended[:, 2 - tap_index : 2 - tap_index + count], axis=(0, 1))
            for tap_index in range(3)
        ]
    )
    grad_skip = jnp.sum(grad_carried.astype(jnp.float32) * product.astype(jnp.float32), axis=(0, 1))
    return (gated, grad_feats, grad_taps, grad_skip, both[batch])


def dft_tables(length):
    fft_length = 2 * length
    bins = length + 1
    freq = lax.broadcasted_iota(jnp.int32, (bins, length), 0)
    time = lax.broadcasted_iota(jnp.int32, (bins, length), 1)
    angle = lax.optimization_barrier((freq * time) % fft_length).astype(jnp.float32) * (
        2.0 * math.pi / fft_length
    )
    table = jnp.concatenate([jnp.cos(angle), -jnp.sin(angle)], axis=0)
    high = table.astype(jnp.bfloat16)
    low = (table - high.astype(jnp.float32)).astype(jnp.bfloat16)
    return high, low


def bf16_dot(left, right, dims):
    return lax.dot_general(left, right, (dims, ((), ())), preferred_element_type=jnp.float32)


def to_spectrum(tables, signal):
    high, low = tables
    forward = ((1,), (0,))
    return bf16_dot(high, signal, forward) + bf16_dot(low, signal, forward)


def to_signal(tables, spectrum):
    high, low = tables
    bins = high.shape[0] // 2
    fft_length = 2 * (bins - 1)
    row = lax.broadcasted_iota(jnp.int32, (2 * bins, 1), 0)
    edge = (row == 0) | (row == bins - 1) | (row == bins) | (row == 2 * bins - 1)
    weight = jnp.where(edge, 1.0 / fft_length, 2.0 / fft_length)
    scaled = spectrum * weight
    spec_high = scaled.astype(jnp.bfloat16)
    spec_low = (scaled - spec_high.astype(jnp.float32)).astype(jnp.bfloat16)
    backward = ((0,), (0,))
    return (
        bf16_dot(high, spec_high, backward)
        + bf16_dot(high, spec_low, backward)
        + bf16_dot(low, spec_high, backward)
    )


def split(spectrum):
    bins = spectrum.shape[0] // 2
    return spectrum[:bins], spectrum[bins:]


def join(real, imag):
    return jnp.concatenate([real, imag], axis=0)


def block_core(feats, cot, resp, taps, skip_gain):
    length = feats.shape[0]
    narrow = feats.shape[2]
    tables = dft_tables(length)
    extended = jnp.concatenate([jnp.zeros((2, 3, narrow), feats.dtype), feats], axis=0)
    mixed = taps[0] * extended[2:] + taps[1] * extended[1:-1] + taps[2] * extended[:-2]
    query_feat = mixed[:, 0]
    key_feat = mixed[:, 1]
    value_feat = mixed[:, 2]
    product = (key_feat * value_feat).astype(jnp.bfloat16)
    first = to_spectrum(tables, jnp.concatenate([product, resp], axis=1))
    prod_re, prod_im = split(first[:, :narrow])
    resp_re, resp_im = split(first[:, narrow:])
    conv_out = to_signal(
        tables, join(prod_re * resp_re - prod_im * resp_im, prod_re * resp_im + prod_im * resp_re)
    )
    carried = conv_out + skip_gain * product
    gated = (query_feat * carried).astype(jnp.bfloat16)
    grad_carried = (cot * query_feat).astype(jnp.bfloat16)
    grad_query = cot * carried
    grad_re, grad_im = split(to_spectrum(tables, grad_carried))
    back_spec = join(grad_re * resp_re + grad_im * resp_im, grad_im * resp_re - grad_re * resp_im)
    filt_spec = join(grad_re * prod_re + grad_im * prod_im, grad_im * prod_re - grad_re * prod_im)
    both = to_signal(tables, jnp.concatenate([back_spec, filt_spec], axis=1))
    grad_product = both[:, :narrow] + skip_gain * grad_carried
    grad_mixed = jnp.stack([grad_query, grad_product * value_feat, grad_product * key_feat], axis=1)
    tail = jnp.concatenate([grad_mixed, jnp.zeros((2, 3, narrow), jnp.float32)], axis=0)
    grad_feats = (
        taps[0] * tail[:length] + taps[1] * tail[1 : length + 1] + taps[2] * tail[2:]
    ).astype(jnp.bfloat16)
    grad_taps = jnp.stack(
        [
            jnp.sum(grad_mixed * extended[2 - tap_index : 2 - tap_index + length], axis=0)
            for tap_index in range(3)
        ]
    )
    grad_skip = jnp.sum(grad_carried.astype(jnp.float32) * product.astype(jnp.float32), axis=0)
    return gated, grad_feats, grad_taps, grad_skip, both[:, narrow:]


def blocked_fallback(moved_in, taps, skip_gain, seq_parts, tok_rows, narrow):
    length = seq_parts * tok_rows
    fft_length = 2 * length
    local_feats = moved_in[None, :, :3]
    extended = jnp.concatenate(
        [jnp.zeros((1, 2, 3, narrow), local_feats.dtype), local_feats], axis=1
    )

    def local_spectrum(signal):
        blocks = signal.reshape(signal.shape[0], seq_parts, tok_rows, narrow).astype(jnp.float32)
        part_real, part_imag = across_blocks(
            blocks, jnp.arange(tok_rows, dtype=jnp.int32), seq_parts, fft_length
        )
        return within_blocks(part_real, part_imag)

    def local_signal(spectrum):
        part_real, part_imag = back_within(
            spectrum[0], spectrum[1], jnp.arange(2 * seq_parts, dtype=jnp.int32), fft_length
        )
        values = back_across(part_real, part_imag, seq_parts, fft_length)
        return values.reshape(values.shape[0], length, narrow)

    def no_rows(rows_part):
        return jnp.zeros_like(rows_part)

    return blocked_core(
        extended,
        moved_in[None, :, 3],
        taps,
        skip_gain,
        moved_in[:, 4],
        local_spectrum,
        local_signal,
        no_rows,
    )


def local(features, short_filter, response, skip_gain, cotangent):
    seq_parts = lax.axis_size("seq")
    dp_parts = lax.axis_size("dp")
    seq_index = lax.axis_index("seq")
    tok_rows = features.shape[1]
    chan_width = features.shape[2] // 3
    length = seq_parts * tok_rows
    narrow = chan_width // seq_parts
    offset = seq_index * narrow
    taps = short_filter.reshape(3, 3, chan_width)
    joined_in = jnp.concatenate(
        [
            features.reshape(tok_rows, 3 * chan_width),
            cotangent.reshape(tok_rows, chan_width),
            response,
        ],
        axis=1,
    )
    arranged = joined_in.reshape(tok_rows, 5, seq_parts, narrow).transpose(2, 0, 1, 3)
    moved_in = lax.all_to_all(arranged, "seq", 0, 0, tiled=True).reshape(length, 5, narrow)
    local_taps = lax.dynamic_slice_in_dim(taps, offset, narrow, 2)
    local_skip = lax.dynamic_slice_in_dim(skip_gain, offset, narrow, 0)
    if length <= 2048:
        gated, grad_feats, grad_taps, grad_skip, filter_part = block_core(
            moved_in[:, :3], moved_in[:, 3], moved_in[:, 4], local_taps, local_skip
        )
    else:
        gated, grad_feats, grad_taps, grad_skip, filter_part = blocked_fallback(
            moved_in, local_taps, local_skip, seq_parts, tok_rows, narrow
        )
        gated = gated.reshape(length, narrow)
        grad_feats = grad_feats.reshape(length, 3, narrow)
    joined_out = jnp.concatenate(
        [gated.reshape(seq_parts, tok_rows, 1, narrow), grad_feats.reshape(seq_parts, tok_rows, 3, narrow)],
        axis=2,
    )
    moved_out = lax.all_to_all(joined_out, "seq", 0, 0, tiled=True).transpose(1, 2, 0, 3)
    gated = moved_out[:, 0]
    grad_feats = moved_out[:, 1:]
    extra = 16
    small = jnp.concatenate(
        [grad_taps.reshape(9, narrow), grad_skip[None], jnp.zeros((extra - 10, narrow), jnp.float32)],
        axis=0,
    )
    chunks = jnp.concatenate(
        [
            filter_part.reshape(seq_parts, tok_rows, narrow),
            jnp.broadcast_to(small[None], (seq_parts, extra, narrow)),
        ],
        axis=1,
    )
    moved = lax.all_to_all(chunks, "seq", 0, 0, tiled=True)
    pair = seq_parts // dp_parts
    small_all = moved[:, tok_rows : tok_rows + 10]
    small_rows = (
        small_all.reshape(dp_parts, pair, 10, narrow)
        .transpose(1, 0, 2, 3)
        .reshape(pair, dp_parts * 10, narrow)
    )
    joined = jnp.concatenate(
        [moved[:, :tok_rows], jnp.tile(small_rows, (dp_parts, 1, 1))], axis=1
    )
    reduced = lax.psum_scatter(joined, "dp", scatter_dimension=0, tiled=True)
    filter_total = reduced[:, :tok_rows].transpose(1, 0, 2).reshape(tok_rows, pair * narrow)
    small_total = (
        reduced[:, tok_rows:]
        .reshape(pair, dp_parts, 10, narrow)
        .transpose(2, 1, 0, 3)
        .reshape(10, chan_width)
    )
    gated = gated.reshape(1, tok_rows, chan_width)
    grad_feats = grad_feats.reshape(1, tok_rows, 3 * chan_width)
    return (
        gated,
        grad_feats,
        small_total[:9].reshape(3, 3 * chan_width),
        small_total[9],
        filter_total,
    )


def solution(mesh):
    placed = (P("dp", "seq", None), P(), P("seq", None), P(), P("dp", "seq", None))
    return jax.shard_map(
        local,
        mesh=mesh,
        in_specs=placed,
        out_specs=(P("dp", "seq", None), P("dp", "seq", None), P(), P(), P("seq", "dp")),
        check_vma=False,
    )
```

```python
import math

import jax
import jax.numpy as jnp
from jax import lax
from jax.sharding import PartitionSpec as P


precise = lax.Precision.HIGHEST


def dft_table(count):
    series = jnp.arange(count, dtype=jnp.int32)
    angle = (series[:, None] * series[None, :] % count).astype(jnp.float32) * (
        2.0 * math.pi / count
    )
    return (jnp.cos(angle), jnp.sin(angle))


def across_blocks(signal, offsets, blocks, fft_length):
    double = jnp.arange(2 * blocks, dtype=jnp.int32)
    single = jnp.arange(blocks, dtype=jnp.int32)
    angle = (double[:, None] * single[None, :] % (2 * blocks)).astype(jnp.float32) * (
        math.pi / blocks
    )
    table = jnp.stack([jnp.cos(angle), -jnp.sin(angle)])
    first = jnp.einsum("oap,bpjk->obajk", table, signal, precision=precise)
    twist = (double[:, None] * offsets[None, :] % fft_length).astype(jnp.float32) * (
        -2.0 * math.pi / fft_length
    )
    cosine = jnp.cos(twist)[None, :, :, None]
    sine = jnp.sin(twist)[None, :, :, None]
    return (first[0] * cosine - first[1] * sine, first[0] * sine + first[1] * cosine)


def within_blocks(part_real, part_imag):
    table_cos, table_sin = dft_table(part_real.shape[2])
    table = jnp.stack([jnp.stack([table_cos, table_sin]), jnp.stack([-table_sin, table_cos])])
    spectra = jnp.einsum(
        "oibj,ixajk->oxabk", table, jnp.stack([part_real, part_imag]), precision=precise
    )
    return (spectra[0], spectra[1])


def back_within(spec_real, spec_imag, firsts, fft_length):
    count = spec_real.shape[2]
    table_cos, table_sin = dft_table(count)
    table = jnp.stack([jnp.stack([table_cos, -table_sin]), jnp.stack([table_sin, table_cos])])
    backs = jnp.einsum(
        "oibj,ixabk->oxajk", table, jnp.stack([spec_real, spec_imag]), precision=precise
    )
    series = jnp.arange(count, dtype=jnp.int32)
    twist = (firsts[:, None] * series[None, :] % fft_length).astype(jnp.float32) * (
        2.0 * math.pi / fft_length
    )
    cosine = jnp.cos(twist)[None, :, :, None]
    sine = jnp.sin(twist)[None, :, :, None]
    return (backs[0] * cosine - backs[1] * sine, backs[0] * sine + backs[1] * cosine)


def back_across(part_real, part_imag, blocks, fft_length):
    double = jnp.arange(2 * blocks, dtype=jnp.int32)
    single = jnp.arange(blocks, dtype=jnp.int32)
    angle = (single[:, None] * double[None, :] % (2 * blocks)).astype(jnp.float32) * (
        math.pi / blocks
    )
    table = jnp.stack([jnp.cos(angle), -jnp.sin(angle)])
    result = jnp.einsum(
        "ipa,ibajk->bpjk", table, jnp.stack([part_real, part_imag]), precision=precise
    )
    return result * (1.0 / fft_length)


def times_spectrum(left, right):
    return (left[0] * right[0] - left[1] * right[1], left[0] * right[1] + left[1] * right[0])


def times_conjugate(left, right):
    return (left[0] * right[0] + left[1] * right[1], left[1] * right[0] - left[0] * right[1])


def blocked_core(extended, cotangent, taps, skip_gain, response, to_spectrum, to_signal, after_rows):
    count = cotangent.shape[1]
    batch = cotangent.shape[0]
    mixed = taps[0] * extended[:, 2:] + taps[1] * extended[:, 1:-1] + taps[2] * extended[:, :-2]
    query_feat = mixed[:, :, 0]
    key_feat = mixed[:, :, 1]
    value_feat = mixed[:, :, 2]
    product = (key_feat * value_feat).astype(jnp.bfloat16)
    stacked = to_spectrum(jnp.concatenate([product, response[None]], axis=0))
    prod_spec = (stacked[0][:batch], stacked[1][:batch])
    resp_spec = (stacked[0][batch:], stacked[1][batch:])
    conv_out = to_signal(times_spectrum(prod_spec, resp_spec))
    carried = conv_out + skip_gain * product
    gated = (query_feat * carried).astype(jnp.bfloat16)
    grad_carried = (cotangent * query_feat).astype(jnp.bfloat16)
    grad_query = cotangent * carried
    grad_spec = to_spectrum(grad_carried)
    back_conv = times_conjugate(grad_spec, resp_spec)
    resp_grad = times_conjugate(grad_spec, prod_spec)
    joined_real = jnp.concatenate(
        [back_conv[0], jnp.sum(resp_grad[0], axis=0, keepdims=True)], axis=0
    )
    joined_imag = jnp.concatenate(
        [back_conv[1], jnp.sum(resp_grad[1], axis=0, keepdims=True)], axis=0
    )
    both = to_signal((joined_real, joined_imag))
    grad_product = both[:batch] + skip_gain * grad_carried
    grad_mixed = jnp.stack([grad_query, grad_product * value_feat, grad_product * key_feat], axis=2)
    tail = jnp.concatenate([grad_mixed, after_rows(grad_mixed[:, :2])], axis=1)
    grad_feats = (
        taps[0] * tail[:, :count] + taps[1] * tail[:, 1 : count + 1] + taps[2] * tail[:, 2:]
    ).astype(jnp.bfloat16)
    grad_taps = jnp.stack(
        [
            jnp.sum(grad_mixed * extended[:, 2 - tap_index : 2 - tap_index + count], axis=(0, 1))
            for tap_index in range(3)
        ]
    )
    grad_skip = jnp.sum(grad_carried.astype(jnp.float32) * product.astype(jnp.float32), axis=(0, 1))
    return (gated, grad_feats, grad_taps, grad_skip, both[batch])


def dft_tables(length):
    fft_length = 2 * length
    bins = length + 1
    freq = lax.broadcasted_iota(jnp.int32, (bins, length), 0)
    time = lax.broadcasted_iota(jnp.int32, (bins, length), 1)
    angle = lax.optimization_barrier((freq * time) % fft_length).astype(jnp.float32) * (
        2.0 * math.pi / fft_length
    )
    table = jnp.concatenate([jnp.cos(angle), -jnp.sin(angle)], axis=0)
    high = table.astype(jnp.bfloat16)
    low = (table - high.astype(jnp.float32)).astype(jnp.bfloat16)
    return high, low


def bf16_dot(left, right, dims):
    return lax.dot_general(left, right, (dims, ((), ())), preferred_element_type=jnp.float32)


def to_spectrum(tables, signal):
    high, low = tables
    forward = ((1,), (0,))
    return bf16_dot(high, signal, forward) + bf16_dot(low, signal, forward)


def to_signal(tables, spectrum):
    high, low = tables
    bins = high.shape[0] // 2
    fft_length = 2 * (bins - 1)
    row = lax.broadcasted_iota(jnp.int32, (2 * bins, 1), 0)
    edge = (row == 0) | (row == bins - 1) | (row == bins) | (row == 2 * bins - 1)
    weight = jnp.where(edge, 1.0 / fft_length, 2.0 / fft_length)
    scaled = spectrum * weight
    spec_high = scaled.astype(jnp.bfloat16)
    spec_low = (scaled - spec_high.astype(jnp.float32)).astype(jnp.bfloat16)
    backward = ((0,), (0,))
    return (
        bf16_dot(high, spec_high, backward)
        + bf16_dot(high, spec_low, backward)
        + bf16_dot(low, spec_high, backward)
    )


def split(spectrum):
    bins = spectrum.shape[0] // 2
    return spectrum[:bins], spectrum[bins:]


def join(real, imag):
    return jnp.concatenate([real, imag], axis=0)


def block_core(feats, cot, resp, taps, skip_gain):
    length = feats.shape[0]
    narrow = feats.shape[2]
    tables = dft_tables(length)
    extended = jnp.concatenate([jnp.zeros((2, 3, narrow), feats.dtype), feats], axis=0)
    mixed = taps[0] * extended[2:] + taps[1] * extended[1:-1] + taps[2] * extended[:-2]
    query_feat = mixed[:, 0]
    key_feat = mixed[:, 1]
    value_feat = mixed[:, 2]
    product = (key_feat * value_feat).astype(jnp.bfloat16)
    first = to_spectrum(tables, jnp.concatenate([product, resp], axis=1))
    prod_re, prod_im = split(first[:, :narrow])
    resp_re, resp_im = split(first[:, narrow:])
    conv_out = to_signal(
        tables, join(prod_re * resp_re - prod_im * resp_im, prod_re * resp_im + prod_im * resp_re)
    )
    carried = conv_out + skip_gain * product
    gated = (query_feat * carried).astype(jnp.bfloat16)
    grad_carried = (cot * query_feat).astype(jnp.bfloat16)
    grad_query = cot * carried
    grad_re, grad_im = split(to_spectrum(tables, grad_carried))
    back_spec = join(grad_re * resp_re + grad_im * resp_im, grad_im * resp_re - grad_re * resp_im)
    filt_spec = join(grad_re * prod_re + grad_im * prod_im, grad_im * prod_re - grad_re * prod_im)
    both = to_signal(tables, jnp.concatenate([back_spec, filt_spec], axis=1))
    grad_product = both[:, :narrow] + skip_gain * grad_carried
    grad_mixed = jnp.stack([grad_query, grad_product * value_feat, grad_product * key_feat], axis=1)
    tail = jnp.concatenate([grad_mixed, jnp.zeros((2, 3, narrow), jnp.float32)], axis=0)
    grad_feats = (
        taps[0] * tail[:length] + taps[1] * tail[1 : length + 1] + taps[2] * tail[2:]
    ).astype(jnp.bfloat16)
    grad_taps = jnp.stack(
        [
            jnp.sum(grad_mixed * extended[2 - tap_index : 2 - tap_index + length], axis=0)
            for tap_index in range(3)
        ]
    )
    grad_skip = jnp.sum(grad_carried.astype(jnp.float32) * product.astype(jnp.float32), axis=0)
    return gated, grad_feats, grad_taps, grad_skip, both[:, narrow:]


def blocked_fallback(moved_in, taps, skip_gain, seq_parts, tok_rows, narrow):
    length = seq_parts * tok_rows
    fft_length = 2 * length
    local_feats = moved_in[None, :, :3]
    extended = jnp.concatenate(
        [jnp.zeros((1, 2, 3, narrow), local_feats.dtype), local_feats], axis=1
    )

    def local_spectrum(signal):
        blocks = signal.reshape(signal.shape[0], seq_parts, tok_rows, narrow).astype(jnp.float32)
        part_real, part_imag = across_blocks(
            blocks, jnp.arange(tok_rows, dtype=jnp.int32), seq_parts, fft_length
        )
        return within_blocks(part_real, part_imag)

    def local_signal(spectrum):
        part_real, part_imag = back_within(
            spectrum[0], spectrum[1], jnp.arange(2 * seq_parts, dtype=jnp.int32), fft_length
        )
        values = back_across(part_real, part_imag, seq_parts, fft_length)
        return values.reshape(values.shape[0], length, narrow)

    def no_rows(rows_part):
        return jnp.zeros_like(rows_part)

    return blocked_core(
        extended,
        moved_in[None, :, 3],
        taps,
        skip_gain,
        moved_in[:, 4],
        local_spectrum,
        local_signal,
        no_rows,
    )


def local(features, short_filter, response, skip_gain, cotangent):
    seq_parts = lax.axis_size("seq")
    dp_parts = lax.axis_size("dp")
    seq_index = lax.axis_index("seq")
    tok_rows = features.shape[1]
    chan_width = features.shape[2] // 3
    length = seq_parts * tok_rows
    narrow = chan_width // seq_parts
    piece = narrow // dp_parts
    taps = short_filter.reshape(3, 3, dp_parts, seq_parts, piece)
    joined_in = jnp.concatenate(
        [
            features.reshape(tok_rows, 3 * chan_width),
            cotangent.reshape(tok_rows, chan_width),
            response,
        ],
        axis=1,
    )
    arranged = joined_in.reshape(tok_rows, 5, dp_parts, seq_parts, piece).transpose(3, 0, 1, 2, 4)
    moved_in = lax.all_to_all(arranged, "seq", 0, 0, tiled=True).reshape(length, 5, narrow)
    local_taps = lax.dynamic_index_in_dim(taps, seq_index, 3, keepdims=False).reshape(3, 3, narrow)
    local_skip = lax.dynamic_index_in_dim(
        skip_gain.reshape(dp_parts, seq_parts, piece), seq_index, 1, keepdims=False
    ).reshape(narrow)
    if length <= 2048:
        gated, grad_feats, grad_taps, grad_skip, filter_part = block_core(
            moved_in[:, :3], moved_in[:, 3], moved_in[:, 4], local_taps, local_skip
        )
    else:
        gated, grad_feats, grad_taps, grad_skip, filter_part = blocked_fallback(
            moved_in, local_taps, local_skip, seq_parts, tok_rows, narrow
        )
        gated = gated.reshape(length, narrow)
        grad_feats = grad_feats.reshape(length, 3, narrow)
    joined_out = jnp.concatenate(
        [gated.reshape(seq_parts, tok_rows, 1, narrow), grad_feats.reshape(seq_parts, tok_rows, 3, narrow)],
        axis=2,
    )
    moved_out = (
        lax.all_to_all(joined_out, "seq", 0, 0, tiled=True)
        .reshape(seq_parts, tok_rows, 4, dp_parts, piece)
        .transpose(1, 2, 3, 0, 4)
        .reshape(tok_rows, 4, chan_width)
    )
    gated = moved_out[:, 0]
    grad_feats = moved_out[:, 1:]
    small = jnp.concatenate([grad_taps.reshape(9, narrow), grad_skip[None]], axis=0)
    small_rows = small.reshape(10, dp_parts, piece).transpose(1, 0, 2).reshape(dp_parts * 10, piece)
    dp_in = jnp.concatenate(
        [
            filter_part.reshape(length, dp_parts, piece).transpose(1, 0, 2),
            jnp.broadcast_to(small_rows[None], (dp_parts, dp_parts * 10, piece)),
        ],
        axis=1,
    )
    dp_sum = lax.psum_scatter(dp_in, "dp", scatter_dimension=0, tiled=True)[0]
    seq_in = jnp.concatenate(
        [
            dp_sum[:length].reshape(seq_parts, tok_rows, piece),
            jnp.broadcast_to(dp_sum[length:][None], (seq_parts, dp_parts * 10, piece)),
        ],
        axis=1,
    )
    seq_out = lax.all_to_all(seq_in, "seq", 0, 0, tiled=True)
    filter_total = seq_out[:, :tok_rows].transpose(1, 0, 2).reshape(tok_rows, seq_parts * piece)
    small_total = (
        seq_out[:, tok_rows:]
        .reshape(seq_parts, dp_parts, 10, piece)
        .transpose(2, 1, 0, 3)
        .reshape(10, chan_width)
    )
    gated = gated.reshape(1, tok_rows, chan_width)
    grad_feats = grad_feats.reshape(1, tok_rows, 3 * chan_width)
    return (
        gated,
        grad_feats,
        small_total[:9].reshape(3, 3 * chan_width),
        small_total[9],
        filter_total,
    )


def solution(mesh):
    placed = (P("dp", "seq", None), P(), P("seq", None), P(), P("dp", "seq", None))
    return jax.shard_map(
        local,
        mesh=mesh,
        in_specs=placed,
        out_specs=(P("dp", "seq", None), P("dp", "seq", None), P(), P(), P("seq", "dp")),
        check_vma=False,
    )
```

```python
import math

import jax
import jax.numpy as jnp
from jax import lax
from jax.sharding import PartitionSpec as P


precise = lax.Precision.HIGHEST


def dft_table(count):
    series = jnp.arange(count, dtype=jnp.int32)
    angle = (series[:, None] * series[None, :] % count).astype(jnp.float32) * (
        2.0 * math.pi / count
    )
    return (jnp.cos(angle), jnp.sin(angle))


def across_blocks(signal, offsets, blocks, fft_length):
    double = jnp.arange(2 * blocks, dtype=jnp.int32)
    single = jnp.arange(blocks, dtype=jnp.int32)
    angle = (double[:, None] * single[None, :] % (2 * blocks)).astype(jnp.float32) * (
        math.pi / blocks
    )
    table = jnp.stack([jnp.cos(angle), -jnp.sin(angle)])
    first = jnp.einsum("oap,bpjk->obajk", table, signal, precision=precise)
    twist = (double[:, None] * offsets[None, :] % fft_length).astype(jnp.float32) * (
        -2.0 * math.pi / fft_length
    )
    cosine = jnp.cos(twist)[None, :, :, None]
    sine = jnp.sin(twist)[None, :, :, None]
    return (first[0] * cosine - first[1] * sine, first[0] * sine + first[1] * cosine)


def within_blocks(part_real, part_imag):
    table_cos, table_sin = dft_table(part_real.shape[2])
    table = jnp.stack([jnp.stack([table_cos, table_sin]), jnp.stack([-table_sin, table_cos])])
    spectra = jnp.einsum(
        "oibj,ixajk->oxabk", table, jnp.stack([part_real, part_imag]), precision=precise
    )
    return (spectra[0], spectra[1])


def back_within(spec_real, spec_imag, firsts, fft_length):
    count = spec_real.shape[2]
    table_cos, table_sin = dft_table(count)
    table = jnp.stack([jnp.stack([table_cos, -table_sin]), jnp.stack([table_sin, table_cos])])
    backs = jnp.einsum(
        "oibj,ixabk->oxajk", table, jnp.stack([spec_real, spec_imag]), precision=precise
    )
    series = jnp.arange(count, dtype=jnp.int32)
    twist = (firsts[:, None] * series[None, :] % fft_length).astype(jnp.float32) * (
        2.0 * math.pi / fft_length
    )
    cosine = jnp.cos(twist)[None, :, :, None]
    sine = jnp.sin(twist)[None, :, :, None]
    return (backs[0] * cosine - backs[1] * sine, backs[0] * sine + backs[1] * cosine)


def back_across(part_real, part_imag, blocks, fft_length):
    double = jnp.arange(2 * blocks, dtype=jnp.int32)
    single = jnp.arange(blocks, dtype=jnp.int32)
    angle = (single[:, None] * double[None, :] % (2 * blocks)).astype(jnp.float32) * (
        math.pi / blocks
    )
    table = jnp.stack([jnp.cos(angle), -jnp.sin(angle)])
    result = jnp.einsum(
        "ipa,ibajk->bpjk", table, jnp.stack([part_real, part_imag]), precision=precise
    )
    return result * (1.0 / fft_length)


def times_spectrum(left, right):
    return (left[0] * right[0] - left[1] * right[1], left[0] * right[1] + left[1] * right[0])


def times_conjugate(left, right):
    return (left[0] * right[0] + left[1] * right[1], left[1] * right[0] - left[0] * right[1])


def blocked_core(extended, cotangent, taps, skip_gain, response, to_spectrum, to_signal, after_rows):
    count = cotangent.shape[1]
    batch = cotangent.shape[0]
    mixed = taps[0] * extended[:, 2:] + taps[1] * extended[:, 1:-1] + taps[2] * extended[:, :-2]
    query_feat = mixed[:, :, 0]
    key_feat = mixed[:, :, 1]
    value_feat = mixed[:, :, 2]
    product = (key_feat * value_feat).astype(jnp.bfloat16)
    stacked = to_spectrum(jnp.concatenate([product, response[None]], axis=0))
    prod_spec = (stacked[0][:batch], stacked[1][:batch])
    resp_spec = (stacked[0][batch:], stacked[1][batch:])
    conv_out = to_signal(times_spectrum(prod_spec, resp_spec))
    carried = conv_out + skip_gain * product
    gated = (query_feat * carried).astype(jnp.bfloat16)
    grad_carried = (cotangent * query_feat).astype(jnp.bfloat16)
    grad_query = cotangent * carried
    grad_spec = to_spectrum(grad_carried)
    back_conv = times_conjugate(grad_spec, resp_spec)
    resp_grad = times_conjugate(grad_spec, prod_spec)
    joined_real = jnp.concatenate(
        [back_conv[0], jnp.sum(resp_grad[0], axis=0, keepdims=True)], axis=0
    )
    joined_imag = jnp.concatenate(
        [back_conv[1], jnp.sum(resp_grad[1], axis=0, keepdims=True)], axis=0
    )
    both = to_signal((joined_real, joined_imag))
    grad_product = both[:batch] + skip_gain * grad_carried
    grad_mixed = jnp.stack([grad_query, grad_product * value_feat, grad_product * key_feat], axis=2)
    tail = jnp.concatenate([grad_mixed, after_rows(grad_mixed[:, :2])], axis=1)
    grad_feats = (
        taps[0] * tail[:, :count] + taps[1] * tail[:, 1 : count + 1] + taps[2] * tail[:, 2:]
    ).astype(jnp.bfloat16)
    grad_taps = jnp.stack(
        [
            jnp.sum(grad_mixed * extended[:, 2 - tap_index : 2 - tap_index + count], axis=(0, 1))
            for tap_index in range(3)
        ]
    )
    grad_skip = jnp.sum(grad_carried.astype(jnp.float32) * product.astype(jnp.float32), axis=(0, 1))
    return (gated, grad_feats, grad_taps, grad_skip, both[batch])


def dft_tables(length):
    fft_length = 2 * length
    bins = length + 1
    freq = lax.broadcasted_iota(jnp.int32, (bins, length), 0)
    time = lax.broadcasted_iota(jnp.int32, (bins, length), 1)
    angle = lax.optimization_barrier((freq * time) % fft_length).astype(jnp.float32) * (
        2.0 * math.pi / fft_length
    )
    table = jnp.concatenate([jnp.cos(angle), -jnp.sin(angle)], axis=0)
    return table.astype(jnp.bfloat16)


def bf16_dot(left, right, dims):
    return lax.dot_general(left, right, (dims, ((), ())), preferred_element_type=jnp.float32)


def to_spectrum(table, signal):
    return bf16_dot(table, signal, ((1,), (0,)))


def to_signal(table, spectrum):
    bins = table.shape[0] // 2
    fft_length = 2 * (bins - 1)
    row = lax.broadcasted_iota(jnp.int32, (2 * bins, 1), 0)
    edge = (row == 0) | (row == bins - 1) | (row == bins) | (row == 2 * bins - 1)
    weight = jnp.where(edge, 1.0 / fft_length, 2.0 / fft_length)
    scaled = spectrum * weight
    spec_high = scaled.astype(jnp.bfloat16)
    spec_low = (scaled - spec_high.astype(jnp.float32)).astype(jnp.bfloat16)
    backward = ((0,), (0,))
    return bf16_dot(table, spec_high, backward) + bf16_dot(table, spec_low, backward)


def split(spectrum):
    bins = spectrum.shape[0] // 2
    return spectrum[:bins], spectrum[bins:]


def join(real, imag):
    return jnp.concatenate([real, imag], axis=0)


def block_core(feats, cot, resp, taps, skip_gain):
    length = feats.shape[0]
    narrow = feats.shape[2]
    tables = dft_tables(length)
    extended = jnp.concatenate([jnp.zeros((2, 3, narrow), feats.dtype), feats], axis=0)
    mixed = taps[0] * extended[2:] + taps[1] * extended[1:-1] + taps[2] * extended[:-2]
    query_feat = mixed[:, 0]
    key_feat = mixed[:, 1]
    value_feat = mixed[:, 2]
    product = (key_feat * value_feat).astype(jnp.bfloat16)
    first = to_spectrum(tables, jnp.concatenate([product, resp], axis=1))
    prod_re, prod_im = split(first[:, :narrow])
    resp_re, resp_im = split(first[:, narrow:])
    conv_out = to_signal(
        tables, join(prod_re * resp_re - prod_im * resp_im, prod_re * resp_im + prod_im * resp_re)
    )
    carried = conv_out + skip_gain * product
    gated = (query_feat * carried).astype(jnp.bfloat16)
    grad_carried = (cot * query_feat).astype(jnp.bfloat16)
    grad_query = cot * carried
    grad_re, grad_im = split(to_spectrum(tables, grad_carried))
    back_spec = join(grad_re * resp_re + grad_im * resp_im, grad_im * resp_re - grad_re * resp_im)
    filt_spec = join(grad_re * prod_re + grad_im * prod_im, grad_im * prod_re - grad_re * prod_im)
    both = to_signal(tables, jnp.concatenate([back_spec, filt_spec], axis=1))
    grad_product = both[:, :narrow] + skip_gain * grad_carried
    grad_mixed = jnp.stack([grad_query, grad_product * value_feat, grad_product * key_feat], axis=1)
    tail = jnp.concatenate([grad_mixed, jnp.zeros((2, 3, narrow), jnp.float32)], axis=0)
    grad_feats = (
        taps[0] * tail[:length] + taps[1] * tail[1 : length + 1] + taps[2] * tail[2:]
    ).astype(jnp.bfloat16)
    grad_taps = jnp.stack(
        [
            jnp.sum(grad_mixed * extended[2 - tap_index : 2 - tap_index + length], axis=0)
            for tap_index in range(3)
        ]
    )
    grad_skip = jnp.sum(grad_carried.astype(jnp.float32) * product.astype(jnp.float32), axis=0)
    return gated, grad_feats, grad_taps, grad_skip, both[:, narrow:]


def blocked_fallback(moved_in, taps, skip_gain, seq_parts, tok_rows, narrow):
    length = seq_parts * tok_rows
    fft_length = 2 * length
    local_feats = moved_in[None, :, :3]
    extended = jnp.concatenate(
        [jnp.zeros((1, 2, 3, narrow), local_feats.dtype), local_feats], axis=1
    )

    def local_spectrum(signal):
        blocks = signal.reshape(signal.shape[0], seq_parts, tok_rows, narrow).astype(jnp.float32)
        part_real, part_imag = across_blocks(
            blocks, jnp.arange(tok_rows, dtype=jnp.int32), seq_parts, fft_length
        )
        return within_blocks(part_real, part_imag)

    def local_signal(spectrum):
        part_real, part_imag = back_within(
            spectrum[0], spectrum[1], jnp.arange(2 * seq_parts, dtype=jnp.int32), fft_length
        )
        values = back_across(part_real, part_imag, seq_parts, fft_length)
        return values.reshape(values.shape[0], length, narrow)

    def no_rows(rows_part):
        return jnp.zeros_like(rows_part)

    return blocked_core(
        extended,
        moved_in[None, :, 3],
        taps,
        skip_gain,
        moved_in[:, 4],
        local_spectrum,
        local_signal,
        no_rows,
    )


def local(features, short_filter, response, skip_gain, cotangent):
    seq_parts = lax.axis_size("seq")
    dp_parts = lax.axis_size("dp")
    seq_index = lax.axis_index("seq")
    tok_rows = features.shape[1]
    chan_width = features.shape[2] // 3
    length = seq_parts * tok_rows
    narrow = chan_width // seq_parts
    offset = seq_index * narrow
    taps = short_filter.reshape(3, 3, chan_width)
    joined_in = jnp.concatenate(
        [
            features.reshape(tok_rows, 3 * chan_width),
            cotangent.reshape(tok_rows, chan_width),
            response,
        ],
        axis=1,
    )
    arranged = joined_in.reshape(tok_rows, 5, seq_parts, narrow).transpose(2, 0, 1, 3)
    moved_in = lax.all_to_all(arranged, "seq", 0, 0, tiled=True).reshape(length, 5, narrow)
    local_taps = lax.dynamic_slice_in_dim(taps, offset, narrow, 2)
    local_skip = lax.dynamic_slice_in_dim(skip_gain, offset, narrow, 0)
    if length <= 2048:
        gated, grad_feats, grad_taps, grad_skip, filter_part = block_core(
            moved_in[:, :3], moved_in[:, 3], moved_in[:, 4], local_taps, local_skip
        )
    else:
        gated, grad_feats, grad_taps, grad_skip, filter_part = blocked_fallback(
            moved_in, local_taps, local_skip, seq_parts, tok_rows, narrow
        )
        gated = gated.reshape(length, narrow)
        grad_feats = grad_feats.reshape(length, 3, narrow)
    joined_out = jnp.concatenate(
        [gated.reshape(seq_parts, tok_rows, 1, narrow), grad_feats.reshape(seq_parts, tok_rows, 3, narrow)],
        axis=2,
    )
    moved_out = lax.all_to_all(joined_out, "seq", 0, 0, tiled=True).transpose(1, 2, 0, 3)
    gated = moved_out[:, 0]
    grad_feats = moved_out[:, 1:]
    extra = 16
    small = jnp.concatenate(
        [grad_taps.reshape(9, narrow), grad_skip[None], jnp.zeros((extra - 10, narrow), jnp.float32)],
        axis=0,
    )
    chunks = jnp.concatenate(
        [
            filter_part.reshape(seq_parts, tok_rows, narrow),
            jnp.broadcast_to(small[None], (seq_parts, extra, narrow)),
        ],
        axis=1,
    )
    moved = lax.all_to_all(chunks, "seq", 0, 0, tiled=True)
    pair = seq_parts // dp_parts
    small_all = moved[:, tok_rows : tok_rows + 10]
    small_rows = (
        small_all.reshape(dp_parts, pair, 10, narrow)
        .transpose(1, 0, 2, 3)
        .reshape(pair, dp_parts * 10, narrow)
    )
    joined = jnp.concatenate(
        [moved[:, :tok_rows], jnp.tile(small_rows, (dp_parts, 1, 1))], axis=1
    )
    reduced = lax.psum_scatter(joined, "dp", scatter_dimension=0, tiled=True)
    filter_total = reduced[:, :tok_rows].transpose(1, 0, 2).reshape(tok_rows, pair * narrow)
    small_total = (
        reduced[:, tok_rows:]
        .reshape(pair, dp_parts, 10, narrow)
        .transpose(2, 1, 0, 3)
        .reshape(10, chan_width)
    )
    gated = gated.reshape(1, tok_rows, chan_width)
    grad_feats = grad_feats.reshape(1, tok_rows, 3 * chan_width)
    return (
        gated,
        grad_feats,
        small_total[:9].reshape(3, 3 * chan_width),
        small_total[9],
        filter_total,
    )


def solution(mesh):
    placed = (P("dp", "seq", None), P(), P("seq", None), P(), P("dp", "seq", None))
    return jax.shard_map(
        local,
        mesh=mesh,
        in_specs=placed,
        out_specs=(P("dp", "seq", None), P("dp", "seq", None), P(), P(), P("seq", "dp")),
        check_vma=False,
    )
```

```python
import math

import jax
import jax.numpy as jnp
from jax import lax
from jax.sharding import PartitionSpec as P


precise = lax.Precision.HIGHEST


def dft_table(count):
    series = jnp.arange(count, dtype=jnp.int32)
    angle = (series[:, None] * series[None, :] % count).astype(jnp.float32) * (
        2.0 * math.pi / count
    )
    return (jnp.cos(angle), jnp.sin(angle))


def across_blocks(signal, offsets, blocks, fft_length):
    double = jnp.arange(2 * blocks, dtype=jnp.int32)
    single = jnp.arange(blocks, dtype=jnp.int32)
    angle = (double[:, None] * single[None, :] % (2 * blocks)).astype(jnp.float32) * (
        math.pi / blocks
    )
    table = jnp.stack([jnp.cos(angle), -jnp.sin(angle)])
    first = jnp.einsum("oap,bpjk->obajk", table, signal, precision=precise)
    twist = (double[:, None] * offsets[None, :] % fft_length).astype(jnp.float32) * (
        -2.0 * math.pi / fft_length
    )
    cosine = jnp.cos(twist)[None, :, :, None]
    sine = jnp.sin(twist)[None, :, :, None]
    return (first[0] * cosine - first[1] * sine, first[0] * sine + first[1] * cosine)


def within_blocks(part_real, part_imag):
    table_cos, table_sin = dft_table(part_real.shape[2])
    table = jnp.stack([jnp.stack([table_cos, table_sin]), jnp.stack([-table_sin, table_cos])])
    spectra = jnp.einsum(
        "oibj,ixajk->oxabk", table, jnp.stack([part_real, part_imag]), precision=precise
    )
    return (spectra[0], spectra[1])


def back_within(spec_real, spec_imag, firsts, fft_length):
    count = spec_real.shape[2]
    table_cos, table_sin = dft_table(count)
    table = jnp.stack([jnp.stack([table_cos, -table_sin]), jnp.stack([table_sin, table_cos])])
    backs = jnp.einsum(
        "oibj,ixabk->oxajk", table, jnp.stack([spec_real, spec_imag]), precision=precise
    )
    series = jnp.arange(count, dtype=jnp.int32)
    twist = (firsts[:, None] * series[None, :] % fft_length).astype(jnp.float32) * (
        2.0 * math.pi / fft_length
    )
    cosine = jnp.cos(twist)[None, :, :, None]
    sine = jnp.sin(twist)[None, :, :, None]
    return (backs[0] * cosine - backs[1] * sine, backs[0] * sine + backs[1] * cosine)


def back_across(part_real, part_imag, blocks, fft_length):
    double = jnp.arange(2 * blocks, dtype=jnp.int32)
    single = jnp.arange(blocks, dtype=jnp.int32)
    angle = (single[:, None] * double[None, :] % (2 * blocks)).astype(jnp.float32) * (
        math.pi / blocks
    )
    table = jnp.stack([jnp.cos(angle), -jnp.sin(angle)])
    result = jnp.einsum(
        "ipa,ibajk->bpjk", table, jnp.stack([part_real, part_imag]), precision=precise
    )
    return result * (1.0 / fft_length)


def times_spectrum(left, right):
    return (left[0] * right[0] - left[1] * right[1], left[0] * right[1] + left[1] * right[0])


def times_conjugate(left, right):
    return (left[0] * right[0] + left[1] * right[1], left[1] * right[0] - left[0] * right[1])


def blocked_core(extended, cotangent, taps, skip_gain, response, to_spectrum, to_signal, after_rows):
    count = cotangent.shape[1]
    batch = cotangent.shape[0]
    mixed = taps[0] * extended[:, 2:] + taps[1] * extended[:, 1:-1] + taps[2] * extended[:, :-2]
    query_feat = mixed[:, :, 0]
    key_feat = mixed[:, :, 1]
    value_feat = mixed[:, :, 2]
    product = (key_feat * value_feat).astype(jnp.bfloat16)
    stacked = to_spectrum(jnp.concatenate([product, response[None]], axis=0))
    prod_spec = (stacked[0][:batch], stacked[1][:batch])
    resp_spec = (stacked[0][batch:], stacked[1][batch:])
    conv_out = to_signal(times_spectrum(prod_spec, resp_spec))
    carried = conv_out + skip_gain * product
    gated = (query_feat * carried).astype(jnp.bfloat16)
    grad_carried = (cotangent * query_feat).astype(jnp.bfloat16)
    grad_query = cotangent * carried
    grad_spec = to_spectrum(grad_carried)
    back_conv = times_conjugate(grad_spec, resp_spec)
    resp_grad = times_conjugate(grad_spec, prod_spec)
    joined_real = jnp.concatenate(
        [back_conv[0], jnp.sum(resp_grad[0], axis=0, keepdims=True)], axis=0
    )
    joined_imag = jnp.concatenate(
        [back_conv[1], jnp.sum(resp_grad[1], axis=0, keepdims=True)], axis=0
    )
    both = to_signal((joined_real, joined_imag))
    grad_product = both[:batch] + skip_gain * grad_carried
    grad_mixed = jnp.stack([grad_query, grad_product * value_feat, grad_product * key_feat], axis=2)
    tail = jnp.concatenate([grad_mixed, after_rows(grad_mixed[:, :2])], axis=1)
    grad_feats = (
        taps[0] * tail[:, :count] + taps[1] * tail[:, 1 : count + 1] + taps[2] * tail[:, 2:]
    ).astype(jnp.bfloat16)
    grad_taps = jnp.stack(
        [
            jnp.sum(grad_mixed * extended[:, 2 - tap_index : 2 - tap_index + count], axis=(0, 1))
            for tap_index in range(3)
        ]
    )
    grad_skip = jnp.sum(grad_carried.astype(jnp.float32) * product.astype(jnp.float32), axis=(0, 1))
    return (gated, grad_feats, grad_taps, grad_skip, both[batch])


def dft_tables(length):
    fft_length = 2 * length
    bins = length + 1
    freq = lax.broadcasted_iota(jnp.int32, (bins, length), 0)
    time = lax.broadcasted_iota(jnp.int32, (bins, length), 1)
    angle = lax.optimization_barrier((freq * time) % fft_length).astype(jnp.float32) * (
        2.0 * math.pi / fft_length
    )
    table = jnp.concatenate([jnp.cos(angle), -jnp.sin(angle)], axis=0)
    return table.astype(jnp.bfloat16)


def bf16_dot(left, right, dims):
    return lax.dot_general(left, right, (dims, ((), ())), preferred_element_type=jnp.float32)


def to_spectrum(table, signal):
    return bf16_dot(table, signal, ((1,), (0,)))


def to_signal(table, spectrum):
    bins = table.shape[0] // 2
    fft_length = 2 * (bins - 1)
    row = lax.broadcasted_iota(jnp.int32, (2 * bins, 1), 0)
    edge = (row == 0) | (row == bins - 1) | (row == bins) | (row == 2 * bins - 1)
    weight = jnp.where(edge, 1.0 / fft_length, 2.0 / fft_length)
    scaled = spectrum * weight
    spec_high = scaled.astype(jnp.bfloat16)
    spec_low = (scaled - spec_high.astype(jnp.float32)).astype(jnp.bfloat16)
    backward = ((0,), (0,))
    return bf16_dot(table, spec_high, backward) + bf16_dot(table, spec_low, backward)


def split(spectrum):
    bins = spectrum.shape[0] // 2
    return spectrum[:bins], spectrum[bins:]


def join(real, imag):
    return jnp.concatenate([real, imag], axis=0)


def block_core(feats, cot, resp, taps, skip_gain, gated_exchange):
    length = feats.shape[0]
    narrow = feats.shape[2]
    tables = dft_tables(length)
    extended = jnp.concatenate([jnp.zeros((2, 3, narrow), feats.dtype), feats], axis=0)
    mixed = taps[0] * extended[2:] + taps[1] * extended[1:-1] + taps[2] * extended[:-2]
    query_feat = mixed[:, 0]
    key_feat = mixed[:, 1]
    value_feat = mixed[:, 2]
    product = (key_feat * value_feat).astype(jnp.bfloat16)
    first = to_spectrum(tables, jnp.concatenate([product, resp], axis=1))
    prod_re, prod_im = split(first[:, :narrow])
    resp_re, resp_im = split(first[:, narrow:])
    conv_out = to_signal(
        tables, join(prod_re * resp_re - prod_im * resp_im, prod_re * resp_im + prod_im * resp_re)
    )
    carried = conv_out + skip_gain * product
    gated = (query_feat * carried).astype(jnp.bfloat16)
    grad_carried = (cot * query_feat).astype(jnp.bfloat16)
    grad_query = cot * carried
    gated_moved = gated_exchange(gated)
    grad_re, grad_im = split(to_spectrum(tables, grad_carried))
    back_spec = join(grad_re * resp_re + grad_im * resp_im, grad_im * resp_re - grad_re * resp_im)
    filt_spec = join(grad_re * prod_re + grad_im * prod_im, grad_im * prod_re - grad_re * prod_im)
    back_spec, gated_moved = lax.optimization_barrier((back_spec, gated_moved))
    both = to_signal(tables, jnp.concatenate([back_spec, filt_spec], axis=1))
    grad_product = both[:, :narrow] + skip_gain * grad_carried
    grad_mixed = jnp.stack([grad_query, grad_product * value_feat, grad_product * key_feat], axis=1)
    tail = jnp.concatenate([grad_mixed, jnp.zeros((2, 3, narrow), jnp.float32)], axis=0)
    grad_feats = (
        taps[0] * tail[:length] + taps[1] * tail[1 : length + 1] + taps[2] * tail[2:]
    ).astype(jnp.bfloat16)
    grad_taps = jnp.stack(
        [
            jnp.sum(grad_mixed * extended[2 - tap_index : 2 - tap_index + length], axis=0)
            for tap_index in range(3)
        ]
    )
    grad_skip = jnp.sum(grad_carried.astype(jnp.float32) * product.astype(jnp.float32), axis=0)
    return gated_moved, grad_feats, grad_taps, grad_skip, both[:, narrow:]


def blocked_fallback(moved_in, taps, skip_gain, seq_parts, tok_rows, narrow):
    length = seq_parts * tok_rows
    fft_length = 2 * length
    local_feats = moved_in[None, :, :3]
    extended = jnp.concatenate(
        [jnp.zeros((1, 2, 3, narrow), local_feats.dtype), local_feats], axis=1
    )

    def local_spectrum(signal):
        blocks = signal.reshape(signal.shape[0], seq_parts, tok_rows, narrow).astype(jnp.float32)
        part_real, part_imag = across_blocks(
            blocks, jnp.arange(tok_rows, dtype=jnp.int32), seq_parts, fft_length
        )
        return within_blocks(part_real, part_imag)

    def local_signal(spectrum):
        part_real, part_imag = back_within(
            spectrum[0], spectrum[1], jnp.arange(2 * seq_parts, dtype=jnp.int32), fft_length
        )
        values = back_across(part_real, part_imag, seq_parts, fft_length)
        return values.reshape(values.shape[0], length, narrow)

    def no_rows(rows_part):
        return jnp.zeros_like(rows_part)

    return blocked_core(
        extended,
        moved_in[None, :, 3],
        taps,
        skip_gain,
        moved_in[:, 4],
        local_spectrum,
        local_signal,
        no_rows,
    )


def local(features, short_filter, response, skip_gain, cotangent):
    seq_parts = lax.axis_size("seq")
    dp_parts = lax.axis_size("dp")
    seq_index = lax.axis_index("seq")
    tok_rows = features.shape[1]
    chan_width = features.shape[2] // 3
    length = seq_parts * tok_rows
    narrow = chan_width // seq_parts
    offset = seq_index * narrow
    taps = short_filter.reshape(3, 3, chan_width)
    joined_in = jnp.concatenate(
        [
            features.reshape(tok_rows, 3 * chan_width),
            cotangent.reshape(tok_rows, chan_width),
            response,
        ],
        axis=1,
    )
    arranged = joined_in.reshape(tok_rows, 5, seq_parts, narrow).transpose(2, 0, 1, 3)
    moved_in = lax.all_to_all(arranged, "seq", 0, 0, tiled=True).reshape(length, 5, narrow)
    local_taps = lax.dynamic_slice_in_dim(taps, offset, narrow, 2)
    local_skip = lax.dynamic_slice_in_dim(skip_gain, offset, narrow, 0)
    def gated_exchange(gated):
        return lax.all_to_all(gated.reshape(seq_parts, tok_rows, narrow), "seq", 0, 0, tiled=True)

    if length <= 2048:
        gated, grad_feats, grad_taps, grad_skip, filter_part = block_core(
            moved_in[:, :3], moved_in[:, 3], moved_in[:, 4], local_taps, local_skip, gated_exchange
        )
    else:
        gated, grad_feats, grad_taps, grad_skip, filter_part = blocked_fallback(
            moved_in, local_taps, local_skip, seq_parts, tok_rows, narrow
        )
        gated = gated_exchange(gated.reshape(length, narrow))
        grad_feats = grad_feats.reshape(length, 3, narrow)
    gated = gated.transpose(1, 0, 2)
    grad_feats = lax.all_to_all(
        grad_feats.reshape(seq_parts, tok_rows, 3, narrow), "seq", 0, 0, tiled=True
    ).transpose(1, 2, 0, 3)
    extra = 16
    small = jnp.concatenate(
        [grad_taps.reshape(9, narrow), grad_skip[None], jnp.zeros((extra - 10, narrow), jnp.float32)],
        axis=0,
    )
    chunks = jnp.concatenate(
        [
            filter_part.reshape(seq_parts, tok_rows, narrow),
            jnp.broadcast_to(small[None], (seq_parts, extra, narrow)),
        ],
        axis=1,
    )
    moved = lax.all_to_all(chunks, "seq", 0, 0, tiled=True)
    pair = seq_parts // dp_parts
    small_all = moved[:, tok_rows : tok_rows + 10]
    small_rows = (
        small_all.reshape(dp_parts, pair, 10, narrow)
        .transpose(1, 0, 2, 3)
        .reshape(pair, dp_parts * 10, narrow)
    )
    joined = jnp.concatenate(
        [moved[:, :tok_rows], jnp.tile(small_rows, (dp_parts, 1, 1))], axis=1
    )
    reduced = lax.psum_scatter(joined, "dp", scatter_dimension=0, tiled=True)
    filter_total = reduced[:, :tok_rows].transpose(1, 0, 2).reshape(tok_rows, pair * narrow)
    small_total = (
        reduced[:, tok_rows:]
        .reshape(pair, dp_parts, 10, narrow)
        .transpose(2, 1, 0, 3)
        .reshape(10, chan_width)
    )
    gated = gated.reshape(1, tok_rows, chan_width)
    grad_feats = grad_feats.reshape(1, tok_rows, 3 * chan_width)
    return (
        gated,
        grad_feats,
        small_total[:9].reshape(3, 3 * chan_width),
        small_total[9],
        filter_total,
    )


def solution(mesh):
    placed = (P("dp", "seq", None), P(), P("seq", None), P(), P("dp", "seq", None))
    return jax.shard_map(
        local,
        mesh=mesh,
        in_specs=placed,
        out_specs=(P("dp", "seq", None), P("dp", "seq", None), P(), P(), P("seq", "dp")),
        check_vma=False,
    )
```

```python
import math

import jax
import jax.numpy as jnp
from jax import lax
from jax.experimental import pallas as pl
from jax.sharding import PartitionSpec as P


precise = lax.Precision.HIGHEST


def dft_table(count):
    series = jnp.arange(count, dtype=jnp.int32)
    angle = (series[:, None] * series[None, :] % count).astype(jnp.float32) * (
        2.0 * math.pi / count
    )
    return (jnp.cos(angle), jnp.sin(angle))


def across_blocks(signal, offsets, blocks, fft_length):
    double = jnp.arange(2 * blocks, dtype=jnp.int32)
    single = jnp.arange(blocks, dtype=jnp.int32)
    angle = (double[:, None] * single[None, :] % (2 * blocks)).astype(jnp.float32) * (
        math.pi / blocks
    )
    table = jnp.stack([jnp.cos(angle), -jnp.sin(angle)])
    first = jnp.einsum("oap,bpjk->obajk", table, signal, precision=precise)
    twist = (double[:, None] * offsets[None, :] % fft_length).astype(jnp.float32) * (
        -2.0 * math.pi / fft_length
    )
    cosine = jnp.cos(twist)[None, :, :, None]
    sine = jnp.sin(twist)[None, :, :, None]
    return (first[0] * cosine - first[1] * sine, first[0] * sine + first[1] * cosine)


def within_blocks(part_real, part_imag):
    table_cos, table_sin = dft_table(part_real.shape[2])
    table = jnp.stack([jnp.stack([table_cos, table_sin]), jnp.stack([-table_sin, table_cos])])
    spectra = jnp.einsum(
        "oibj,ixajk->oxabk", table, jnp.stack([part_real, part_imag]), precision=precise
    )
    return (spectra[0], spectra[1])


def back_within(spec_real, spec_imag, firsts, fft_length):
    count = spec_real.shape[2]
    table_cos, table_sin = dft_table(count)
    table = jnp.stack([jnp.stack([table_cos, -table_sin]), jnp.stack([table_sin, table_cos])])
    backs = jnp.einsum(
        "oibj,ixabk->oxajk", table, jnp.stack([spec_real, spec_imag]), precision=precise
    )
    series = jnp.arange(count, dtype=jnp.int32)
    twist = (firsts[:, None] * series[None, :] % fft_length).astype(jnp.float32) * (
        2.0 * math.pi / fft_length
    )
    cosine = jnp.cos(twist)[None, :, :, None]
    sine = jnp.sin(twist)[None, :, :, None]
    return (backs[0] * cosine - backs[1] * sine, backs[0] * sine + backs[1] * cosine)


def back_across(part_real, part_imag, blocks, fft_length):
    double = jnp.arange(2 * blocks, dtype=jnp.int32)
    single = jnp.arange(blocks, dtype=jnp.int32)
    angle = (single[:, None] * double[None, :] % (2 * blocks)).astype(jnp.float32) * (
        math.pi / blocks
    )
    table = jnp.stack([jnp.cos(angle), -jnp.sin(angle)])
    result = jnp.einsum(
        "ipa,ibajk->bpjk", table, jnp.stack([part_real, part_imag]), precision=precise
    )
    return result * (1.0 / fft_length)


def times_spectrum(left, right):
    return (left[0] * right[0] - left[1] * right[1], left[0] * right[1] + left[1] * right[0])


def times_conjugate(left, right):
    return (left[0] * right[0] + left[1] * right[1], left[1] * right[0] - left[0] * right[1])


def blocked_core(extended, cotangent, taps, skip_gain, response, to_spectrum, to_signal, after_rows):
    count = cotangent.shape[1]
    batch = cotangent.shape[0]
    mixed = taps[0] * extended[:, 2:] + taps[1] * extended[:, 1:-1] + taps[2] * extended[:, :-2]
    query_feat = mixed[:, :, 0]
    key_feat = mixed[:, :, 1]
    value_feat = mixed[:, :, 2]
    product = (key_feat * value_feat).astype(jnp.bfloat16)
    stacked = to_spectrum(jnp.concatenate([product, response[None]], axis=0))
    prod_spec = (stacked[0][:batch], stacked[1][:batch])
    resp_spec = (stacked[0][batch:], stacked[1][batch:])
    conv_out = to_signal(times_spectrum(prod_spec, resp_spec))
    carried = conv_out + skip_gain * product
    gated = (query_feat * carried).astype(jnp.bfloat16)
    grad_carried = (cotangent * query_feat).astype(jnp.bfloat16)
    grad_query = cotangent * carried
    grad_spec = to_spectrum(grad_carried)
    back_conv = times_conjugate(grad_spec, resp_spec)
    resp_grad = times_conjugate(grad_spec, prod_spec)
    joined_real = jnp.concatenate(
        [back_conv[0], jnp.sum(resp_grad[0], axis=0, keepdims=True)], axis=0
    )
    joined_imag = jnp.concatenate(
        [back_conv[1], jnp.sum(resp_grad[1], axis=0, keepdims=True)], axis=0
    )
    both = to_signal((joined_real, joined_imag))
    grad_product = both[:batch] + skip_gain * grad_carried
    grad_mixed = jnp.stack([grad_query, grad_product * value_feat, grad_product * key_feat], axis=2)
    tail = jnp.concatenate([grad_mixed, after_rows(grad_mixed[:, :2])], axis=1)
    grad_feats = (
        taps[0] * tail[:, :count] + taps[1] * tail[:, 1 : count + 1] + taps[2] * tail[:, 2:]
    ).astype(jnp.bfloat16)
    grad_taps = jnp.stack(
        [
            jnp.sum(grad_mixed * extended[:, 2 - tap_index : 2 - tap_index + count], axis=(0, 1))
            for tap_index in range(3)
        ]
    )
    grad_skip = jnp.sum(grad_carried.astype(jnp.float32) * product.astype(jnp.float32), axis=(0, 1))
    return (gated, grad_feats, grad_taps, grad_skip, both[batch])


def dft_tables(length):
    fft_length = 2 * length
    bins = length + 1
    freq = lax.broadcasted_iota(jnp.int32, (bins, length), 0)
    time = lax.broadcasted_iota(jnp.int32, (bins, length), 1)
    angle = lax.optimization_barrier((freq * time) % fft_length).astype(jnp.float32) * (
        2.0 * math.pi / fft_length
    )
    table = jnp.concatenate([jnp.cos(angle), -jnp.sin(angle)], axis=0)
    return table.astype(jnp.bfloat16)


def bf16_dot(left, right, dims):
    return lax.dot_general(left, right, (dims, ((), ())), preferred_element_type=jnp.float32)


def to_spectrum(table, signal):
    return bf16_dot(table, signal, ((1,), (0,)))


def to_signal(table, spectrum):
    bins = table.shape[0] // 2
    fft_length = 2 * (bins - 1)
    row = lax.broadcasted_iota(jnp.int32, (2 * bins, 1), 0)
    edge = (row == 0) | (row == bins - 1) | (row == bins) | (row == 2 * bins - 1)
    weight = jnp.where(edge, 1.0 / fft_length, 2.0 / fft_length)
    scaled = spectrum * weight
    spec_high = scaled.astype(jnp.bfloat16)
    spec_low = (scaled - spec_high.astype(jnp.float32)).astype(jnp.bfloat16)
    backward = ((0,), (0,))
    return bf16_dot(table, spec_high, backward) + bf16_dot(table, spec_low, backward)


def split(spectrum):
    bins = spectrum.shape[0] // 2
    return spectrum[:bins], spectrum[bins:]


def join(real, imag):
    return jnp.concatenate([real, imag], axis=0)


def block_core(feats, cot, resp, taps, skip_gain):
    length = feats.shape[0]
    narrow = feats.shape[2]
    tables = dft_tables(length)
    extended = jnp.concatenate([jnp.zeros((2, 3, narrow), feats.dtype), feats], axis=0)
    mixed = taps[0] * extended[2:] + taps[1] * extended[1:-1] + taps[2] * extended[:-2]
    query_feat = mixed[:, 0]
    key_feat = mixed[:, 1]
    value_feat = mixed[:, 2]
    product = (key_feat * value_feat).astype(jnp.bfloat16)
    first = to_spectrum(tables, jnp.concatenate([product, resp], axis=1))
    prod_re, prod_im = split(first[:, :narrow])
    resp_re, resp_im = split(first[:, narrow:])
    conv_out = to_signal(
        tables, join(prod_re * resp_re - prod_im * resp_im, prod_re * resp_im + prod_im * resp_re)
    )
    carried = conv_out + skip_gain * product
    gated = (query_feat * carried).astype(jnp.bfloat16)
    grad_carried = (cot * query_feat).astype(jnp.bfloat16)
    grad_query = cot * carried
    grad_re, grad_im = split(to_spectrum(tables, grad_carried))
    back_spec = join(grad_re * resp_re + grad_im * resp_im, grad_im * resp_re - grad_re * resp_im)
    filt_spec = join(grad_re * prod_re + grad_im * prod_im, grad_im * prod_re - grad_re * prod_im)
    both = to_signal(tables, jnp.concatenate([back_spec, filt_spec], axis=1))
    grad_product = both[:, :narrow] + skip_gain * grad_carried
    grad_mixed = jnp.stack([grad_query, grad_product * value_feat, grad_product * key_feat], axis=1)
    tail = jnp.concatenate([grad_mixed, jnp.zeros((2, 3, narrow), jnp.float32)], axis=0)
    grad_feats = (
        taps[0] * tail[:length] + taps[1] * tail[1 : length + 1] + taps[2] * tail[2:]
    ).astype(jnp.bfloat16)
    grad_taps = jnp.stack(
        [
            jnp.sum(grad_mixed * extended[2 - tap_index : 2 - tap_index + length], axis=0)
            for tap_index in range(3)
        ]
    )
    grad_skip = jnp.sum(grad_carried.astype(jnp.float32) * product.astype(jnp.float32), axis=0)
    return gated, grad_feats, grad_taps, grad_skip, both[:, narrow:]


def blocked_fallback(moved_in, taps, skip_gain, seq_parts, tok_rows, narrow):
    length = seq_parts * tok_rows
    fft_length = 2 * length
    local_feats = moved_in[None, :, :3]
    extended = jnp.concatenate(
        [jnp.zeros((1, 2, 3, narrow), local_feats.dtype), local_feats], axis=1
    )

    def local_spectrum(signal):
        blocks = signal.reshape(signal.shape[0], seq_parts, tok_rows, narrow).astype(jnp.float32)
        part_real, part_imag = across_blocks(
            blocks, jnp.arange(tok_rows, dtype=jnp.int32), seq_parts, fft_length
        )
        return within_blocks(part_real, part_imag)

    def local_signal(spectrum):
        part_real, part_imag = back_within(
            spectrum[0], spectrum[1], jnp.arange(2 * seq_parts, dtype=jnp.int32), fft_length
        )
        values = back_across(part_real, part_imag, seq_parts, fft_length)
        return values.reshape(values.shape[0], length, narrow)

    def no_rows(rows_part):
        return jnp.zeros_like(rows_part)

    return blocked_core(
        extended,
        moved_in[None, :, 3],
        taps,
        skip_gain,
        moved_in[:, 4],
        local_spectrum,
        local_signal,
        no_rows,
    )


def gather_tiles(features2d, cot2d, resp2d, seq_parts, narrow):
    rows = features2d.shape[0]

    def body(f0, f1, f2, c_ref, r_ref, out_ref):
        out_ref[0, 0] = f0[...]
        out_ref[0, 1] = f1[...]
        out_ref[0, 2] = f2[...]
        out_ref[0, 3] = c_ref[...]
        out_ref[0, 4] = r_ref[...]

    def group_spec(group):
        return pl.BlockSpec((rows, narrow), lambda s: (0, group * seq_parts + s))

    return pl.pallas_call(
        body,
        grid=(seq_parts,),
        in_specs=[group_spec(0), group_spec(1), group_spec(2), group_spec(0), group_spec(0)],
        out_specs=pl.BlockSpec((1, 5, rows, narrow), lambda s: (s, 0, 0, 0)),
        out_shape=jax.ShapeDtypeStruct((seq_parts, 5, rows, narrow), features2d.dtype),
    )(features2d, features2d, features2d, cot2d, resp2d)


def local(features, short_filter, response, skip_gain, cotangent):
    seq_parts = lax.axis_size("seq")
    dp_parts = lax.axis_size("dp")
    seq_index = lax.axis_index("seq")
    tok_rows = features.shape[1]
    chan_width = features.shape[2] // 3
    length = seq_parts * tok_rows
    narrow = chan_width // seq_parts
    offset = seq_index * narrow
    taps = short_filter.reshape(3, 3, chan_width)
    if narrow % 128 == 0 and tok_rows % 16 == 0:
        arranged = gather_tiles(
            features.reshape(tok_rows, 3 * chan_width),
            cotangent.reshape(tok_rows, chan_width),
            response,
            seq_parts,
            narrow,
        )
        moved_in = (
            lax.all_to_all(arranged, "seq", 0, 0, tiled=True)
            .transpose(0, 2, 1, 3)
            .reshape(length, 5, narrow)
        )
    else:
        joined_in = jnp.concatenate(
            [
                features.reshape(tok_rows, 3 * chan_width),
                cotangent.reshape(tok_rows, chan_width),
                response,
            ],
            axis=1,
        )
        arranged = joined_in.reshape(tok_rows, 5, seq_parts, narrow).transpose(2, 0, 1, 3)
        moved_in = lax.all_to_all(arranged, "seq", 0, 0, tiled=True).reshape(length, 5, narrow)
    local_taps = lax.dynamic_slice_in_dim(taps, offset, narrow, 2)
    local_skip = lax.dynamic_slice_in_dim(skip_gain, offset, narrow, 0)
    if length <= 2048:
        gated, grad_feats, grad_taps, grad_skip, filter_part = block_core(
            moved_in[:, :3], moved_in[:, 3], moved_in[:, 4], local_taps, local_skip
        )
    else:
        gated, grad_feats, grad_taps, grad_skip, filter_part = blocked_fallback(
            moved_in, local_taps, local_skip, seq_parts, tok_rows, narrow
        )
        gated = gated.reshape(length, narrow)
        grad_feats = grad_feats.reshape(length, 3, narrow)
    joined_out = jnp.concatenate(
        [gated.reshape(seq_parts, tok_rows, 1, narrow), grad_feats.reshape(seq_parts, tok_rows, 3, narrow)],
        axis=2,
    )
    moved_out = lax.all_to_all(joined_out, "seq", 0, 0, tiled=True).transpose(1, 2, 0, 3)
    gated = moved_out[:, 0]
    grad_feats = moved_out[:, 1:]
    extra = 16
    small = jnp.concatenate(
        [grad_taps.reshape(9, narrow), grad_skip[None], jnp.zeros((extra - 10, narrow), jnp.float32)],
        axis=0,
    )
    chunks = jnp.concatenate(
        [
            filter_part.reshape(seq_parts, tok_rows, narrow),
            jnp.broadcast_to(small[None], (seq_parts, extra, narrow)),
        ],
        axis=1,
    )
    moved = lax.all_to_all(chunks, "seq", 0, 0, tiled=True)
    pair = seq_parts // dp_parts
    small_all = moved[:, tok_rows : tok_rows + 10]
    small_rows = (
        small_all.reshape(dp_parts, pair, 10, narrow)
        .transpose(1, 0, 2, 3)
        .reshape(pair, dp_parts * 10, narrow)
    )
    joined = jnp.concatenate(
        [moved[:, :tok_rows], jnp.tile(small_rows, (dp_parts, 1, 1))], axis=1
    )
    reduced = lax.psum_scatter(joined, "dp", scatter_dimension=0, tiled=True)
    filter_total = reduced[:, :tok_rows].transpose(1, 0, 2).reshape(tok_rows, pair * narrow)
    small_total = (
        reduced[:, tok_rows:]
        .reshape(pair, dp_parts, 10, narrow)
        .transpose(2, 1, 0, 3)
        .reshape(10, chan_width)
    )
    gated = gated.reshape(1, tok_rows, chan_width)
    grad_feats = grad_feats.reshape(1, tok_rows, 3 * chan_width)
    return (
        gated,
        grad_feats,
        small_total[:9].reshape(3, 3 * chan_width),
        small_total[9],
        filter_total,
    )


def solution(mesh):
    placed = (P("dp", "seq", None), P(), P("seq", None), P(), P("dp", "seq", None))
    return jax.shard_map(
        local,
        mesh=mesh,
        in_specs=placed,
        out_specs=(P("dp", "seq", None), P("dp", "seq", None), P(), P(), P("seq", "dp")),
        check_vma=False,
    )
```

```python
import math

import jax
import jax.numpy as jnp
from jax import lax
from jax.experimental import pallas as pl
from jax.sharding import PartitionSpec as P


precise = lax.Precision.HIGHEST


def dft_table(count):
    series = jnp.arange(count, dtype=jnp.int32)
    angle = (series[:, None] * series[None, :] % count).astype(jnp.float32) * (
        2.0 * math.pi / count
    )
    return (jnp.cos(angle), jnp.sin(angle))


def across_blocks(signal, offsets, blocks, fft_length):
    double = jnp.arange(2 * blocks, dtype=jnp.int32)
    single = jnp.arange(blocks, dtype=jnp.int32)
    angle = (double[:, None] * single[None, :] % (2 * blocks)).astype(jnp.float32) * (
        math.pi / blocks
    )
    table = jnp.stack([jnp.cos(angle), -jnp.sin(angle)])
    first = jnp.einsum("oap,bpjk->obajk", table, signal, precision=precise)
    twist = (double[:, None] * offsets[None, :] % fft_length).astype(jnp.float32) * (
        -2.0 * math.pi / fft_length
    )
    cosine = jnp.cos(twist)[None, :, :, None]
    sine = jnp.sin(twist)[None, :, :, None]
    return (first[0] * cosine - first[1] * sine, first[0] * sine + first[1] * cosine)


def within_blocks(part_real, part_imag):
    table_cos, table_sin = dft_table(part_real.shape[2])
    table = jnp.stack([jnp.stack([table_cos, table_sin]), jnp.stack([-table_sin, table_cos])])
    spectra = jnp.einsum(
        "oibj,ixajk->oxabk", table, jnp.stack([part_real, part_imag]), precision=precise
    )
    return (spectra[0], spectra[1])


def back_within(spec_real, spec_imag, firsts, fft_length):
    count = spec_real.shape[2]
    table_cos, table_sin = dft_table(count)
    table = jnp.stack([jnp.stack([table_cos, -table_sin]), jnp.stack([table_sin, table_cos])])
    backs = jnp.einsum(
        "oibj,ixabk->oxajk", table, jnp.stack([spec_real, spec_imag]), precision=precise
    )
    series = jnp.arange(count, dtype=jnp.int32)
    twist = (firsts[:, None] * series[None, :] % fft_length).astype(jnp.float32) * (
        2.0 * math.pi / fft_length
    )
    cosine = jnp.cos(twist)[None, :, :, None]
    sine = jnp.sin(twist)[None, :, :, None]
    return (backs[0] * cosine - backs[1] * sine, backs[0] * sine + backs[1] * cosine)


def back_across(part_real, part_imag, blocks, fft_length):
    double = jnp.arange(2 * blocks, dtype=jnp.int32)
    single = jnp.arange(blocks, dtype=jnp.int32)
    angle = (single[:, None] * double[None, :] % (2 * blocks)).astype(jnp.float32) * (
        math.pi / blocks
    )
    table = jnp.stack([jnp.cos(angle), -jnp.sin(angle)])
    result = jnp.einsum(
        "ipa,ibajk->bpjk", table, jnp.stack([part_real, part_imag]), precision=precise
    )
    return result * (1.0 / fft_length)


def times_spectrum(left, right):
    return (left[0] * right[0] - left[1] * right[1], left[0] * right[1] + left[1] * right[0])


def times_conjugate(left, right):
    return (left[0] * right[0] + left[1] * right[1], left[1] * right[0] - left[0] * right[1])


def blocked_core(extended, cotangent, taps, skip_gain, response, to_spectrum, to_signal, after_rows):
    count = cotangent.shape[1]
    batch = cotangent.shape[0]
    mixed = taps[0] * extended[:, 2:] + taps[1] * extended[:, 1:-1] + taps[2] * extended[:, :-2]
    query_feat = mixed[:, :, 0]
    key_feat = mixed[:, :, 1]
    value_feat = mixed[:, :, 2]
    product = (key_feat * value_feat).astype(jnp.bfloat16)
    stacked = to_spectrum(jnp.concatenate([product, response[None]], axis=0))
    prod_spec = (stacked[0][:batch], stacked[1][:batch])
    resp_spec = (stacked[0][batch:], stacked[1][batch:])
    conv_out = to_signal(times_spectrum(prod_spec, resp_spec))
    carried = conv_out + skip_gain * product
    gated = (query_feat * carried).astype(jnp.bfloat16)
    grad_carried = (cotangent * query_feat).astype(jnp.bfloat16)
    grad_query = cotangent * carried
    grad_spec = to_spectrum(grad_carried)
    back_conv = times_conjugate(grad_spec, resp_spec)
    resp_grad = times_conjugate(grad_spec, prod_spec)
    joined_real = jnp.concatenate(
        [back_conv[0], jnp.sum(resp_grad[0], axis=0, keepdims=True)], axis=0
    )
    joined_imag = jnp.concatenate(
        [back_conv[1], jnp.sum(resp_grad[1], axis=0, keepdims=True)], axis=0
    )
    both = to_signal((joined_real, joined_imag))
    grad_product = both[:batch] + skip_gain * grad_carried
    grad_mixed = jnp.stack([grad_query, grad_product * value_feat, grad_product * key_feat], axis=2)
    tail = jnp.concatenate([grad_mixed, after_rows(grad_mixed[:, :2])], axis=1)
    grad_feats = (
        taps[0] * tail[:, :count] + taps[1] * tail[:, 1 : count + 1] + taps[2] * tail[:, 2:]
    ).astype(jnp.bfloat16)
    grad_taps = jnp.stack(
        [
            jnp.sum(grad_mixed * extended[:, 2 - tap_index : 2 - tap_index + count], axis=(0, 1))
            for tap_index in range(3)
        ]
    )
    grad_skip = jnp.sum(grad_carried.astype(jnp.float32) * product.astype(jnp.float32), axis=(0, 1))
    return (gated, grad_feats, grad_taps, grad_skip, both[batch])


def dft_tables(length):
    fft_length = 2 * length
    bins = length + 1
    freq = lax.broadcasted_iota(jnp.int32, (bins, length), 0)
    time = lax.broadcasted_iota(jnp.int32, (bins, length), 1)
    angle = lax.optimization_barrier((freq * time) % fft_length).astype(jnp.float32) * (
        2.0 * math.pi / fft_length
    )
    table = jnp.concatenate([jnp.cos(angle), -jnp.sin(angle)], axis=0)
    return table.astype(jnp.bfloat16)


def bf16_dot(left, right, dims):
    return lax.dot_general(left, right, (dims, ((), ())), preferred_element_type=jnp.float32)


def to_spectrum(table, signal):
    return bf16_dot(table, signal, ((1,), (0,)))


def to_signal(table, spectrum):
    bins = table.shape[0] // 2
    fft_length = 2 * (bins - 1)
    row = lax.broadcasted_iota(jnp.int32, (2 * bins, 1), 0)
    edge = (row == 0) | (row == bins - 1) | (row == bins) | (row == 2 * bins - 1)
    weight = jnp.where(edge, 1.0 / fft_length, 2.0 / fft_length)
    scaled = spectrum * weight
    spec_high = scaled.astype(jnp.bfloat16)
    spec_low = (scaled - spec_high.astype(jnp.float32)).astype(jnp.bfloat16)
    backward = ((0,), (0,))
    return bf16_dot(table, spec_high, backward) + bf16_dot(table, spec_low, backward)


def split(spectrum):
    bins = spectrum.shape[0] // 2
    return spectrum[:bins], spectrum[bins:]


def join(real, imag):
    return jnp.concatenate([real, imag], axis=0)


def block_core(feats, cot, resp, taps, skip_gain):
    length = feats.shape[0]
    narrow = feats.shape[2]
    tables = dft_tables(length)
    extended = jnp.concatenate([jnp.zeros((2, 3, narrow), feats.dtype), feats], axis=0)
    mixed = taps[0] * extended[2:] + taps[1] * extended[1:-1] + taps[2] * extended[:-2]
    query_feat = mixed[:, 0]
    key_feat = mixed[:, 1]
    value_feat = mixed[:, 2]
    product = (key_feat * value_feat).astype(jnp.bfloat16)
    first = to_spectrum(tables, jnp.concatenate([product, resp], axis=1))
    prod_re, prod_im = split(first[:, :narrow])
    resp_re, resp_im = split(first[:, narrow:])
    conv_out = to_signal(
        tables, join(prod_re * resp_re - prod_im * resp_im, prod_re * resp_im + prod_im * resp_re)
    )
    carried = conv_out + skip_gain * product
    gated = (query_feat * carried).astype(jnp.bfloat16)
    grad_carried = (cot * query_feat).astype(jnp.bfloat16)
    grad_query = cot * carried
    grad_re, grad_im = split(to_spectrum(tables, grad_carried))
    back_spec = join(grad_re * resp_re + grad_im * resp_im, grad_im * resp_re - grad_re * resp_im)
    filt_spec = join(grad_re * prod_re + grad_im * prod_im, grad_im * prod_re - grad_re * prod_im)
    both = to_signal(tables, jnp.concatenate([back_spec, filt_spec], axis=1))
    grad_product = both[:, :narrow] + skip_gain * grad_carried
    grad_mixed = jnp.stack([grad_query, grad_product * value_feat, grad_product * key_feat], axis=1)
    tail = jnp.concatenate([grad_mixed, jnp.zeros((2, 3, narrow), jnp.float32)], axis=0)
    grad_feats = (
        taps[0] * tail[:length] + taps[1] * tail[1 : length + 1] + taps[2] * tail[2:]
    ).astype(jnp.bfloat16)
    grad_taps = jnp.stack(
        [
            jnp.sum(grad_mixed * extended[2 - tap_index : 2 - tap_index + length], axis=0)
            for tap_index in range(3)
        ]
    )
    grad_skip = jnp.sum(grad_carried.astype(jnp.float32) * product.astype(jnp.float32), axis=0)
    return gated, grad_feats, grad_taps, grad_skip, both[:, narrow:]


def blocked_fallback(moved_in, taps, skip_gain, seq_parts, tok_rows, narrow):
    length = seq_parts * tok_rows
    fft_length = 2 * length
    local_feats = moved_in[None, :, :3]
    extended = jnp.concatenate(
        [jnp.zeros((1, 2, 3, narrow), local_feats.dtype), local_feats], axis=1
    )

    def local_spectrum(signal):
        blocks = signal.reshape(signal.shape[0], seq_parts, tok_rows, narrow).astype(jnp.float32)
        part_real, part_imag = across_blocks(
            blocks, jnp.arange(tok_rows, dtype=jnp.int32), seq_parts, fft_length
        )
        return within_blocks(part_real, part_imag)

    def local_signal(spectrum):
        part_real, part_imag = back_within(
            spectrum[0], spectrum[1], jnp.arange(2 * seq_parts, dtype=jnp.int32), fft_length
        )
        values = back_across(part_real, part_imag, seq_parts, fft_length)
        return values.reshape(values.shape[0], length, narrow)

    def no_rows(rows_part):
        return jnp.zeros_like(rows_part)

    return blocked_core(
        extended,
        moved_in[None, :, 3],
        taps,
        skip_gain,
        moved_in[:, 4],
        local_spectrum,
        local_signal,
        no_rows,
    )


def gather_tiles(features2d, cot2d, resp2d, seq_parts, narrow):
    rows = features2d.shape[0]

    def body(f0, f1, f2, c_ref, r_ref, out_ref):
        out_ref[0, 0] = f0[...]
        out_ref[0, 1] = f1[...]
        out_ref[0, 2] = f2[...]
        out_ref[0, 3] = c_ref[...]
        out_ref[0, 4] = r_ref[...]

    def group_spec(group):
        return pl.BlockSpec((rows, narrow), lambda s: (0, group * seq_parts + s))

    return pl.pallas_call(
        body,
        grid=(seq_parts,),
        in_specs=[group_spec(0), group_spec(1), group_spec(2), group_spec(0), group_spec(0)],
        out_specs=pl.BlockSpec((1, 5, rows, narrow), lambda s: (s, 0, 0, 0)),
        out_shape=jax.ShapeDtypeStruct((seq_parts, 5, rows, narrow), features2d.dtype),
    )(features2d, features2d, features2d, cot2d, resp2d)


def scatter_tiles(moved, seq_parts, narrow):
    rows = moved.shape[2]

    def body(in_ref, gated_ref, feats_ref):
        group = pl.program_id(0)

        @pl.when(group == 0)
        def _():
            for source in range(seq_parts):
                gated_ref[:, source * narrow : (source + 1) * narrow] = in_ref[source, 0]

        @pl.when(group > 0)
        def _():
            for source in range(seq_parts):
                feats_ref[:, source * narrow : (source + 1) * narrow] = in_ref[source, 0]

    width = seq_parts * narrow
    return pl.pallas_call(
        body,
        grid=(4,),
        in_specs=[pl.BlockSpec((seq_parts, 1, rows, narrow), lambda g: (0, g, 0, 0))],
        out_specs=[
            pl.BlockSpec((rows, width), lambda g: (0, 0)),
            pl.BlockSpec((rows, width), lambda g: (0, jnp.maximum(g - 1, 0))),
        ],
        out_shape=[
            jax.ShapeDtypeStruct((rows, width), moved.dtype),
            jax.ShapeDtypeStruct((rows, 3 * width), moved.dtype),
        ],
    )(moved)


def local(features, short_filter, response, skip_gain, cotangent):
    seq_parts = lax.axis_size("seq")
    dp_parts = lax.axis_size("dp")
    seq_index = lax.axis_index("seq")
    tok_rows = features.shape[1]
    chan_width = features.shape[2] // 3
    length = seq_parts * tok_rows
    narrow = chan_width // seq_parts
    offset = seq_index * narrow
    taps = short_filter.reshape(3, 3, chan_width)
    if narrow % 128 == 0 and tok_rows % 16 == 0:
        arranged = gather_tiles(
            features.reshape(tok_rows, 3 * chan_width),
            cotangent.reshape(tok_rows, chan_width),
            response,
            seq_parts,
            narrow,
        )
        moved_in = (
            lax.all_to_all(arranged, "seq", 0, 0, tiled=True)
            .transpose(0, 2, 1, 3)
            .reshape(length, 5, narrow)
        )
    else:
        joined_in = jnp.concatenate(
            [
                features.reshape(tok_rows, 3 * chan_width),
                cotangent.reshape(tok_rows, chan_width),
                response,
            ],
            axis=1,
        )
        arranged = joined_in.reshape(tok_rows, 5, seq_parts, narrow).transpose(2, 0, 1, 3)
        moved_in = lax.all_to_all(arranged, "seq", 0, 0, tiled=True).reshape(length, 5, narrow)
    local_taps = lax.dynamic_slice_in_dim(taps, offset, narrow, 2)
    local_skip = lax.dynamic_slice_in_dim(skip_gain, offset, narrow, 0)
    if length <= 2048:
        gated, grad_feats, grad_taps, grad_skip, filter_part = block_core(
            moved_in[:, :3], moved_in[:, 3], moved_in[:, 4], local_taps, local_skip
        )
    else:
        gated, grad_feats, grad_taps, grad_skip, filter_part = blocked_fallback(
            moved_in, local_taps, local_skip, seq_parts, tok_rows, narrow
        )
        gated = gated.reshape(length, narrow)
        grad_feats = grad_feats.reshape(length, 3, narrow)
    if narrow % 128 == 0 and tok_rows % 16 == 0:
        joined_out = jnp.concatenate(
            [
                gated.reshape(seq_parts, 1, tok_rows, narrow),
                grad_feats.reshape(seq_parts, tok_rows, 3, narrow).transpose(0, 2, 1, 3),
            ],
            axis=1,
        )
        moved_out = lax.all_to_all(joined_out, "seq", 0, 0, tiled=True)
        gated, grad_feats = scatter_tiles(moved_out, seq_parts, narrow)
    else:
        joined_out = jnp.concatenate(
            [gated.reshape(seq_parts, tok_rows, 1, narrow), grad_feats.reshape(seq_parts, tok_rows, 3, narrow)],
            axis=2,
        )
        moved_out = lax.all_to_all(joined_out, "seq", 0, 0, tiled=True).transpose(1, 2, 0, 3)
        gated = moved_out[:, 0]
        grad_feats = moved_out[:, 1:]
    extra = 16
    small = jnp.concatenate(
        [grad_taps.reshape(9, narrow), grad_skip[None], jnp.zeros((extra - 10, narrow), jnp.float32)],
        axis=0,
    )
    chunks = jnp.concatenate(
        [
            filter_part.reshape(seq_parts, tok_rows, narrow),
            jnp.broadcast_to(small[None], (seq_parts, extra, narrow)),
        ],
        axis=1,
    )
    moved = lax.all_to_all(chunks, "seq", 0, 0, tiled=True)
    pair = seq_parts // dp_parts
    small_all = moved[:, tok_rows : tok_rows + 10]
    small_rows = (
        small_all.reshape(dp_parts, pair, 10, narrow)
        .transpose(1, 0, 2, 3)
        .reshape(pair, dp_parts * 10, narrow)
    )
    joined = jnp.concatenate(
        [moved[:, :tok_rows], jnp.tile(small_rows, (dp_parts, 1, 1))], axis=1
    )
    reduced = lax.psum_scatter(joined, "dp", scatter_dimension=0, tiled=True)
    filter_total = reduced[:, :tok_rows].transpose(1, 0, 2).reshape(tok_rows, pair * narrow)
    small_total = (
        reduced[:, tok_rows:]
        .reshape(pair, dp_parts, 10, narrow)
        .transpose(2, 1, 0, 3)
        .reshape(10, chan_width)
    )
    gated = gated.reshape(1, tok_rows, chan_width)
    grad_feats = grad_feats.reshape(1, tok_rows, 3 * chan_width)
    return (
        gated,
        grad_feats,
        small_total[:9].reshape(3, 3 * chan_width),
        small_total[9],
        filter_total,
    )


def solution(mesh):
    placed = (P("dp", "seq", None), P(), P("seq", None), P(), P("dp", "seq", None))
    return jax.shard_map(
        local,
        mesh=mesh,
        in_specs=placed,
        out_specs=(P("dp", "seq", None), P("dp", "seq", None), P(), P(), P("seq", "dp")),
        check_vma=False,
    )
```

```python
import math

import jax
import jax.numpy as jnp
from jax import lax
from jax.experimental import pallas as pl
from jax.sharding import PartitionSpec as P


precise = lax.Precision.HIGHEST


def dft_table(count):
    series = jnp.arange(count, dtype=jnp.int32)
    angle = (series[:, None] * series[None, :] % count).astype(jnp.float32) * (
        2.0 * math.pi / count
    )
    return (jnp.cos(angle), jnp.sin(angle))


def across_blocks(signal, offsets, blocks, fft_length):
    double = jnp.arange(2 * blocks, dtype=jnp.int32)
    single = jnp.arange(blocks, dtype=jnp.int32)
    angle = (double[:, None] * single[None, :] % (2 * blocks)).astype(jnp.float32) * (
        math.pi / blocks
    )
    table = jnp.stack([jnp.cos(angle), -jnp.sin(angle)])
    first = jnp.einsum("oap,bpjk->obajk", table, signal, precision=precise)
    twist = (double[:, None] * offsets[None, :] % fft_length).astype(jnp.float32) * (
        -2.0 * math.pi / fft_length
    )
    cosine = jnp.cos(twist)[None, :, :, None]
    sine = jnp.sin(twist)[None, :, :, None]
    return (first[0] * cosine - first[1] * sine, first[0] * sine + first[1] * cosine)


def within_blocks(part_real, part_imag):
    table_cos, table_sin = dft_table(part_real.shape[2])
    table = jnp.stack([jnp.stack([table_cos, table_sin]), jnp.stack([-table_sin, table_cos])])
    spectra = jnp.einsum(
        "oibj,ixajk->oxabk", table, jnp.stack([part_real, part_imag]), precision=precise
    )
    return (spectra[0], spectra[1])


def back_within(spec_real, spec_imag, firsts, fft_length):
    count = spec_real.shape[2]
    table_cos, table_sin = dft_table(count)
    table = jnp.stack([jnp.stack([table_cos, -table_sin]), jnp.stack([table_sin, table_cos])])
    backs = jnp.einsum(
        "oibj,ixabk->oxajk", table, jnp.stack([spec_real, spec_imag]), precision=precise
    )
    series = jnp.arange(count, dtype=jnp.int32)
    twist = (firsts[:, None] * series[None, :] % fft_length).astype(jnp.float32) * (
        2.0 * math.pi / fft_length
    )
    cosine = jnp.cos(twist)[None, :, :, None]
    sine = jnp.sin(twist)[None, :, :, None]
    return (backs[0] * cosine - backs[1] * sine, backs[0] * sine + backs[1] * cosine)


def back_across(part_real, part_imag, blocks, fft_length):
    double = jnp.arange(2 * blocks, dtype=jnp.int32)
    single = jnp.arange(blocks, dtype=jnp.int32)
    angle = (single[:, None] * double[None, :] % (2 * blocks)).astype(jnp.float32) * (
        math.pi / blocks
    )
    table = jnp.stack([jnp.cos(angle), -jnp.sin(angle)])
    result = jnp.einsum(
        "ipa,ibajk->bpjk", table, jnp.stack([part_real, part_imag]), precision=precise
    )
    return result * (1.0 / fft_length)


def times_spectrum(left, right):
    return (left[0] * right[0] - left[1] * right[1], left[0] * right[1] + left[1] * right[0])


def times_conjugate(left, right):
    return (left[0] * right[0] + left[1] * right[1], left[1] * right[0] - left[0] * right[1])


def blocked_core(extended, cotangent, taps, skip_gain, response, to_spectrum, to_signal, after_rows):
    count = cotangent.shape[1]
    batch = cotangent.shape[0]
    mixed = taps[0] * extended[:, 2:] + taps[1] * extended[:, 1:-1] + taps[2] * extended[:, :-2]
    query_feat = mixed[:, :, 0]
    key_feat = mixed[:, :, 1]
    value_feat = mixed[:, :, 2]
    product = (key_feat * value_feat).astype(jnp.bfloat16)
    stacked = to_spectrum(jnp.concatenate([product, response[None]], axis=0))
    prod_spec = (stacked[0][:batch], stacked[1][:batch])
    resp_spec = (stacked[0][batch:], stacked[1][batch:])
    conv_out = to_signal(times_spectrum(prod_spec, resp_spec))
    carried = conv_out + skip_gain * product
    gated = (query_feat * carried).astype(jnp.bfloat16)
    grad_carried = (cotangent * query_feat).astype(jnp.bfloat16)
    grad_query = cotangent * carried
    grad_spec = to_spectrum(grad_carried)
    back_conv = times_conjugate(grad_spec, resp_spec)
    resp_grad = times_conjugate(grad_spec, prod_spec)
    joined_real = jnp.concatenate(
        [back_conv[0], jnp.sum(resp_grad[0], axis=0, keepdims=True)], axis=0
    )
    joined_imag = jnp.concatenate(
        [back_conv[1], jnp.sum(resp_grad[1], axis=0, keepdims=True)], axis=0
    )
    both = to_signal((joined_real, joined_imag))
    grad_product = both[:batch] + skip_gain * grad_carried
    grad_mixed = jnp.stack([grad_query, grad_product * value_feat, grad_product * key_feat], axis=2)
    tail = jnp.concatenate([grad_mixed, after_rows(grad_mixed[:, :2])], axis=1)
    grad_feats = (
        taps[0] * tail[:, :count] + taps[1] * tail[:, 1 : count + 1] + taps[2] * tail[:, 2:]
    ).astype(jnp.bfloat16)
    grad_taps = jnp.stack(
        [
            jnp.sum(grad_mixed * extended[:, 2 - tap_index : 2 - tap_index + count], axis=(0, 1))
            for tap_index in range(3)
        ]
    )
    grad_skip = jnp.sum(grad_carried.astype(jnp.float32) * product.astype(jnp.float32), axis=(0, 1))
    return (gated, grad_feats, grad_taps, grad_skip, both[batch])


def dft_tables(length):
    fft_length = 2 * length
    bins = length + 1
    freq = lax.broadcasted_iota(jnp.int32, (bins, length), 0)
    time = lax.broadcasted_iota(jnp.int32, (bins, length), 1)
    angle = lax.optimization_barrier((freq * time) % fft_length).astype(jnp.float32) * (
        2.0 * math.pi / fft_length
    )
    table = jnp.concatenate([jnp.cos(angle), -jnp.sin(angle)], axis=0)
    return table.astype(jnp.bfloat16)


def bf16_dot(left, right, dims):
    return lax.dot_general(left, right, (dims, ((), ())), preferred_element_type=jnp.float32)


def to_spectrum(table, signal):
    return bf16_dot(table, signal, ((1,), (0,)))


def to_signal(table, spectrum):
    bins = table.shape[0] // 2
    fft_length = 2 * (bins - 1)
    row = lax.broadcasted_iota(jnp.int32, (2 * bins, 1), 0)
    edge = (row == 0) | (row == bins - 1) | (row == bins) | (row == 2 * bins - 1)
    weight = jnp.where(edge, 1.0 / fft_length, 2.0 / fft_length)
    scaled = spectrum * weight
    spec_high = scaled.astype(jnp.bfloat16)
    spec_low = (scaled - spec_high.astype(jnp.float32)).astype(jnp.bfloat16)
    backward = ((0,), (0,))
    return bf16_dot(table, spec_high, backward) + bf16_dot(table, spec_low, backward)


def split(spectrum):
    bins = spectrum.shape[0] // 2
    return spectrum[:bins], spectrum[bins:]


def join(real, imag):
    return jnp.concatenate([real, imag], axis=0)


def block_core(feats, cot, resp, taps, skip_gain):
    length = feats.shape[0]
    narrow = feats.shape[2]
    tables = dft_tables(length)
    extended = jnp.concatenate([jnp.zeros((2, 3, narrow), feats.dtype), feats], axis=0)
    mixed = taps[0] * extended[2:] + taps[1] * extended[1:-1] + taps[2] * extended[:-2]
    query_feat = mixed[:, 0]
    key_feat = mixed[:, 1]
    value_feat = mixed[:, 2]
    product = (key_feat * value_feat).astype(jnp.bfloat16)
    first = to_spectrum(tables, jnp.concatenate([product, resp], axis=1))
    prod_re, prod_im = split(first[:, :narrow])
    resp_re, resp_im = split(first[:, narrow:])
    conv_out = to_signal(
        tables, join(prod_re * resp_re - prod_im * resp_im, prod_re * resp_im + prod_im * resp_re)
    )
    carried = conv_out + skip_gain * product
    gated = (query_feat * carried).astype(jnp.bfloat16)
    grad_carried = (cot * query_feat).astype(jnp.bfloat16)
    grad_query = cot * carried
    grad_re, grad_im = split(to_spectrum(tables, grad_carried))
    back_spec = join(grad_re * resp_re + grad_im * resp_im, grad_im * resp_re - grad_re * resp_im)
    filt_spec = join(grad_re * prod_re + grad_im * prod_im, grad_im * prod_re - grad_re * prod_im)
    both = to_signal(tables, jnp.concatenate([back_spec, filt_spec], axis=1))
    grad_product = both[:, :narrow] + skip_gain * grad_carried
    grad_mixed = jnp.stack([grad_query, grad_product * value_feat, grad_product * key_feat], axis=1)
    tail = jnp.concatenate([grad_mixed, jnp.zeros((2, 3, narrow), jnp.float32)], axis=0)
    grad_feats = (
        taps[0] * tail[:length] + taps[1] * tail[1 : length + 1] + taps[2] * tail[2:]
    ).astype(jnp.bfloat16)
    grad_taps = jnp.stack(
        [
            jnp.sum(grad_mixed * extended[2 - tap_index : 2 - tap_index + length], axis=0)
            for tap_index in range(3)
        ]
    )
    grad_skip = jnp.sum(grad_carried.astype(jnp.float32) * product.astype(jnp.float32), axis=0)
    return gated, grad_feats, grad_taps, grad_skip, both[:, narrow:]


def blocked_fallback(moved_in, taps, skip_gain, seq_parts, tok_rows, narrow):
    length = seq_parts * tok_rows
    fft_length = 2 * length
    local_feats = moved_in[None, :, :3]
    extended = jnp.concatenate(
        [jnp.zeros((1, 2, 3, narrow), local_feats.dtype), local_feats], axis=1
    )

    def local_spectrum(signal):
        blocks = signal.reshape(signal.shape[0], seq_parts, tok_rows, narrow).astype(jnp.float32)
        part_real, part_imag = across_blocks(
            blocks, jnp.arange(tok_rows, dtype=jnp.int32), seq_parts, fft_length
        )
        return within_blocks(part_real, part_imag)

    def local_signal(spectrum):
        part_real, part_imag = back_within(
            spectrum[0], spectrum[1], jnp.arange(2 * seq_parts, dtype=jnp.int32), fft_length
        )
        values = back_across(part_real, part_imag, seq_parts, fft_length)
        return values.reshape(values.shape[0], length, narrow)

    def no_rows(rows_part):
        return jnp.zeros_like(rows_part)

    return blocked_core(
        extended,
        moved_in[None, :, 3],
        taps,
        skip_gain,
        moved_in[:, 4],
        local_spectrum,
        local_signal,
        no_rows,
    )


def gather_tiles(features2d, cot2d, resp2d, seq_parts, narrow):
    rows = features2d.shape[0]
    width = seq_parts * narrow

    def body(f_ref, c_ref, r_ref, out_ref):
        group = pl.program_id(0)

        def spread(src_ref):
            for dest in range(seq_parts):
                out_ref[dest, 0] = src_ref[:, dest * narrow : (dest + 1) * narrow]

        @pl.when(group < 3)
        def _():
            spread(f_ref)

        @pl.when(group == 3)
        def _():
            spread(c_ref)

        @pl.when(group == 4)
        def _():
            spread(r_ref)

    return pl.pallas_call(
        body,
        grid=(5,),
        in_specs=[
            pl.BlockSpec((rows, width), lambda g: (0, jnp.minimum(g, 2))),
            pl.BlockSpec((rows, width), lambda g: (0, 0)),
            pl.BlockSpec((rows, width), lambda g: (0, 0)),
        ],
        out_specs=pl.BlockSpec((seq_parts, 1, rows, narrow), lambda g: (0, g, 0, 0)),
        out_shape=jax.ShapeDtypeStruct((seq_parts, 5, rows, narrow), features2d.dtype),
    )(features2d, cot2d, resp2d)


def scatter_tiles(moved, seq_parts, narrow):
    rows = moved.shape[2]

    def body(in_ref, gated_ref, feats_ref):
        group = pl.program_id(0)

        @pl.when(group == 0)
        def _():
            for source in range(seq_parts):
                gated_ref[:, source * narrow : (source + 1) * narrow] = in_ref[source, 0]

        @pl.when(group > 0)
        def _():
            for source in range(seq_parts):
                feats_ref[:, source * narrow : (source + 1) * narrow] = in_ref[source, 0]

    width = seq_parts * narrow
    return pl.pallas_call(
        body,
        grid=(4,),
        in_specs=[pl.BlockSpec((seq_parts, 1, rows, narrow), lambda g: (0, g, 0, 0))],
        out_specs=[
            pl.BlockSpec((rows, width), lambda g: (0, 0)),
            pl.BlockSpec((rows, width), lambda g: (0, jnp.maximum(g - 1, 0))),
        ],
        out_shape=[
            jax.ShapeDtypeStruct((rows, width), moved.dtype),
            jax.ShapeDtypeStruct((rows, 3 * width), moved.dtype),
        ],
    )(moved)


def local(features, short_filter, response, skip_gain, cotangent):
    seq_parts = lax.axis_size("seq")
    dp_parts = lax.axis_size("dp")
    seq_index = lax.axis_index("seq")
    tok_rows = features.shape[1]
    chan_width = features.shape[2] // 3
    length = seq_parts * tok_rows
    narrow = chan_width // seq_parts
    offset = seq_index * narrow
    taps = short_filter.reshape(3, 3, chan_width)
    if narrow % 128 == 0 and tok_rows % 16 == 0:
        arranged = gather_tiles(
            features.reshape(tok_rows, 3 * chan_width),
            cotangent.reshape(tok_rows, chan_width),
            response,
            seq_parts,
            narrow,
        )
        moved_in = (
            lax.all_to_all(arranged, "seq", 0, 0, tiled=True)
            .transpose(0, 2, 1, 3)
            .reshape(length, 5, narrow)
        )
    else:
        joined_in = jnp.concatenate(
            [
                features.reshape(tok_rows, 3 * chan_width),
                cotangent.reshape(tok_rows, chan_width),
                response,
            ],
            axis=1,
        )
        arranged = joined_in.reshape(tok_rows, 5, seq_parts, narrow).transpose(2, 0, 1, 3)
        moved_in = lax.all_to_all(arranged, "seq", 0, 0, tiled=True).reshape(length, 5, narrow)
    local_taps = lax.dynamic_slice_in_dim(taps, offset, narrow, 2)
    local_skip = lax.dynamic_slice_in_dim(skip_gain, offset, narrow, 0)
    if length <= 2048:
        gated, grad_feats, grad_taps, grad_skip, filter_part = block_core(
            moved_in[:, :3], moved_in[:, 3], moved_in[:, 4], local_taps, local_skip
        )
    else:
        gated, grad_feats, grad_taps, grad_skip, filter_part = blocked_fallback(
            moved_in, local_taps, local_skip, seq_parts, tok_rows, narrow
        )
        gated = gated.reshape(length, narrow)
        grad_feats = grad_feats.reshape(length, 3, narrow)
    if narrow % 128 == 0 and tok_rows % 16 == 0:
        joined_out = jnp.concatenate(
            [
                gated.reshape(seq_parts, 1, tok_rows, narrow),
                grad_feats.reshape(seq_parts, tok_rows, 3, narrow).transpose(0, 2, 1, 3),
            ],
            axis=1,
        )
        moved_out = lax.all_to_all(joined_out, "seq", 0, 0, tiled=True)
        gated, grad_feats = scatter_tiles(moved_out, seq_parts, narrow)
    else:
        joined_out = jnp.concatenate(
            [gated.reshape(seq_parts, tok_rows, 1, narrow), grad_feats.reshape(seq_parts, tok_rows, 3, narrow)],
            axis=2,
        )
        moved_out = lax.all_to_all(joined_out, "seq", 0, 0, tiled=True).transpose(1, 2, 0, 3)
        gated = moved_out[:, 0]
        grad_feats = moved_out[:, 1:]
    extra = 16
    small = jnp.concatenate(
        [grad_taps.reshape(9, narrow), grad_skip[None], jnp.zeros((extra - 10, narrow), jnp.float32)],
        axis=0,
    )
    chunks = jnp.concatenate(
        [
            filter_part.reshape(seq_parts, tok_rows, narrow),
            jnp.broadcast_to(small[None], (seq_parts, extra, narrow)),
        ],
        axis=1,
    )
    moved = lax.all_to_all(chunks, "seq", 0, 0, tiled=True)
    pair = seq_parts // dp_parts
    small_all = moved[:, tok_rows : tok_rows + 10]
    small_rows = (
        small_all.reshape(dp_parts, pair, 10, narrow)
        .transpose(1, 0, 2, 3)
        .reshape(pair, dp_parts * 10, narrow)
    )
    joined = jnp.concatenate(
        [moved[:, :tok_rows], jnp.tile(small_rows, (dp_parts, 1, 1))], axis=1
    )
    reduced = lax.psum_scatter(joined, "dp", scatter_dimension=0, tiled=True)
    filter_total = reduced[:, :tok_rows].transpose(1, 0, 2).reshape(tok_rows, pair * narrow)
    small_total = (
        reduced[:, tok_rows:]
        .reshape(pair, dp_parts, 10, narrow)
        .transpose(2, 1, 0, 3)
        .reshape(10, chan_width)
    )
    gated = gated.reshape(1, tok_rows, chan_width)
    grad_feats = grad_feats.reshape(1, tok_rows, 3 * chan_width)
    return (
        gated,
        grad_feats,
        small_total[:9].reshape(3, 3 * chan_width),
        small_total[9],
        filter_total,
    )


def solution(mesh):
    placed = (P("dp", "seq", None), P(), P("seq", None), P(), P("dp", "seq", None))
    return jax.shard_map(
        local,
        mesh=mesh,
        in_specs=placed,
        out_specs=(P("dp", "seq", None), P("dp", "seq", None), P(), P(), P("seq", "dp")),
        check_vma=False,
    )
```

```python
import math

import jax
import jax.numpy as jnp
from jax import lax
from jax.experimental import pallas as pl
from jax.sharding import PartitionSpec as P


precise = lax.Precision.HIGHEST


def dft_table(count):
    series = jnp.arange(count, dtype=jnp.int32)
    angle = (series[:, None] * series[None, :] % count).astype(jnp.float32) * (
        2.0 * math.pi / count
    )
    return (jnp.cos(angle), jnp.sin(angle))


def across_blocks(signal, offsets, blocks, fft_length):
    double = jnp.arange(2 * blocks, dtype=jnp.int32)
    single = jnp.arange(blocks, dtype=jnp.int32)
    angle = (double[:, None] * single[None, :] % (2 * blocks)).astype(jnp.float32) * (
        math.pi / blocks
    )
    table = jnp.stack([jnp.cos(angle), -jnp.sin(angle)])
    first = jnp.einsum("oap,bpjk->obajk", table, signal, precision=precise)
    twist = (double[:, None] * offsets[None, :] % fft_length).astype(jnp.float32) * (
        -2.0 * math.pi / fft_length
    )
    cosine = jnp.cos(twist)[None, :, :, None]
    sine = jnp.sin(twist)[None, :, :, None]
    return (first[0] * cosine - first[1] * sine, first[0] * sine + first[1] * cosine)


def within_blocks(part_real, part_imag):
    table_cos, table_sin = dft_table(part_real.shape[2])
    table = jnp.stack([jnp.stack([table_cos, table_sin]), jnp.stack([-table_sin, table_cos])])
    spectra = jnp.einsum(
        "oibj,ixajk->oxabk", table, jnp.stack([part_real, part_imag]), precision=precise
    )
    return (spectra[0], spectra[1])


def back_within(spec_real, spec_imag, firsts, fft_length):
    count = spec_real.shape[2]
    table_cos, table_sin = dft_table(count)
    table = jnp.stack([jnp.stack([table_cos, -table_sin]), jnp.stack([table_sin, table_cos])])
    backs = jnp.einsum(
        "oibj,ixabk->oxajk", table, jnp.stack([spec_real, spec_imag]), precision=precise
    )
    series = jnp.arange(count, dtype=jnp.int32)
    twist = (firsts[:, None] * series[None, :] % fft_length).astype(jnp.float32) * (
        2.0 * math.pi / fft_length
    )
    cosine = jnp.cos(twist)[None, :, :, None]
    sine = jnp.sin(twist)[None, :, :, None]
    return (backs[0] * cosine - backs[1] * sine, backs[0] * sine + backs[1] * cosine)


def back_across(part_real, part_imag, blocks, fft_length):
    double = jnp.arange(2 * blocks, dtype=jnp.int32)
    single = jnp.arange(blocks, dtype=jnp.int32)
    angle = (single[:, None] * double[None, :] % (2 * blocks)).astype(jnp.float32) * (
        math.pi / blocks
    )
    table = jnp.stack([jnp.cos(angle), -jnp.sin(angle)])
    result = jnp.einsum(
        "ipa,ibajk->bpjk", table, jnp.stack([part_real, part_imag]), precision=precise
    )
    return result * (1.0 / fft_length)


def times_spectrum(left, right):
    return (left[0] * right[0] - left[1] * right[1], left[0] * right[1] + left[1] * right[0])


def times_conjugate(left, right):
    return (left[0] * right[0] + left[1] * right[1], left[1] * right[0] - left[0] * right[1])


def blocked_core(extended, cotangent, taps, skip_gain, response, to_spectrum, to_signal, after_rows):
    count = cotangent.shape[1]
    batch = cotangent.shape[0]
    mixed = taps[0] * extended[:, 2:] + taps[1] * extended[:, 1:-1] + taps[2] * extended[:, :-2]
    query_feat = mixed[:, :, 0]
    key_feat = mixed[:, :, 1]
    value_feat = mixed[:, :, 2]
    product = (key_feat * value_feat).astype(jnp.bfloat16)
    stacked = to_spectrum(jnp.concatenate([product, response[None]], axis=0))
    prod_spec = (stacked[0][:batch], stacked[1][:batch])
    resp_spec = (stacked[0][batch:], stacked[1][batch:])
    conv_out = to_signal(times_spectrum(prod_spec, resp_spec))
    carried = conv_out + skip_gain * product
    gated = (query_feat * carried).astype(jnp.bfloat16)
    grad_carried = (cotangent * query_feat).astype(jnp.bfloat16)
    grad_query = cotangent * carried
    grad_spec = to_spectrum(grad_carried)
    back_conv = times_conjugate(grad_spec, resp_spec)
    resp_grad = times_conjugate(grad_spec, prod_spec)
    joined_real = jnp.concatenate(
        [back_conv[0], jnp.sum(resp_grad[0], axis=0, keepdims=True)], axis=0
    )
    joined_imag = jnp.concatenate(
        [back_conv[1], jnp.sum(resp_grad[1], axis=0, keepdims=True)], axis=0
    )
    both = to_signal((joined_real, joined_imag))
    grad_product = both[:batch] + skip_gain * grad_carried
    grad_mixed = jnp.stack([grad_query, grad_product * value_feat, grad_product * key_feat], axis=2)
    tail = jnp.concatenate([grad_mixed, after_rows(grad_mixed[:, :2])], axis=1)
    grad_feats = (
        taps[0] * tail[:, :count] + taps[1] * tail[:, 1 : count + 1] + taps[2] * tail[:, 2:]
    ).astype(jnp.bfloat16)
    grad_taps = jnp.stack(
        [
            jnp.sum(grad_mixed * extended[:, 2 - tap_index : 2 - tap_index + count], axis=(0, 1))
            for tap_index in range(3)
        ]
    )
    grad_skip = jnp.sum(grad_carried.astype(jnp.float32) * product.astype(jnp.float32), axis=(0, 1))
    return (gated, grad_feats, grad_taps, grad_skip, both[batch])


def dft_tables(length):
    fft_length = 2 * length
    bins = length + 1
    freq = lax.broadcasted_iota(jnp.int32, (bins, length), 0)
    time = lax.broadcasted_iota(jnp.int32, (bins, length), 1)
    angle = lax.optimization_barrier((freq * time) % fft_length).astype(jnp.float32) * (
        2.0 * math.pi / fft_length
    )
    table = jnp.concatenate([jnp.cos(angle), -jnp.sin(angle)], axis=0)
    return table.astype(jnp.bfloat16)


def bf16_dot(left, right, dims):
    return lax.dot_general(left, right, (dims, ((), ())), preferred_element_type=jnp.float32)


def to_spectrum(table, signal):
    return bf16_dot(table, signal, ((1,), (0,)))


def to_signal(table, spectrum):
    bins = table.shape[0] // 2
    fft_length = 2 * (bins - 1)
    row = lax.broadcasted_iota(jnp.int32, (2 * bins, 1), 0)
    edge = (row == 0) | (row == bins - 1) | (row == bins) | (row == 2 * bins - 1)
    weight = jnp.where(edge, 1.0 / fft_length, 2.0 / fft_length)
    scaled = (spectrum * weight).astype(jnp.bfloat16)
    return bf16_dot(table, scaled, ((0,), (0,)))


def split(spectrum):
    bins = spectrum.shape[0] // 2
    return spectrum[:bins], spectrum[bins:]


def join(real, imag):
    return jnp.concatenate([real, imag], axis=0)


def block_core(feats, cot, resp, taps, skip_gain):
    length = feats.shape[0]
    narrow = feats.shape[2]
    tables = dft_tables(length)
    extended = jnp.concatenate([jnp.zeros((2, 3, narrow), feats.dtype), feats], axis=0)
    mixed = taps[0] * extended[2:] + taps[1] * extended[1:-1] + taps[2] * extended[:-2]
    query_feat = mixed[:, 0]
    key_feat = mixed[:, 1]
    value_feat = mixed[:, 2]
    product = (key_feat * value_feat).astype(jnp.bfloat16)
    first = to_spectrum(tables, jnp.concatenate([product, resp], axis=1))
    prod_re, prod_im = split(first[:, :narrow])
    resp_re, resp_im = split(first[:, narrow:])
    conv_out = to_signal(
        tables, join(prod_re * resp_re - prod_im * resp_im, prod_re * resp_im + prod_im * resp_re)
    )
    carried = conv_out + skip_gain * product
    gated = (query_feat * carried).astype(jnp.bfloat16)
    grad_carried = (cot * query_feat).astype(jnp.bfloat16)
    grad_query = cot * carried
    grad_re, grad_im = split(to_spectrum(tables, grad_carried))
    back_spec = join(grad_re * resp_re + grad_im * resp_im, grad_im * resp_re - grad_re * resp_im)
    filt_spec = join(grad_re * prod_re + grad_im * prod_im, grad_im * prod_re - grad_re * prod_im)
    both = to_signal(tables, jnp.concatenate([back_spec, filt_spec], axis=1))
    grad_product = both[:, :narrow] + skip_gain * grad_carried
    grad_mixed = jnp.stack([grad_query, grad_product * value_feat, grad_product * key_feat], axis=1)
    tail = jnp.concatenate([grad_mixed, jnp.zeros((2, 3, narrow), jnp.float32)], axis=0)
    grad_feats = (
        taps[0] * tail[:length] + taps[1] * tail[1 : length + 1] + taps[2] * tail[2:]
    ).astype(jnp.bfloat16)
    grad_taps = jnp.stack(
        [
            jnp.sum(grad_mixed * extended[2 - tap_index : 2 - tap_index + length], axis=0)
            for tap_index in range(3)
        ]
    )
    grad_skip = jnp.sum(grad_carried.astype(jnp.float32) * product.astype(jnp.float32), axis=0)
    return gated, grad_feats, grad_taps, grad_skip, both[:, narrow:]


def blocked_fallback(moved_in, taps, skip_gain, seq_parts, tok_rows, narrow):
    length = seq_parts * tok_rows
    fft_length = 2 * length
    local_feats = moved_in[None, :, :3]
    extended = jnp.concatenate(
        [jnp.zeros((1, 2, 3, narrow), local_feats.dtype), local_feats], axis=1
    )

    def local_spectrum(signal):
        blocks = signal.reshape(signal.shape[0], seq_parts, tok_rows, narrow).astype(jnp.float32)
        part_real, part_imag = across_blocks(
            blocks, jnp.arange(tok_rows, dtype=jnp.int32), seq_parts, fft_length
        )
        return within_blocks(part_real, part_imag)

    def local_signal(spectrum):
        part_real, part_imag = back_within(
            spectrum[0], spectrum[1], jnp.arange(2 * seq_parts, dtype=jnp.int32), fft_length
        )
        values = back_across(part_real, part_imag, seq_parts, fft_length)
        return values.reshape(values.shape[0], length, narrow)

    def no_rows(rows_part):
        return jnp.zeros_like(rows_part)

    return blocked_core(
        extended,
        moved_in[None, :, 3],
        taps,
        skip_gain,
        moved_in[:, 4],
        local_spectrum,
        local_signal,
        no_rows,
    )


def gather_tiles(features2d, cot2d, resp2d, seq_parts, narrow):
    rows = features2d.shape[0]
    width = seq_parts * narrow

    def body(f_ref, c_ref, r_ref, out_ref):
        group = pl.program_id(0)

        def spread(src_ref):
            for dest in range(seq_parts):
                out_ref[dest, 0] = src_ref[:, dest * narrow : (dest + 1) * narrow]

        @pl.when(group < 3)
        def _():
            spread(f_ref)

        @pl.when(group == 3)
        def _():
            spread(c_ref)

        @pl.when(group == 4)
        def _():
            spread(r_ref)

    return pl.pallas_call(
        body,
        grid=(5,),
        in_specs=[
            pl.BlockSpec((rows, width), lambda g: (0, jnp.minimum(g, 2))),
            pl.BlockSpec((rows, width), lambda g: (0, 0)),
            pl.BlockSpec((rows, width), lambda g: (0, 0)),
        ],
        out_specs=pl.BlockSpec((seq_parts, 1, rows, narrow), lambda g: (0, g, 0, 0)),
        out_shape=jax.ShapeDtypeStruct((seq_parts, 5, rows, narrow), features2d.dtype),
    )(features2d, cot2d, resp2d)


def scatter_tiles(moved, seq_parts, narrow):
    rows = moved.shape[2]

    def body(in_ref, gated_ref, feats_ref):
        group = pl.program_id(0)

        @pl.when(group == 0)
        def _():
            for source in range(seq_parts):
                gated_ref[:, source * narrow : (source + 1) * narrow] = in_ref[source, 0]

        @pl.when(group > 0)
        def _():
            for source in range(seq_parts):
                feats_ref[:, source * narrow : (source + 1) * narrow] = in_ref[source, 0]

    width = seq_parts * narrow
    return pl.pallas_call(
        body,
        grid=(4,),
        in_specs=[pl.BlockSpec((seq_parts, 1, rows, narrow), lambda g: (0, g, 0, 0))],
        out_specs=[
            pl.BlockSpec((rows, width), lambda g: (0, 0)),
            pl.BlockSpec((rows, width), lambda g: (0, jnp.maximum(g - 1, 0))),
        ],
        out_shape=[
            jax.ShapeDtypeStruct((rows, width), moved.dtype),
            jax.ShapeDtypeStruct((rows, 3 * width), moved.dtype),
        ],
    )(moved)


def local(features, short_filter, response, skip_gain, cotangent):
    seq_parts = lax.axis_size("seq")
    dp_parts = lax.axis_size("dp")
    seq_index = lax.axis_index("seq")
    tok_rows = features.shape[1]
    chan_width = features.shape[2] // 3
    length = seq_parts * tok_rows
    narrow = chan_width // seq_parts
    offset = seq_index * narrow
    taps = short_filter.reshape(3, 3, chan_width)
    if narrow % 128 == 0 and tok_rows % 16 == 0:
        arranged = gather_tiles(
            features.reshape(tok_rows, 3 * chan_width),
            cotangent.reshape(tok_rows, chan_width),
            response,
            seq_parts,
            narrow,
        )
        moved_in = (
            lax.all_to_all(arranged, "seq", 0, 0, tiled=True)
            .transpose(0, 2, 1, 3)
            .reshape(length, 5, narrow)
        )
    else:
        joined_in = jnp.concatenate(
            [
                features.reshape(tok_rows, 3 * chan_width),
                cotangent.reshape(tok_rows, chan_width),
                response,
            ],
            axis=1,
        )
        arranged = joined_in.reshape(tok_rows, 5, seq_parts, narrow).transpose(2, 0, 1, 3)
        moved_in = lax.all_to_all(arranged, "seq", 0, 0, tiled=True).reshape(length, 5, narrow)
    local_taps = lax.dynamic_slice_in_dim(taps, offset, narrow, 2)
    local_skip = lax.dynamic_slice_in_dim(skip_gain, offset, narrow, 0)
    if length <= 2048:
        gated, grad_feats, grad_taps, grad_skip, filter_part = block_core(
            moved_in[:, :3], moved_in[:, 3], moved_in[:, 4], local_taps, local_skip
        )
    else:
        gated, grad_feats, grad_taps, grad_skip, filter_part = blocked_fallback(
            moved_in, local_taps, local_skip, seq_parts, tok_rows, narrow
        )
        gated = gated.reshape(length, narrow)
        grad_feats = grad_feats.reshape(length, 3, narrow)
    if narrow % 128 == 0 and tok_rows % 16 == 0:
        joined_out = jnp.concatenate(
            [
                gated.reshape(seq_parts, 1, tok_rows, narrow),
                grad_feats.reshape(seq_parts, tok_rows, 3, narrow).transpose(0, 2, 1, 3),
            ],
            axis=1,
        )
        moved_out = lax.all_to_all(joined_out, "seq", 0, 0, tiled=True)
        gated, grad_feats = scatter_tiles(moved_out, seq_parts, narrow)
    else:
        joined_out = jnp.concatenate(
            [gated.reshape(seq_parts, tok_rows, 1, narrow), grad_feats.reshape(seq_parts, tok_rows, 3, narrow)],
            axis=2,
        )
        moved_out = lax.all_to_all(joined_out, "seq", 0, 0, tiled=True).transpose(1, 2, 0, 3)
        gated = moved_out[:, 0]
        grad_feats = moved_out[:, 1:]
    extra = 16
    small = jnp.concatenate(
        [grad_taps.reshape(9, narrow), grad_skip[None], jnp.zeros((extra - 10, narrow), jnp.float32)],
        axis=0,
    )
    chunks = jnp.concatenate(
        [
            filter_part.reshape(seq_parts, tok_rows, narrow),
            jnp.broadcast_to(small[None], (seq_parts, extra, narrow)),
        ],
        axis=1,
    )
    moved = lax.all_to_all(chunks, "seq", 0, 0, tiled=True)
    pair = seq_parts // dp_parts
    small_all = moved[:, tok_rows : tok_rows + 10]
    small_rows = (
        small_all.reshape(dp_parts, pair, 10, narrow)
        .transpose(1, 0, 2, 3)
        .reshape(pair, dp_parts * 10, narrow)
    )
    joined = jnp.concatenate(
        [moved[:, :tok_rows], jnp.tile(small_rows, (dp_parts, 1, 1))], axis=1
    )
    reduced = lax.psum_scatter(joined, "dp", scatter_dimension=0, tiled=True)
    filter_total = reduced[:, :tok_rows].transpose(1, 0, 2).reshape(tok_rows, pair * narrow)
    small_total = (
        reduced[:, tok_rows:]
        .reshape(pair, dp_parts, 10, narrow)
        .transpose(2, 1, 0, 3)
        .reshape(10, chan_width)
    )
    gated = gated.reshape(1, tok_rows, chan_width)
    grad_feats = grad_feats.reshape(1, tok_rows, 3 * chan_width)
    return (
        gated,
        grad_feats,
        small_total[:9].reshape(3, 3 * chan_width),
        small_total[9],
        filter_total,
    )


def solution(mesh):
    placed = (P("dp", "seq", None), P(), P("seq", None), P(), P("dp", "seq", None))
    return jax.shard_map(
        local,
        mesh=mesh,
        in_specs=placed,
        out_specs=(P("dp", "seq", None), P("dp", "seq", None), P(), P(), P("seq", "dp")),
        check_vma=False,
    )
```

```python
import math

import jax
import jax.numpy as jnp
from jax import lax
from jax.experimental import pallas as pl
from jax.sharding import PartitionSpec as P


precise = lax.Precision.HIGHEST


def dft_table(count):
    series = jnp.arange(count, dtype=jnp.int32)
    angle = (series[:, None] * series[None, :] % count).astype(jnp.float32) * (
        2.0 * math.pi / count
    )
    return (jnp.cos(angle), jnp.sin(angle))


def across_blocks(signal, offsets, blocks, fft_length):
    double = jnp.arange(2 * blocks, dtype=jnp.int32)
    single = jnp.arange(blocks, dtype=jnp.int32)
    angle = (double[:, None] * single[None, :] % (2 * blocks)).astype(jnp.float32) * (
        math.pi / blocks
    )
    table = jnp.stack([jnp.cos(angle), -jnp.sin(angle)])
    first = jnp.einsum("oap,bpjk->obajk", table, signal, precision=precise)
    twist = (double[:, None] * offsets[None, :] % fft_length).astype(jnp.float32) * (
        -2.0 * math.pi / fft_length
    )
    cosine = jnp.cos(twist)[None, :, :, None]
    sine = jnp.sin(twist)[None, :, :, None]
    return (first[0] * cosine - first[1] * sine, first[0] * sine + first[1] * cosine)


def within_blocks(part_real, part_imag):
    table_cos, table_sin = dft_table(part_real.shape[2])
    table = jnp.stack([jnp.stack([table_cos, table_sin]), jnp.stack([-table_sin, table_cos])])
    spectra = jnp.einsum(
        "oibj,ixajk->oxabk", table, jnp.stack([part_real, part_imag]), precision=precise
    )
    return (spectra[0], spectra[1])


def back_within(spec_real, spec_imag, firsts, fft_length):
    count = spec_real.shape[2]
    table_cos, table_sin = dft_table(count)
    table = jnp.stack([jnp.stack([table_cos, -table_sin]), jnp.stack([table_sin, table_cos])])
    backs = jnp.einsum(
        "oibj,ixabk->oxajk", table, jnp.stack([spec_real, spec_imag]), precision=precise
    )
    series = jnp.arange(count, dtype=jnp.int32)
    twist = (firsts[:, None] * series[None, :] % fft_length).astype(jnp.float32) * (
        2.0 * math.pi / fft_length
    )
    cosine = jnp.cos(twist)[None, :, :, None]
    sine = jnp.sin(twist)[None, :, :, None]
    return (backs[0] * cosine - backs[1] * sine, backs[0] * sine + backs[1] * cosine)


def back_across(part_real, part_imag, blocks, fft_length):
    double = jnp.arange(2 * blocks, dtype=jnp.int32)
    single = jnp.arange(blocks, dtype=jnp.int32)
    angle = (single[:, None] * double[None, :] % (2 * blocks)).astype(jnp.float32) * (
        math.pi / blocks
    )
    table = jnp.stack([jnp.cos(angle), -jnp.sin(angle)])
    result = jnp.einsum(
        "ipa,ibajk->bpjk", table, jnp.stack([part_real, part_imag]), precision=precise
    )
    return result * (1.0 / fft_length)


def times_spectrum(left, right):
    return (left[0] * right[0] - left[1] * right[1], left[0] * right[1] + left[1] * right[0])


def times_conjugate(left, right):
    return (left[0] * right[0] + left[1] * right[1], left[1] * right[0] - left[0] * right[1])


def blocked_core(extended, cotangent, taps, skip_gain, response, to_spectrum, to_signal, after_rows):
    count = cotangent.shape[1]
    batch = cotangent.shape[0]
    mixed = taps[0] * extended[:, 2:] + taps[1] * extended[:, 1:-1] + taps[2] * extended[:, :-2]
    query_feat = mixed[:, :, 0]
    key_feat = mixed[:, :, 1]
    value_feat = mixed[:, :, 2]
    product = (key_feat * value_feat).astype(jnp.bfloat16)
    stacked = to_spectrum(jnp.concatenate([product, response[None]], axis=0))
    prod_spec = (stacked[0][:batch], stacked[1][:batch])
    resp_spec = (stacked[0][batch:], stacked[1][batch:])
    conv_out = to_signal(times_spectrum(prod_spec, resp_spec))
    carried = conv_out + skip_gain * product
    gated = (query_feat * carried).astype(jnp.bfloat16)
    grad_carried = (cotangent * query_feat).astype(jnp.bfloat16)
    grad_query = cotangent * carried
    grad_spec = to_spectrum(grad_carried)
    back_conv = times_conjugate(grad_spec, resp_spec)
    resp_grad = times_conjugate(grad_spec, prod_spec)
    joined_real = jnp.concatenate(
        [back_conv[0], jnp.sum(resp_grad[0], axis=0, keepdims=True)], axis=0
    )
    joined_imag = jnp.concatenate(
        [back_conv[1], jnp.sum(resp_grad[1], axis=0, keepdims=True)], axis=0
    )
    both = to_signal((joined_real, joined_imag))
    grad_product = both[:batch] + skip_gain * grad_carried
    grad_mixed = jnp.stack([grad_query, grad_product * value_feat, grad_product * key_feat], axis=2)
    tail = jnp.concatenate([grad_mixed, after_rows(grad_mixed[:, :2])], axis=1)
    grad_feats = (
        taps[0] * tail[:, :count] + taps[1] * tail[:, 1 : count + 1] + taps[2] * tail[:, 2:]
    ).astype(jnp.bfloat16)
    grad_taps = jnp.stack(
        [
            jnp.sum(grad_mixed * extended[:, 2 - tap_index : 2 - tap_index + count], axis=(0, 1))
            for tap_index in range(3)
        ]
    )
    grad_skip = jnp.sum(grad_carried.astype(jnp.float32) * product.astype(jnp.float32), axis=(0, 1))
    return (gated, grad_feats, grad_taps, grad_skip, both[batch])


def dft_tables(length):
    fft_length = 2 * length
    bins = length + 1
    freq = lax.broadcasted_iota(jnp.int32, (bins, length), 0)
    time = lax.broadcasted_iota(jnp.int32, (bins, length), 1)
    angle = lax.optimization_barrier((freq * time) % fft_length).astype(jnp.float32) * (
        2.0 * math.pi / fft_length
    )
    table = jnp.concatenate([jnp.cos(angle), -jnp.sin(angle)], axis=0)
    return table.astype(jnp.bfloat16)


def bf16_dot(left, right, dims):
    return lax.dot_general(left, right, (dims, ((), ())), preferred_element_type=jnp.float32)


def to_spectrum(table, signal):
    return bf16_dot(table, signal, ((1,), (0,)))


def to_signal(table, spectrum):
    bins = table.shape[0] // 2
    fft_length = 2 * (bins - 1)
    row = lax.broadcasted_iota(jnp.int32, (2 * bins, 1), 0)
    edge = (row == 0) | (row == bins - 1) | (row == bins) | (row == 2 * bins - 1)
    weight = jnp.where(edge, 1.0 / fft_length, 2.0 / fft_length)
    scaled = (spectrum * weight).astype(jnp.bfloat16)
    return bf16_dot(table, scaled, ((0,), (0,)))


def split(spectrum):
    bins = spectrum.shape[0] // 2
    return spectrum[:bins], spectrum[bins:]


def join(real, imag):
    return jnp.concatenate([real, imag], axis=0)


def block_core(feats, cot, resp, taps, skip_gain):
    length = feats.shape[0]
    narrow = feats.shape[2]
    tables = dft_tables(length)
    extended = jnp.concatenate([jnp.zeros((2, 3, narrow), feats.dtype), feats], axis=0)
    mixed = taps[0] * extended[2:] + taps[1] * extended[1:-1] + taps[2] * extended[:-2]
    query_feat = mixed[:, 0]
    key_feat = mixed[:, 1]
    value_feat = mixed[:, 2]
    product = (key_feat * value_feat).astype(jnp.bfloat16)
    prod_re, prod_im = split(to_spectrum(tables, product))
    resp_re, resp_im = split(to_spectrum(tables, resp))
    conv_out = to_signal(
        tables, join(prod_re * resp_re - prod_im * resp_im, prod_re * resp_im + prod_im * resp_re)
    )
    carried = conv_out + skip_gain * product
    gated = (query_feat * carried).astype(jnp.bfloat16)
    grad_carried = (cot * query_feat).astype(jnp.bfloat16)
    grad_query = cot * carried
    grad_re, grad_im = split(to_spectrum(tables, grad_carried))
    back_spec = join(grad_re * resp_re + grad_im * resp_im, grad_im * resp_re - grad_re * resp_im)
    filt_spec = join(grad_re * prod_re + grad_im * prod_im, grad_im * prod_re - grad_re * prod_im)
    both = to_signal(tables, jnp.concatenate([back_spec, filt_spec], axis=1))
    grad_product = both[:, :narrow] + skip_gain * grad_carried
    grad_mixed = jnp.stack([grad_query, grad_product * value_feat, grad_product * key_feat], axis=1)
    tail = jnp.concatenate([grad_mixed, jnp.zeros((2, 3, narrow), jnp.float32)], axis=0)
    grad_feats = (
        taps[0] * tail[:length] + taps[1] * tail[1 : length + 1] + taps[2] * tail[2:]
    ).astype(jnp.bfloat16)
    grad_taps = jnp.stack(
        [
            jnp.sum(grad_mixed * extended[2 - tap_index : 2 - tap_index + length], axis=0)
            for tap_index in range(3)
        ]
    )
    grad_skip = jnp.sum(grad_carried.astype(jnp.float32) * product.astype(jnp.float32), axis=0)
    return gated, grad_feats, grad_taps, grad_skip, both[:, narrow:]


def blocked_fallback(moved_in, taps, skip_gain, seq_parts, tok_rows, narrow):
    length = seq_parts * tok_rows
    fft_length = 2 * length
    local_feats = moved_in[None, :, :3]
    extended = jnp.concatenate(
        [jnp.zeros((1, 2, 3, narrow), local_feats.dtype), local_feats], axis=1
    )

    def local_spectrum(signal):
        blocks = signal.reshape(signal.shape[0], seq_parts, tok_rows, narrow).astype(jnp.float32)
        part_real, part_imag = across_blocks(
            blocks, jnp.arange(tok_rows, dtype=jnp.int32), seq_parts, fft_length
        )
        return within_blocks(part_real, part_imag)

    def local_signal(spectrum):
        part_real, part_imag = back_within(
            spectrum[0], spectrum[1], jnp.arange(2 * seq_parts, dtype=jnp.int32), fft_length
        )
        values = back_across(part_real, part_imag, seq_parts, fft_length)
        return values.reshape(values.shape[0], length, narrow)

    def no_rows(rows_part):
        return jnp.zeros_like(rows_part)

    return blocked_core(
        extended,
        moved_in[None, :, 3],
        taps,
        skip_gain,
        moved_in[:, 4],
        local_spectrum,
        local_signal,
        no_rows,
    )


def gather_tiles(features2d, cot2d, resp2d, seq_parts, narrow):
    rows = features2d.shape[0]
    width = seq_parts * narrow

    def body(f_ref, c_ref, r_ref, out_ref):
        group = pl.program_id(0)

        def spread(src_ref):
            for dest in range(seq_parts):
                out_ref[dest, 0] = src_ref[:, dest * narrow : (dest + 1) * narrow]

        @pl.when(group < 3)
        def _():
            spread(f_ref)

        @pl.when(group == 3)
        def _():
            spread(c_ref)

        @pl.when(group == 4)
        def _():
            spread(r_ref)

    return pl.pallas_call(
        body,
        grid=(5,),
        in_specs=[
            pl.BlockSpec((rows, width), lambda g: (0, jnp.minimum(g, 2))),
            pl.BlockSpec((rows, width), lambda g: (0, 0)),
            pl.BlockSpec((rows, width), lambda g: (0, 0)),
        ],
        out_specs=pl.BlockSpec((seq_parts, 1, rows, narrow), lambda g: (0, g, 0, 0)),
        out_shape=jax.ShapeDtypeStruct((seq_parts, 5, rows, narrow), features2d.dtype),
    )(features2d, cot2d, resp2d)


def scatter_tiles(moved, seq_parts, narrow):
    rows = moved.shape[2]

    def body(in_ref, gated_ref, feats_ref):
        group = pl.program_id(0)

        @pl.when(group == 0)
        def _():
            for source in range(seq_parts):
                gated_ref[:, source * narrow : (source + 1) * narrow] = in_ref[source, 0]

        @pl.when(group > 0)
        def _():
            for source in range(seq_parts):
                feats_ref[:, source * narrow : (source + 1) * narrow] = in_ref[source, 0]

    width = seq_parts * narrow
    return pl.pallas_call(
        body,
        grid=(4,),
        in_specs=[pl.BlockSpec((seq_parts, 1, rows, narrow), lambda g: (0, g, 0, 0))],
        out_specs=[
            pl.BlockSpec((rows, width), lambda g: (0, 0)),
            pl.BlockSpec((rows, width), lambda g: (0, jnp.maximum(g - 1, 0))),
        ],
        out_shape=[
            jax.ShapeDtypeStruct((rows, width), moved.dtype),
            jax.ShapeDtypeStruct((rows, 3 * width), moved.dtype),
        ],
    )(moved)


def local(features, short_filter, response, skip_gain, cotangent):
    seq_parts = lax.axis_size("seq")
    dp_parts = lax.axis_size("dp")
    seq_index = lax.axis_index("seq")
    tok_rows = features.shape[1]
    chan_width = features.shape[2] // 3
    length = seq_parts * tok_rows
    narrow = chan_width // seq_parts
    offset = seq_index * narrow
    taps = short_filter.reshape(3, 3, chan_width)
    if narrow % 128 == 0 and tok_rows % 16 == 0:
        arranged = gather_tiles(
            features.reshape(tok_rows, 3 * chan_width),
            cotangent.reshape(tok_rows, chan_width),
            response,
            seq_parts,
            narrow,
        )
        moved_in = (
            lax.all_to_all(arranged, "seq", 0, 0, tiled=True)
            .transpose(0, 2, 1, 3)
            .reshape(length, 5, narrow)
        )
    else:
        joined_in = jnp.concatenate(
            [
                features.reshape(tok_rows, 3 * chan_width),
                cotangent.reshape(tok_rows, chan_width),
                response,
            ],
            axis=1,
        )
        arranged = joined_in.reshape(tok_rows, 5, seq_parts, narrow).transpose(2, 0, 1, 3)
        moved_in = lax.all_to_all(arranged, "seq", 0, 0, tiled=True).reshape(length, 5, narrow)
    local_taps = lax.dynamic_slice_in_dim(taps, offset, narrow, 2)
    local_skip = lax.dynamic_slice_in_dim(skip_gain, offset, narrow, 0)
    if length <= 2048:
        gated, grad_feats, grad_taps, grad_skip, filter_part = block_core(
            moved_in[:, :3], moved_in[:, 3], moved_in[:, 4], local_taps, local_skip
        )
    else:
        gated, grad_feats, grad_taps, grad_skip, filter_part = blocked_fallback(
            moved_in, local_taps, local_skip, seq_parts, tok_rows, narrow
        )
        gated = gated.reshape(length, narrow)
        grad_feats = grad_feats.reshape(length, 3, narrow)
    if narrow % 128 == 0 and tok_rows % 16 == 0:
        joined_out = jnp.concatenate(
            [
                gated.reshape(seq_parts, 1, tok_rows, narrow),
                grad_feats.reshape(seq_parts, tok_rows, 3, narrow).transpose(0, 2, 1, 3),
            ],
            axis=1,
        )
        moved_out = lax.all_to_all(joined_out, "seq", 0, 0, tiled=True)
        gated, grad_feats = scatter_tiles(moved_out, seq_parts, narrow)
    else:
        joined_out = jnp.concatenate(
            [gated.reshape(seq_parts, tok_rows, 1, narrow), grad_feats.reshape(seq_parts, tok_rows, 3, narrow)],
            axis=2,
        )
        moved_out = lax.all_to_all(joined_out, "seq", 0, 0, tiled=True).transpose(1, 2, 0, 3)
        gated = moved_out[:, 0]
        grad_feats = moved_out[:, 1:]
    extra = 16
    small = jnp.concatenate(
        [grad_taps.reshape(9, narrow), grad_skip[None], jnp.zeros((extra - 10, narrow), jnp.float32)],
        axis=0,
    )
    chunks = jnp.concatenate(
        [
            filter_part.reshape(seq_parts, tok_rows, narrow),
            jnp.broadcast_to(small[None], (seq_parts, extra, narrow)),
        ],
        axis=1,
    )
    moved = lax.all_to_all(chunks, "seq", 0, 0, tiled=True)
    pair = seq_parts // dp_parts
    small_all = moved[:, tok_rows : tok_rows + 10]
    small_rows = (
        small_all.reshape(dp_parts, pair, 10, narrow)
        .transpose(1, 0, 2, 3)
        .reshape(pair, dp_parts * 10, narrow)
    )
    joined = jnp.concatenate(
        [moved[:, :tok_rows], jnp.tile(small_rows, (dp_parts, 1, 1))], axis=1
    )
    reduced = lax.psum_scatter(joined, "dp", scatter_dimension=0, tiled=True)
    filter_total = reduced[:, :tok_rows].transpose(1, 0, 2).reshape(tok_rows, pair * narrow)
    small_total = (
        reduced[:, tok_rows:]
        .reshape(pair, dp_parts, 10, narrow)
        .transpose(2, 1, 0, 3)
        .reshape(10, chan_width)
    )
    gated = gated.reshape(1, tok_rows, chan_width)
    grad_feats = grad_feats.reshape(1, tok_rows, 3 * chan_width)
    return (
        gated,
        grad_feats,
        small_total[:9].reshape(3, 3 * chan_width),
        small_total[9],
        filter_total,
    )


def solution(mesh):
    placed = (P("dp", "seq", None), P(), P("seq", None), P(), P("dp", "seq", None))
    return jax.shard_map(
        local,
        mesh=mesh,
        in_specs=placed,
        out_specs=(P("dp", "seq", None), P("dp", "seq", None), P(), P(), P("seq", "dp")),
        check_vma=False,
    )
```
